32 devices in a mesh: col: 8 (over z, y), row: 4 (over x, core).
Axes of the slice: x: 2, y: 2, z: 4, core: 2. Of those that a mesh axis runs over, the one named last changes fastest.
Arguments:
- tiles: bfloat16 [2, 4096, 8192], P(None, 'row', 'col')
- extents: int32 [2, 4, 8], replicated, may hold values from 32 to 128
- offsets: int32 [2, 4, 8], replicated, may hold values from 0 to 127, as said below
- bands: int32 [2, 4, 8], replicated, may hold values from 0 to 8, as said below
Outputs:
- blended: float32 [2, 4096, 8192], P(None, 'row', 'col')
- weight_total: float32 [4096, 8192], P('row', 'col')
The draws below stay inside these ranges and needn't reach their ends.
Inputs may be any that keep to these rules, and one draw needn't show every extreme that they name: Some tile has both offsets equal to 127 and some tile has both equal to 0. `bands`: entry 0 of a tile is smaller than entry 1; some tile has the band 0 to 8.
All inputs are finite; a program needn't handle non-finite values.
Results may differ from the reference program's by a relative error of at most 0.0003.
Values may be sent and summed in bfloat16 or wider, within the bound.
No kernel may reach another device: no remote copies, remote signals or barrier semaphores. Data moves between devices by JAX's collectives and lax.ppermute only.
A program may use at most 128 MiB of HBM per device.

```python
import jax
import jax.numpy as jnp
from jax import lax

PLANES = 2
TILE = 1024
STRIP = 128
SPILL = 128
BLOCK = 128
GRID_ROWS = 4
GRID_COLS = 8
ROWS_PX = 4096
COLS_PX = 8192
N_COL = 8
N_ROW = 4


def draw_tiles(key, part):
    grid_rows = ROWS_PX // TILE
    grid_cols = COLS_PX // TILE
    subkeys = jax.random.split(key, 9)
    full_shape = (PLANES, grid_rows, TILE, grid_cols, TILE)
    base_noise = jax.random.normal(subkeys[0], full_shape, jnp.float32)
    spread = 0.7
    horiz_share = jax.random.normal(subkeys[1], (PLANES, grid_rows, TILE, grid_cols, STRIP), jnp.float32)
    horiz_share = horiz_share * jax.random.uniform(subkeys[2], (PLANES, grid_rows, 1, grid_cols, 1), jnp.float32, 0.5, 2.0)
    vert_share = jax.random.normal(subkeys[3], (PLANES, grid_rows, STRIP, grid_cols, TILE), jnp.float32)
    vert_share = vert_share * jax.random.uniform(subkeys[4], (PLANES, grid_rows, 1, grid_cols, 1), jnp.float32, 0.5, 2.0)
    horiz_left = jnp.concatenate([jnp.zeros((PLANES, grid_rows, TILE, 1, STRIP), jnp.float32), horiz_share[:, :, :, :-1, :]], axis=3)
    horiz_field = jnp.concatenate([horiz_left, jnp.zeros((PLANES, grid_rows, TILE, grid_cols, TILE - 2 * STRIP), jnp.float32), horiz_share], axis=4)
    vert_top = jnp.concatenate([jnp.zeros((PLANES, 1, STRIP, grid_cols, TILE), jnp.float32), vert_share[:, :-1]], axis=1)
    vert_field = jnp.concatenate([vert_top, jnp.zeros((PLANES, grid_rows, TILE - 2 * STRIP, grid_cols, TILE), jnp.float32), vert_share], axis=2)
    row_factor = jnp.exp(jax.random.uniform(subkeys[5], (PLANES, grid_rows, TILE, grid_cols, 1), jnp.float32, -0.4, 0.4))
    col_factor = jnp.exp(jax.random.uniform(subkeys[6], (PLANES, grid_rows, 1, grid_cols, TILE), jnp.float32, -0.4, 0.4))
    tile_gain = jnp.exp(jax.random.uniform(subkeys[7], (PLANES, grid_rows, 1, grid_cols, 1), jnp.float32, -spread, spread))
    tile_offset = jax.random.uniform(subkeys[8], (PLANES, grid_rows, 1, grid_cols, 1), jnp.float32, -1.0, 1.0)
    values = tile_gain * row_factor * col_factor * (base_noise + horiz_field + vert_field) + tile_offset
    return values.reshape(PLANES, ROWS_PX, COLS_PX).astype(jnp.bfloat16)


def draw_offsets(key, part):
    grid_rows = ROWS_PX // TILE
    grid_cols = COLS_PX // TILE
    count_tiles = grid_rows * grid_cols
    values = jax.random.randint(key, (2, count_tiles), 0, SPILL, dtype=jnp.int32)
    chosen = jax.random.randint(jax.random.fold_in(key, 7), (), 0, count_tiles, dtype=jnp.int32)
    tile_ids = jnp.arange(count_tiles, dtype=jnp.int32)
    values = jnp.where(tile_ids[None, :] == chosen, SPILL - 1, values)
    values = jnp.where(tile_ids[None, :] == (chosen + 1) % count_tiles, 0, values)
    return values.reshape(2, grid_rows, grid_cols)


def draw_bands(key, part):
    grid_rows = ROWS_PX // TILE
    grid_cols = COLS_PX // TILE
    count_tiles = grid_rows * grid_cols
    blocks = TILE // BLOCK
    band_low = jax.random.randint(jax.random.fold_in(key, 1), (count_tiles,), 0, (blocks + 1) // 2, dtype=jnp.int32)
    band_high = blocks - jax.random.randint(jax.random.fold_in(key, 2), (count_tiles,), 0, blocks // 2, dtype=jnp.int32)
    chosen = jax.random.randint(jax.random.fold_in(key, 3), (), 0, count_tiles, dtype=jnp.int32)
    tile_ids = jnp.arange(count_tiles, dtype=jnp.int32)
    band_low = jnp.where(tile_ids == chosen, 0, band_low)
    band_high = jnp.where(tile_ids == chosen, blocks, band_high)
    return jnp.stack([band_low, band_high]).reshape(2, grid_rows, grid_cols)


def set_ends(entries, own_key, smallest, high):
    longest = entries.shape.index(max(entries.shape))
    spots = []
    for shift in (0, 1):
        where = [jax.random.randint(jax.random.fold_in(own_key, axis), (), 0, length) for axis, length in enumerate(entries.shape)]
        where[longest] = (where[longest] + shift) % entries.shape[longest]
        spots.append(tuple(where))
    return entries.at[spots[0]].set(smallest).at[spots[1]].set(high)


def setup_inputs(seed: int = 0) -> dict:
    key_list = jax.random.split(jax.random.key(seed), 5)
    return {
        "tiles": draw_tiles(jax.random.fold_in(key_list[4], 71), 0),
        "extents": set_ends(jax.random.randint(key_list[1], (2, GRID_ROWS, GRID_COLS), STRIP // 4, STRIP + 1), jax.random.fold_in(key_list[1], 1), STRIP // 4, STRIP).astype(jnp.int32),
        "offsets": draw_offsets(jax.random.fold_in(key_list[4], 71), 0),
        "bands": draw_bands(jax.random.fold_in(key_list[4], 71), 0),
    }


eps = 1e-6


def pair_terms(former, latter, window):
    full_window = jnp.broadcast_to(window, former.shape)
    number = jnp.sum(full_window, axis=(-2, -1), keepdims=True)
    mean_former = jnp.sum(former * full_window, axis=(-2, -1), keepdims=True) / number
    mean_latter = jnp.sum(latter * full_window, axis=(-2, -1), keepdims=True) / number
    dev_former = (former - mean_former) * full_window
    dev_latter = (latter - mean_latter) * full_window
    flat_number = number[..., 0, 0]
    var_former = jnp.sum(dev_former * dev_former, axis=(-2, -1)) / flat_number
    var_latter = jnp.sum(dev_latter * dev_latter, axis=(-2, -1)) / flat_number
    covariance = jnp.sum(dev_former * dev_latter, axis=(-2, -1)) / flat_number
    weight = covariance * covariance / ((var_former + eps) * (var_latter + eps))
    log_ratio = 0.25 * (jnp.log(var_latter + eps) - jnp.log(var_former + eps))
    shift_term = 0.5 * (mean_latter - mean_former)[..., 0, 0]
    return weight, weight * log_ratio, weight * shift_term


def combine(right_pair, down_pair, left_pair, upper_pair):
    denominator = 1.0 + right_pair[0] + down_pair[0] + left_pair[0] + upper_pair[0]
    log_gain = (right_pair[1] + down_pair[1] - left_pair[1] - upper_pair[1]) / denominator
    offset = (right_pair[2] + down_pair[2] - left_pair[2] - upper_pair[2]) / denominator
    return log_gain, offset


def blend_weight(row_ids, col_ids, band_low, band_high, tile_px):
    half = tile_px / 2.0
    row_fade = (jnp.minimum(row_ids, tile_px - 1 - row_ids) + 1).astype(jnp.float32) / half
    col_fade = (jnp.minimum(col_ids, tile_px - 1 - col_ids) + 1).astype(jnp.float32) / half
    live = ((row_ids >= band_low * BLOCK) & (row_ids < band_high * BLOCK)).astype(jnp.float32)
    return (live * row_fade)[:, None] * col_fade[None, :]


def make_contrib(raw_data, log_gain, offset, row_ids, col_ids, band_low, band_high, tile_px):
    weight = blend_weight(row_ids, col_ids, band_low, band_high, tile_px)
    values = (jnp.exp(log_gain)[:, None, None] * raw_data.astype(jnp.float32) + offset[:, None, None]) * weight[None]
    return jnp.concatenate([values, weight[None]], axis=0)


def add_at(canvas, contrib, top_row, left_col):
    start = (jnp.zeros((), jnp.int32), top_row.astype(jnp.int32), left_col.astype(jnp.int32))
    current = lax.dynamic_slice(canvas, start, contrib.shape)
    return lax.dynamic_update_slice(canvas, current + contrib, start)


def tile_terms(horiz_terms, vert_terms):
    first_h = tuple(jnp.pad(item, ((0, 0), (0, 1), (0, 0))) for item in horiz_terms)
    second_h = tuple(jnp.pad(item, ((0, 0), (1, 0), (0, 0))) for item in horiz_terms)
    first_v = tuple(jnp.pad(item, ((0, 1), (0, 0), (0, 0))) for item in vert_terms)
    second_v = tuple(jnp.pad(item, ((1, 0), (0, 0), (0, 0))) for item in vert_terms)
    return combine(first_h, first_v, second_h, second_v)


def reference(tiles, extents, offsets, bands):
    tile_grid = tiles.reshape(PLANES, N_ROW, TILE, N_COL, TILE).transpose(1, 3, 0, 2, 4)
    strip_ids = jnp.arange(STRIP, dtype=jnp.int32)
    horiz_window = (strip_ids[None, None, :] < extents[0, :, :-1, None]).astype(jnp.float32)[:, :, None, None, :]
    vert_window = (strip_ids[None, None, :] < extents[1, :-1, :, None]).astype(jnp.float32)[:, :, None, :, None]
    horiz_first = tile_grid[:, :-1, :, :, TILE - STRIP:].astype(jnp.float32)
    horiz_second = tile_grid[:, 1:, :, :, :STRIP].astype(jnp.float32)
    vert_first = tile_grid[:-1, :, :, TILE - STRIP:, :].astype(jnp.float32)
    vert_second = tile_grid[1:, :, :, :STRIP, :].astype(jnp.float32)
    gain_one, level_one = tile_terms(pair_terms(horiz_first, horiz_second, horiz_window),
                                     pair_terms(vert_first, vert_second, vert_window))

    def corrected(strips, gain_part, level_part):
        return jnp.exp(gain_part)[..., None, None] * strips + level_part[..., None, None]

    horiz_terms = pair_terms(corrected(horiz_first, gain_one[:, :-1], level_one[:, :-1]),
                             corrected(horiz_second, gain_one[:, 1:], level_one[:, 1:]), horiz_window)
    vert_terms = pair_terms(corrected(vert_first, gain_one[:-1], level_one[:-1]),
                            corrected(vert_second, gain_one[1:], level_one[1:]), vert_window)
    gain_two, level_two = tile_terms(horiz_terms, vert_terms)
    log_gain = gain_one + gain_two
    level = jnp.exp(gain_two) * level_one + level_two
    everything = jnp.arange(TILE, dtype=jnp.int32)
    canvas = jnp.zeros((PLANES + 1, ROWS_PX + SPILL, COLS_PX + SPILL), jnp.float32)

    def place_tile(tile_index, canvas):
        grid_row = tile_index // N_COL
        grid_col = tile_index % N_COL
        raw_data = lax.dynamic_index_in_dim(lax.dynamic_index_in_dim(tile_grid, grid_row, 0, False), grid_col, 0, False)
        contrib = make_contrib(raw_data, log_gain[grid_row, grid_col], level[grid_row, grid_col], everything, everything,
                               bands[0, grid_row, grid_col], bands[1, grid_row, grid_col], TILE)
        return add_at(canvas, contrib, grid_row * TILE + offsets[0, grid_row, grid_col],
                      grid_col * TILE + offsets[1, grid_row, grid_col])

    canvas = lax.fori_loop(jnp.int32(0), jnp.int32(N_ROW * N_COL), place_tile, canvas)
    return canvas[:PLANES, :ROWS_PX, :COLS_PX], canvas[PLANES, :ROWS_PX, :COLS_PX]
```

```python
import jax
import jax.numpy as jnp
from jax import lax
from jax.sharding import PartitionSpec as P

STRIP = 128
SPILL = 128
BLOCK = 128


eps = 1e-06


def from_behind(block, axis, count):
    return lax.ppermute(block, axis, [(i, i + 1) for i in range(count - 1)])


def strip_stats(former, latter, window):
    full = jnp.broadcast_to(window, former.shape)
    number = jnp.sum(full, axis=(-2, -1))
    mean_former = jnp.sum(former * full, axis=(-2, -1)) / number
    mean_latter = jnp.sum(latter * full, axis=(-2, -1)) / number
    dev_former = (former - mean_former[:, None, None]) * full
    dev_latter = (latter - mean_latter[:, None, None]) * full
    var_former = jnp.sum(dev_former * dev_former, axis=(-2, -1)) / number
    var_latter = jnp.sum(dev_latter * dev_latter, axis=(-2, -1)) / number
    covariance = jnp.sum(dev_former * dev_latter, axis=(-2, -1)) / number
    return jnp.stack([mean_former, mean_latter, var_former, var_latter, covariance])


def pair_terms(stats):
    mean_former, mean_latter, var_former, var_latter, covariance = stats
    weight = covariance * covariance / ((var_former + eps) * (var_latter + eps))
    log_ratio = 0.25 * (jnp.log(var_latter + eps) - jnp.log(var_former + eps))
    shift_term = 0.5 * (mean_latter - mean_former)
    return (weight, weight * log_ratio, weight * shift_term)


def corrected_stats(stats, gain_a, level_a, gain_b, level_b):
    mean_former, mean_latter, var_former, var_latter, covariance = stats
    return (
        gain_a * mean_former + level_a,
        gain_b * mean_latter + level_b,
        gain_a * gain_a * var_former,
        gain_b * gain_b * var_latter,
        gain_a * gain_b * covariance,
    )


def tile_terms(horiz_terms, vert_terms):
    first_h = tuple(jnp.pad(item, ((0, 0), (0, 1), (0, 0))) for item in horiz_terms)
    second_h = tuple(jnp.pad(item, ((0, 0), (1, 0), (0, 0))) for item in horiz_terms)
    first_v = tuple(jnp.pad(item, ((0, 1), (0, 0), (0, 0))) for item in vert_terms)
    second_v = tuple(jnp.pad(item, ((1, 0), (0, 0), (0, 0))) for item in vert_terms)
    denominator = 1.0 + first_h[0] + first_v[0] + second_h[0] + second_v[0]
    log_gain = (first_h[1] + first_v[1] - second_h[1] - second_v[1]) / denominator
    offset = (first_h[2] + first_v[2] - second_h[2] - second_v[2]) / denominator
    return log_gain, offset


def grid_solve(horiz_stats, vert_stats):
    gain_one, level_one = tile_terms(pair_terms(horiz_stats), pair_terms(vert_stats))
    scale = jnp.exp(gain_one)
    horiz_two = corrected_stats(
        horiz_stats, scale[:, :-1], level_one[:, :-1], scale[:, 1:], level_one[:, 1:]
    )
    vert_two = corrected_stats(
        vert_stats, scale[:-1], level_one[:-1], scale[1:], level_one[1:]
    )
    gain_two, level_two = tile_terms(pair_terms(horiz_two), pair_terms(vert_two))
    log_gain = gain_one + gain_two
    level = jnp.exp(gain_two) * level_one + level_two
    return log_gain, level


def fade(ids, tile_px):
    return (jnp.minimum(ids, tile_px - 1 - ids) + 1).astype(jnp.float32) / (tile_px / 2.0)


def row_weight(ids, band_low, band_high, tile_px, present):
    live = (ids >= band_low * BLOCK) & (ids < band_high * BLOCK) & (ids >= 0) & (ids < tile_px)
    return live.astype(jnp.float32) * present * fade(ids, tile_px)


def col_weight(ids, tile_px, present):
    live = (ids >= 0) & (ids < tile_px)
    return live.astype(jnp.float32) * present * fade(ids, tile_px)


def piece(source, pads, start, size, rows_w, cols_w, log_gain, level):
    padded = jnp.pad(source, pads)
    zero = jnp.zeros((), jnp.int32)
    window = lax.dynamic_slice(padded, (zero, start[0], start[1]), size)
    weight = rows_w[:, None] * cols_w[None, :]
    values = (
        jnp.exp(log_gain)[:, None, None] * window.astype(jnp.float32) + level[:, None, None]
    ) * weight[None]
    return values, weight


def local(tiles, extents, offsets, bands):
    planes, tile_px, _ = tiles.shape
    n_row = lax.axis_size("row")
    n_col = lax.axis_size("col")
    row_index = lax.axis_index("row")
    col_index = lax.axis_index("col")
    width = STRIP

    right_strip = tiles[:, :, tile_px - width :]
    down_strip = tiles[:, tile_px - width :, :]
    corner = tiles[:, tile_px - width :, tile_px - width :]
    from_left = from_behind(right_strip, "col", n_col)
    from_up = from_behind(down_strip, "row", n_row)
    diagonal = [
        (j * n_row + i, (j + 1) * n_row + i + 1) for i in range(n_row - 1) for j in range(n_col - 1)
    ]
    from_corner = lax.ppermute(corner, ("col", "row"), diagonal)

    left_col = jnp.maximum(col_index - 1, 0)
    upper_row = jnp.maximum(row_index - 1, 0)
    strip_ids = jnp.arange(width, dtype=jnp.int32)
    horiz_window = (strip_ids < extents[0, row_index, left_col]).astype(jnp.float32)[None, None, :]
    vert_window = (strip_ids < extents[1, upper_row, col_index]).astype(jnp.float32)[None, :, None]
    horiz = strip_stats(
        from_left.astype(jnp.float32), tiles[:, :, :width].astype(jnp.float32), horiz_window
    )
    vert = strip_stats(
        from_up.astype(jnp.float32), tiles[:, :width, :].astype(jnp.float32), vert_window
    )
    gathered = lax.all_gather(jnp.stack([horiz, vert]), ("col", "row"))
    gathered = gathered.reshape((n_col, n_row) + gathered.shape[1:]).swapaxes(0, 1)
    horiz_stats = tuple(gathered[:, 1:, 0, k] for k in range(5))
    vert_stats = tuple(gathered[1:, :, 1, k] for k in range(5))
    log_gain, level = grid_solve(horiz_stats, vert_stats)

    def terms_at(r, c):
        return log_gain[r, c], level[r, c]

    has_left = (col_index > 0).astype(jnp.float32)
    has_up = (row_index > 0).astype(jnp.float32)
    ids = jnp.arange(tile_px, dtype=jnp.int32)
    edge = jnp.arange(width, dtype=jnp.int32)

    def weights_of(r, c, row_ids, col_ids, present):
        rows_w = row_weight(row_ids, bands[0, r, c], bands[1, r, c], tile_px, present)
        cols_w = col_weight(col_ids, tile_px, jnp.float32(1.0))
        return rows_w, cols_w

    top, left = offsets[0, row_index, col_index], offsets[1, row_index, col_index]
    rows_w, cols_w = weights_of(row_index, col_index, ids - top, ids - left, jnp.float32(1.0))
    own_vals, own_w = piece(
        tiles, ((0, 0), (SPILL, 0), (SPILL, 0)), (SPILL - top, SPILL - left),
        (planes, tile_px, tile_px), rows_w, cols_w, *terms_at(row_index, col_index),
    )
    top_l, left_l = offsets[0, row_index, left_col], offsets[1, row_index, left_col]
    rows_w, cols_w = weights_of(
        row_index, left_col, ids - top_l, edge + tile_px - left_l, has_left
    )
    left_vals, left_w = piece(
        from_left, ((0, 0), (SPILL, 0), (0, width)), (SPILL - top_l, width - left_l),
        (planes, tile_px, width), rows_w, cols_w, *terms_at(row_index, left_col),
    )
    top_u, left_u = offsets[0, upper_row, col_index], offsets[1, upper_row, col_index]
    rows_w, cols_w = weights_of(
        upper_row, col_index, edge + tile_px - top_u, ids - left_u, has_up
    )
    up_vals, up_w = piece(
        from_up, ((0, 0), (0, width), (SPILL, 0)), (width - top_u, SPILL - left_u),
        (planes, width, tile_px), rows_w, cols_w, *terms_at(upper_row, col_index),
    )
    top_c, left_c = offsets[0, upper_row, left_col], offsets[1, upper_row, left_col]
    rows_w, cols_w = weights_of(
        upper_row, left_col, edge + tile_px - top_c, edge + tile_px - left_c, has_up * has_left
    )
    corner_vals, corner_w = piece(
        from_corner, ((0, 0), (0, width), (0, width)), (width - top_c, width - left_c),
        (planes, width, width), rows_w, cols_w, *terms_at(upper_row, left_col),
    )

    blended = own_vals.at[:, :, :width].add(left_vals)
    blended = blended.at[:, :width, :].add(up_vals)
    blended = blended.at[:, :width, :width].add(corner_vals)
    weight = own_w.at[:, :width].add(left_w)
    weight = weight.at[:width, :].add(up_w)
    weight = weight.at[:width, :width].add(corner_w)
    return blended, weight


def solution(mesh):
    return jax.shard_map(
        local,
        mesh=mesh,
        in_specs=(P(None, "row", "col"), P(), P(), P()),
        out_specs=(P(None, "row", "col"), P("row", "col")),
        check_vma=False,
    )
```

```python
import jax
import jax.numpy as jnp
from jax import lax
from jax.sharding import PartitionSpec as P

STRIP = 128
SPILL = 128
BLOCK = 128


eps = 1e-06


def from_behind(block, axis, count):
    return lax.ppermute(block, axis, [(i, i + 1) for i in range(count - 1)])


def strip_stats(former, latter, window):
    full = jnp.broadcast_to(window, former.shape)
    number = jnp.sum(full, axis=(-2, -1))
    mean_former = jnp.sum(former * full, axis=(-2, -1)) / number
    mean_latter = jnp.sum(latter * full, axis=(-2, -1)) / number
    dev_former = (former - mean_former[:, None, None]) * full
    dev_latter = (latter - mean_latter[:, None, None]) * full
    var_former = jnp.sum(dev_former * dev_former, axis=(-2, -1)) / number
    var_latter = jnp.sum(dev_latter * dev_latter, axis=(-2, -1)) / number
    covariance = jnp.sum(dev_former * dev_latter, axis=(-2, -1)) / number
    return jnp.stack([mean_former, mean_latter, var_former, var_latter, covariance])


def pair_terms(stats):
    mean_former, mean_latter, var_former, var_latter, covariance = stats
    weight = covariance * covariance / ((var_former + eps) * (var_latter + eps))
    log_ratio = 0.25 * (jnp.log(var_latter + eps) - jnp.log(var_former + eps))
    shift_term = 0.5 * (mean_latter - mean_former)
    return (weight, weight * log_ratio, weight * shift_term)


def corrected_stats(stats, gain_a, level_a, gain_b, level_b):
    mean_former, mean_latter, var_former, var_latter, covariance = stats
    return (
        gain_a * mean_former + level_a,
        gain_b * mean_latter + level_b,
        gain_a * gain_a * var_former,
        gain_b * gain_b * var_latter,
        gain_a * gain_b * covariance,
    )


def tile_terms(horiz_terms, vert_terms):
    first_h = tuple(jnp.pad(item, ((0, 0), (0, 1), (0, 0))) for item in horiz_terms)
    second_h = tuple(jnp.pad(item, ((0, 0), (1, 0), (0, 0))) for item in horiz_terms)
    first_v = tuple(jnp.pad(item, ((0, 1), (0, 0), (0, 0))) for item in vert_terms)
    second_v = tuple(jnp.pad(item, ((1, 0), (0, 0), (0, 0))) for item in vert_terms)
    denominator = 1.0 + first_h[0] + first_v[0] + second_h[0] + second_v[0]
    log_gain = (first_h[1] + first_v[1] - second_h[1] - second_v[1]) / denominator
    offset = (first_h[2] + first_v[2] - second_h[2] - second_v[2]) / denominator
    return log_gain, offset


def grid_solve(horiz_stats, vert_stats):
    gain_one, level_one = tile_terms(pair_terms(horiz_stats), pair_terms(vert_stats))
    scale = jnp.exp(gain_one)
    horiz_two = corrected_stats(
        horiz_stats, scale[:, :-1], level_one[:, :-1], scale[:, 1:], level_one[:, 1:]
    )
    vert_two = corrected_stats(
        vert_stats, scale[:-1], level_one[:-1], scale[1:], level_one[1:]
    )
    gain_two, level_two = tile_terms(pair_terms(horiz_two), pair_terms(vert_two))
    log_gain = gain_one + gain_two
    level = jnp.exp(gain_two) * level_one + level_two
    return log_gain, level


def fade(ids, tile_px):
    return (jnp.minimum(ids, tile_px - 1 - ids) + 1).astype(jnp.float32) / (tile_px / 2.0)


def row_weight(ids, band_low, band_high, tile_px, present):
    live = (ids >= band_low * BLOCK) & (ids < band_high * BLOCK) & (ids >= 0) & (ids < tile_px)
    return live.astype(jnp.float32) * present * fade(ids, tile_px)


def col_weight(ids, tile_px, present):
    live = (ids >= 0) & (ids < tile_px)
    return live.astype(jnp.float32) * present * fade(ids, tile_px)


def piece(source, pads, start, size, rows_w, cols_w, log_gain, level):
    padded = jnp.pad(source, pads)
    zero = jnp.zeros((), jnp.int32)
    window = lax.dynamic_slice(padded, (zero, start[0], start[1]), size)
    weight = rows_w[:, None] * cols_w[None, :]
    values = (
        jnp.exp(log_gain)[:, None, None] * window.astype(jnp.float32) + level[:, None, None]
    ) * weight[None]
    return values, weight


def local(tiles, extents, offsets, bands):
    planes, tile_px, _ = tiles.shape
    n_row = lax.axis_size("row")
    n_col = lax.axis_size("col")
    row_index = lax.axis_index("row")
    col_index = lax.axis_index("col")
    width = STRIP

    right_strip = tiles[:, :, tile_px - width :]
    down_strip = tiles[:, tile_px - width :, :]
    corner = tiles[:, tile_px - width :, tile_px - width :]
    from_left = from_behind(right_strip, "col", n_col)
    from_up = from_behind(down_strip, "row", n_row)
    diagonal = [
        (j * n_row + i, (j + 1) * n_row + i + 1) for i in range(n_row - 1) for j in range(n_col - 1)
    ]
    from_corner = lax.ppermute(corner, ("col", "row"), diagonal)

    left_col = jnp.maximum(col_index - 1, 0)
    upper_row = jnp.maximum(row_index - 1, 0)
    strip_ids = jnp.arange(width, dtype=jnp.int32)
    horiz_window = (strip_ids < extents[0, row_index, left_col]).astype(jnp.float32)[None, None, :]
    vert_window = (strip_ids < extents[1, upper_row, col_index]).astype(jnp.float32)[None, :, None]
    horiz = strip_stats(
        from_left.astype(jnp.float32), tiles[:, :, :width].astype(jnp.float32), horiz_window
    )
    vert = strip_stats(
        from_up.astype(jnp.float32), tiles[:, :width, :].astype(jnp.float32), vert_window
    )
    own_stats = jnp.stack([horiz, vert])
    slot = (
        (jnp.arange(n_row)[:, None] == row_index) & (jnp.arange(n_col)[None, :] == col_index)
    ).astype(jnp.float32)
    gathered = lax.psum(slot[:, :, None, None, None] * own_stats[None, None], ("col", "row"))
    horiz_stats = tuple(gathered[:, 1:, 0, k] for k in range(5))
    vert_stats = tuple(gathered[1:, :, 1, k] for k in range(5))
    log_gain, level = grid_solve(horiz_stats, vert_stats)

    def terms_at(r, c):
        return log_gain[r, c], level[r, c]

    has_left = (col_index > 0).astype(jnp.float32)
    has_up = (row_index > 0).astype(jnp.float32)
    ids = jnp.arange(tile_px, dtype=jnp.int32)
    edge = jnp.arange(width, dtype=jnp.int32)

    def weights_of(r, c, row_ids, col_ids, present):
        rows_w = row_weight(row_ids, bands[0, r, c], bands[1, r, c], tile_px, present)
        cols_w = col_weight(col_ids, tile_px, jnp.float32(1.0))
        return rows_w, cols_w

    top, left = offsets[0, row_index, col_index], offsets[1, row_index, col_index]
    rows_w, cols_w = weights_of(row_index, col_index, ids - top, ids - left, jnp.float32(1.0))
    own_vals, own_w = piece(
        tiles, ((0, 0), (SPILL, 0), (SPILL, 0)), (SPILL - top, SPILL - left),
        (planes, tile_px, tile_px), rows_w, cols_w, *terms_at(row_index, col_index),
    )
    top_l, left_l = offsets[0, row_index, left_col], offsets[1, row_index, left_col]
    rows_w, cols_w = weights_of(
        row_index, left_col, ids - top_l, edge + tile_px - left_l, has_left
    )
    left_vals, left_w = piece(
        from_left, ((0, 0), (SPILL, 0), (0, width)), (SPILL - top_l, width - left_l),
        (planes, tile_px, width), rows_w, cols_w, *terms_at(row_index, left_col),
    )
    top_u, left_u = offsets[0, upper_row, col_index], offsets[1, upper_row, col_index]
    rows_w, cols_w = weights_of(
        upper_row, col_index, edge + tile_px - top_u, ids - left_u, has_up
    )
    up_vals, up_w = piece(
        from_up, ((0, 0), (0, width), (SPILL, 0)), (width - top_u, SPILL - left_u),
        (planes, width, tile_px), rows_w, cols_w, *terms_at(upper_row, col_index),
    )
    top_c, left_c = offsets[0, upper_row, left_col], offsets[1, upper_row, left_col]
    rows_w, cols_w = weights_of(
        upper_row, left_col, edge + tile_px - top_c, edge + tile_px - left_c, has_up * has_left
    )
    corner_vals, corner_w = piece(
        from_corner, ((0, 0), (0, width), (0, width)), (width - top_c, width - left_c),
        (planes, width, width), rows_w, cols_w, *terms_at(upper_row, left_col),
    )

    blended = own_vals.at[:, :, :width].add(left_vals)
    blended = blended.at[:, :width, :].add(up_vals)
    blended = blended.at[:, :width, :width].add(corner_vals)
    weight = own_w.at[:, :width].add(left_w)
    weight = weight.at[:width, :].add(up_w)
    weight = weight.at[:width, :width].add(corner_w)
    return blended, weight


def solution(mesh):
    return jax.shard_map(
        local,
        mesh=mesh,
        in_specs=(P(None, "row", "col"), P(), P(), P()),
        out_specs=(P(None, "row", "col"), P("row", "col")),
        check_vma=False,
    )
```

```python
import jax
import jax.numpy as jnp
from jax import lax
from jax.sharding import PartitionSpec as P

STRIP = 128
SPILL = 128
BLOCK = 128


eps = 1e-06


def strip_stats(former, latter, window):
    full = jnp.broadcast_to(window, former.shape)
    number = jnp.sum(full, axis=(-2, -1))
    mean_former = jnp.sum(former * full, axis=(-2, -1)) / number
    mean_latter = jnp.sum(latter * full, axis=(-2, -1)) / number
    dev_former = (former - mean_former[:, None, None]) * full
    dev_latter = (latter - mean_latter[:, None, None]) * full
    var_former = jnp.sum(dev_former * dev_former, axis=(-2, -1)) / number
    var_latter = jnp.sum(dev_latter * dev_latter, axis=(-2, -1)) / number
    covariance = jnp.sum(dev_former * dev_latter, axis=(-2, -1)) / number
    return jnp.stack([mean_former, mean_latter, var_former, var_latter, covariance])


def pair_terms(stats):
    mean_former, mean_latter, var_former, var_latter, covariance = stats
    weight = covariance * covariance / ((var_former + eps) * (var_latter + eps))
    log_ratio = 0.25 * (jnp.log(var_latter + eps) - jnp.log(var_former + eps))
    shift_term = 0.5 * (mean_latter - mean_former)
    return (weight, weight * log_ratio, weight * shift_term)


def corrected_stats(stats, gain_a, level_a, gain_b, level_b):
    mean_former, mean_latter, var_former, var_latter, covariance = stats
    return (
        gain_a * mean_former + level_a,
        gain_b * mean_latter + level_b,
        gain_a * gain_a * var_former,
        gain_b * gain_b * var_latter,
        gain_a * gain_b * covariance,
    )


def fade(ids, tile_px):
    return (jnp.minimum(ids, tile_px - 1 - ids) + 1).astype(jnp.float32) / (tile_px / 2.0)


def row_weight(ids, band_low, band_high, tile_px, present):
    live = (ids >= band_low * BLOCK) & (ids < band_high * BLOCK) & (ids >= 0) & (ids < tile_px)
    return live.astype(jnp.float32) * present * fade(ids, tile_px)


def col_weight(ids, tile_px, present):
    live = (ids >= 0) & (ids < tile_px)
    return live.astype(jnp.float32) * present * fade(ids, tile_px)


def piece(source, pads, start, size, rows_w, cols_w, log_gain, level):
    padded = jnp.pad(source, pads)
    zero = jnp.zeros((), jnp.int32)
    window = lax.dynamic_slice(padded, (zero, start[0], start[1]), size)
    weight = rows_w[:, None] * cols_w[None, :]
    values = (
        jnp.exp(log_gain)[:, None, None] * window.astype(jnp.float32) + level[:, None, None]
    ) * weight[None]
    return values, weight


def shifted(block, axis, count, step):
    if step > 0:
        route = [(i, i + 1) for i in range(count - 1)]
    else:
        route = [(i + 1, i) for i in range(count - 1)]
    return lax.ppermute(block, axis, route)


def combine(right_pair, down_pair, left_pair, upper_pair):
    denominator = 1.0 + right_pair[0] + down_pair[0] + left_pair[0] + upper_pair[0]
    log_gain = (right_pair[1] + down_pair[1] - left_pair[1] - upper_pair[1]) / denominator
    offset = (right_pair[2] + down_pair[2] - left_pair[2] - upper_pair[2]) / denominator
    return log_gain, offset


def masked_terms(stats, present):
    return tuple(jnp.where(present, item, 0.0) for item in pair_terms(stats))


def local(tiles, extents, offsets, bands):
    planes, tile_px, _ = tiles.shape
    n_row = lax.axis_size("row")
    n_col = lax.axis_size("col")
    row_index = lax.axis_index("row")
    col_index = lax.axis_index("col")
    width = STRIP

    right_strip = tiles[:, :, tile_px - width :]
    down_strip = tiles[:, tile_px - width :, :]
    left_strip = tiles[:, :, :width]
    up_strip = tiles[:, :width, :]
    corner = tiles[:, tile_px - width :, tile_px - width :]
    from_left = shifted(right_strip, "col", n_col, 1)
    from_up = shifted(down_strip, "row", n_row, 1)
    from_right = shifted(left_strip, "col", n_col, -1)
    from_down = shifted(up_strip, "row", n_row, -1)
    diagonal = [
        (j * n_row + i, (j + 1) * n_row + i + 1) for i in range(n_row - 1) for j in range(n_col - 1)
    ]
    from_corner = lax.ppermute(corner, ("col", "row"), diagonal)

    left_col = jnp.maximum(col_index - 1, 0)
    upper_row = jnp.maximum(row_index - 1, 0)
    strip_ids = jnp.arange(width, dtype=jnp.int32)

    def across(extent):
        return (strip_ids < extent).astype(jnp.float32)[None, None, :]

    def along(extent):
        return (strip_ids < extent).astype(jnp.float32)[None, :, None]

    f32 = jnp.float32
    right_stats = strip_stats(
        right_strip.astype(f32), from_right.astype(f32), across(extents[0, row_index, col_index])
    )
    down_stats = strip_stats(
        down_strip.astype(f32), from_down.astype(f32), along(extents[1, row_index, col_index])
    )
    left_stats = strip_stats(
        from_left.astype(f32), left_strip.astype(f32), across(extents[0, row_index, left_col])
    )
    up_stats = strip_stats(
        from_up.astype(f32), up_strip.astype(f32), along(extents[1, upper_row, col_index])
    )
    has_right = col_index < n_col - 1
    has_down = row_index < n_row - 1
    has_left_pair = col_index > 0
    has_up_pair = row_index > 0
    gain_one, level_one = combine(
        masked_terms(right_stats, has_right),
        masked_terms(down_stats, has_down),
        masked_terms(left_stats, has_left_pair),
        masked_terms(up_stats, has_up_pair),
    )
    first = jnp.concatenate([gain_one, level_one])
    near = [
        shifted(first, "col", n_col, -1),
        shifted(first, "row", n_row, -1),
        shifted(first, "col", n_col, 1),
        shifted(first, "row", n_row, 1),
    ]
    scale = jnp.exp(gain_one)
    near_scale = [jnp.exp(item[:planes]) for item in near]
    near_level = [item[planes:] for item in near]
    right_two = corrected_stats(right_stats, scale, level_one, near_scale[0], near_level[0])
    down_two = corrected_stats(down_stats, scale, level_one, near_scale[1], near_level[1])
    left_two = corrected_stats(left_stats, near_scale[2], near_level[2], scale, level_one)
    up_two = corrected_stats(up_stats, near_scale[3], near_level[3], scale, level_one)
    gain_two, level_two = combine(
        masked_terms(right_two, has_right),
        masked_terms(down_two, has_down),
        masked_terms(left_two, has_left_pair),
        masked_terms(up_two, has_up_pair),
    )
    own_gain = gain_one + gain_two
    own_level = jnp.exp(gain_two) * level_one + level_two
    final = jnp.concatenate([own_gain, own_level])
    final_left = shifted(final, "col", n_col, 1)
    final_up = shifted(final, "row", n_row, 1)
    final_corner = lax.ppermute(final, ("col", "row"), diagonal)
    found = {
        "own": (own_gain, own_level),
        "left": (final_left[:planes], final_left[planes:]),
        "up": (final_up[:planes], final_up[planes:]),
        "corner": (final_corner[:planes], final_corner[planes:]),
    }

    def terms_at(which):
        return found[which]

    has_left = (col_index > 0).astype(jnp.float32)
    has_up = (row_index > 0).astype(jnp.float32)
    ids = jnp.arange(tile_px, dtype=jnp.int32)
    edge = jnp.arange(width, dtype=jnp.int32)

    def weights_of(r, c, row_ids, col_ids, present):
        rows_w = row_weight(row_ids, bands[0, r, c], bands[1, r, c], tile_px, present)
        cols_w = col_weight(col_ids, tile_px, jnp.float32(1.0))
        return rows_w, cols_w

    top, left = offsets[0, row_index, col_index], offsets[1, row_index, col_index]
    rows_w, cols_w = weights_of(row_index, col_index, ids - top, ids - left, jnp.float32(1.0))
    own_vals, own_w = piece(
        tiles, ((0, 0), (SPILL, 0), (SPILL, 0)), (SPILL - top, SPILL - left),
        (planes, tile_px, tile_px), rows_w, cols_w, *terms_at("own"),
    )
    top_l, left_l = offsets[0, row_index, left_col], offsets[1, row_index, left_col]
    rows_w, cols_w = weights_of(
        row_index, left_col, ids - top_l, edge + tile_px - left_l, has_left
    )
    left_vals, left_w = piece(
        from_left, ((0, 0), (SPILL, 0), (0, width)), (SPILL - top_l, width - left_l),
        (planes, tile_px, width), rows_w, cols_w, *terms_at("left"),
    )
    top_u, left_u = offsets[0, upper_row, col_index], offsets[1, upper_row, col_index]
    rows_w, cols_w = weights_of(
        upper_row, col_index, edge + tile_px - top_u, ids - left_u, has_up
    )
    up_vals, up_w = piece(
        from_up, ((0, 0), (0, width), (SPILL, 0)), (width - top_u, SPILL - left_u),
        (planes, width, tile_px), rows_w, cols_w, *terms_at("up"),
    )
    top_c, left_c = offsets[0, upper_row, left_col], offsets[1, upper_row, left_col]
    rows_w, cols_w = weights_of(
        upper_row, left_col, edge + tile_px - top_c, edge + tile_px - left_c, has_up * has_left
    )
    corner_vals, corner_w = piece(
        from_corner, ((0, 0), (0, width), (0, width)), (width - top_c, width - left_c),
        (planes, width, width), rows_w, cols_w, *terms_at("corner"),
    )

    blended = own_vals.at[:, :, :width].add(left_vals)
    blended = blended.at[:, :width, :].add(up_vals)
    blended = blended.at[:, :width, :width].add(corner_vals)
    weight = own_w.at[:, :width].add(left_w)
    weight = weight.at[:width, :].add(up_w)
    weight = weight.at[:width, :width].add(corner_w)
    return blended, weight


def solution(mesh):
    return jax.shard_map(
        local,
        mesh=mesh,
        in_specs=(P(None, "row", "col"), P(), P(), P()),
        out_specs=(P(None, "row", "col"), P("row", "col")),
        check_vma=False,
    )
```

```python
import functools

import jax
import jax.numpy as jnp
from jax import lax
from jax.sharding import PartitionSpec as P
from jax.experimental import pallas as pl
from jax.experimental.pallas import tpu as pltpu

STRIP = 128
SPILL = 128
BLOCK = 128
ROWS = 256


eps = 1e-06


def strip_stats(former, latter, window):
    full = jnp.broadcast_to(window, former.shape)
    number = jnp.sum(full, axis=(-2, -1))
    mean_former = jnp.sum(former * full, axis=(-2, -1)) / number
    mean_latter = jnp.sum(latter * full, axis=(-2, -1)) / number
    dev_former = (former - mean_former[:, None, None]) * full
    dev_latter = (latter - mean_latter[:, None, None]) * full
    var_former = jnp.sum(dev_former * dev_former, axis=(-2, -1)) / number
    var_latter = jnp.sum(dev_latter * dev_latter, axis=(-2, -1)) / number
    covariance = jnp.sum(dev_former * dev_latter, axis=(-2, -1)) / number
    return jnp.stack([mean_former, mean_latter, var_former, var_latter, covariance])


def pair_terms(stats):
    mean_former, mean_latter, var_former, var_latter, covariance = stats
    weight = covariance * covariance / ((var_former + eps) * (var_latter + eps))
    log_ratio = 0.25 * (jnp.log(var_latter + eps) - jnp.log(var_former + eps))
    shift_term = 0.5 * (mean_latter - mean_former)
    return (weight, weight * log_ratio, weight * shift_term)


def corrected_stats(stats, gain_a, level_a, gain_b, level_b):
    mean_former, mean_latter, var_former, var_latter, covariance = stats
    return (
        gain_a * mean_former + level_a,
        gain_b * mean_latter + level_b,
        gain_a * gain_a * var_former,
        gain_b * gain_b * var_latter,
        gain_a * gain_b * covariance,
    )


def blend_kernel(idx_ref, off_ref, band_ref, terms_ref, cur_ref, prev_ref, lcur_ref, lprev_ref,
                 up_ref, corner_ref, out_ref, w_ref, *, n_row, n_col):
    f32 = jnp.float32
    step = pl.program_id(0)
    planes, rows, tile_px = cur_ref.shape
    width = lcur_ref.shape[2]
    cells = n_row * n_col
    r = idx_ref[0]
    c = idx_ref[1]
    lc = jnp.maximum(c - 1, 0)
    ur = jnp.maximum(r - 1, 0)
    has_left = c > 0
    has_up = r > 0

    def table(ref, k, rr, cc):
        return ref[k * cells + rr * n_col + cc]

    def fade(ids):
        return (jnp.minimum(ids, tile_px - 1 - ids) + 1).astype(f32) / (tile_px / 2.0)

    def band_rows(ids, rr, cc, extra):
        live = (ids >= table(band_ref, 0, rr, cc) * BLOCK) & (ids < table(band_ref, 1, rr, cc) * BLOCK)
        live = live & (ids >= 0) & (ids < tile_px) & extra
        return jnp.where(live, fade(ids), 0.0)

    def gain(k, p):
        return terms_ref[k * 2 * planes + p], terms_ref[k * 2 * planes + planes + p]

    t = lax.broadcasted_iota(jnp.int32, (rows, 1), 0)
    x = lax.broadcasted_iota(jnp.int32, (1, tile_px), 1)
    xs = lax.broadcasted_iota(jnp.int32, (1, width), 1)
    y = step * rows + t
    top = table(off_ref, 0, r, c)
    left = table(off_ref, 1, r, c)
    top_l = table(off_ref, 0, r, lc)
    left_l = table(off_ref, 1, r, lc)
    j = x - left
    w_own = band_rows(y - top, r, c, True) * jnp.where(j >= 0, fade(j), 0.0)
    j_l = xs + tile_px - left_l
    w_left = band_rows(y - top_l, r, lc, has_left) * jnp.where(j_l < tile_px, fade(j_l), 0.0)
    w_ref[...] = w_own
    w_ref[:, :width] += w_left
    for p in range(planes):
        cur = cur_ref[p].astype(f32)
        prev = prev_ref[p].astype(f32)
        shifted_rows = jnp.where(t >= top, pltpu.roll(cur, top, 0), pltpu.roll(prev, top, 0))
        window = pltpu.roll(shifted_rows, left, 1)
        scale, level = gain(0, p)
        out_ref[p] = (scale * window + level) * w_own
        lcur = lcur_ref[p].astype(f32)
        lprev = lprev_ref[p].astype(f32)
        shifted_rows = jnp.where(t >= top_l, pltpu.roll(lcur, top_l, 0), pltpu.roll(lprev, top_l, 0))
        window = pltpu.roll(shifted_rows, left_l, 1)
        scale, level = gain(1, p)
        out_ref[p, :, :width] += (scale * window + level) * w_left

    @pl.when(step == 0)
    def _():
        te = lax.broadcasted_iota(jnp.int32, (width, 1), 0)
        top_u = table(off_ref, 0, ur, c)
        left_u = table(off_ref, 1, ur, c)
        top_c = table(off_ref, 0, ur, lc)
        left_c = table(off_ref, 1, ur, lc)
        j_u = x - left_u
        w_up = band_rows(te + tile_px - top_u, ur, c, has_up) * jnp.where(j_u >= 0, fade(j_u), 0.0)
        j_c = xs + tile_px - left_c
        w_corner = band_rows(te + tile_px - top_c, ur, lc, has_up & has_left) * jnp.where(
            j_c < tile_px, fade(j_c), 0.0
        )
        w_ref[:width, :] += w_up
        w_ref[:width, :width] += w_corner
        for p in range(planes):
            window = pltpu.roll(pltpu.roll(up_ref[p].astype(f32), top_u, 0), left_u, 1)
            scale, level = gain(2, p)
            out_ref[p, :width, :] += (scale * window + level) * w_up
            window = pltpu.roll(pltpu.roll(corner_ref[p].astype(f32), top_c, 0), left_c, 1)
            scale, level = gain(3, p)
            out_ref[p, :width, :width] += (scale * window + level) * w_corner


def blend(idx, offsets, bands, terms, tiles, from_left, from_up, from_corner, n_row, n_col):
    planes, tile_px, _ = tiles.shape
    width = from_left.shape[2]
    rows = min(ROWS, tile_px)
    steps = tile_px // rows

    def cur(b, *_):
        return (0, b, 0)

    def prev(b, *_):
        return (0, jnp.maximum(b - 1, 0), 0)

    def fixed(b, *_):
        return (0, 0, 0)

    grid_spec = pltpu.PrefetchScalarGridSpec(
        num_scalar_prefetch=3,
        grid=(steps,),
        in_specs=[
            pl.BlockSpec(memory_space=pltpu.SMEM),
            pl.BlockSpec((planes, rows, tile_px), cur),
            pl.BlockSpec((planes, rows, tile_px), prev),
            pl.BlockSpec((planes, rows, width), cur),
            pl.BlockSpec((planes, rows, width), prev),
            pl.BlockSpec((planes, width, tile_px), fixed),
            pl.BlockSpec((planes, width, width), fixed),
        ],
        out_specs=[
            pl.BlockSpec((planes, rows, tile_px), cur),
            pl.BlockSpec((rows, tile_px), lambda b, *_: (b, 0)),
        ],
    )
    out_bytes = 4 * (planes + 1) * tile_px * tile_px
    in_bytes = 2 * 2 * planes * tile_px * (tile_px + width)
    return pl.pallas_call(
        functools.partial(blend_kernel, n_row=n_row, n_col=n_col),
        grid_spec=grid_spec,
        out_shape=[
            jax.ShapeDtypeStruct((planes, tile_px, tile_px), jnp.float32),
            jax.ShapeDtypeStruct((tile_px, tile_px), jnp.float32),
        ],
        compiler_params=pltpu.CompilerParams(dimension_semantics=("arbitrary",)),
        cost_estimate=pl.CostEstimate(
            flops=12 * planes * tile_px * tile_px, transcendentals=0,
            bytes_accessed=out_bytes + in_bytes,
        ),
    )(idx, offsets.reshape(-1), bands.reshape(-1), terms, tiles, tiles, from_left, from_left,
      from_up, from_corner)


def shifted(block, axis, count, step):
    if step > 0:
        route = [(i, i + 1) for i in range(count - 1)]
    else:
        route = [(i + 1, i) for i in range(count - 1)]
    return lax.ppermute(block, axis, route)


def combine(right_pair, down_pair, left_pair, upper_pair):
    denominator = 1.0 + right_pair[0] + down_pair[0] + left_pair[0] + upper_pair[0]
    log_gain = (right_pair[1] + down_pair[1] - left_pair[1] - upper_pair[1]) / denominator
    offset = (right_pair[2] + down_pair[2] - left_pair[2] - upper_pair[2]) / denominator
    return log_gain, offset


def masked_terms(stats, present):
    return tuple(jnp.where(present, item, 0.0) for item in pair_terms(stats))


def local(tiles, extents, offsets, bands):
    planes, tile_px, _ = tiles.shape
    n_row = lax.axis_size("row")
    n_col = lax.axis_size("col")
    row_index = lax.axis_index("row")
    col_index = lax.axis_index("col")
    width = STRIP

    right_strip = tiles[:, :, tile_px - width :]
    down_strip = tiles[:, tile_px - width :, :]
    left_strip = tiles[:, :, :width]
    up_strip = tiles[:, :width, :]
    corner = tiles[:, tile_px - width :, tile_px - width :]
    from_left = shifted(right_strip, "col", n_col, 1)
    from_up = shifted(down_strip, "row", n_row, 1)
    from_right = shifted(left_strip, "col", n_col, -1)
    from_down = shifted(up_strip, "row", n_row, -1)
    diagonal = [
        (j * n_row + i, (j + 1) * n_row + i + 1) for i in range(n_row - 1) for j in range(n_col - 1)
    ]
    from_corner = lax.ppermute(corner, ("col", "row"), diagonal)

    left_col = jnp.maximum(col_index - 1, 0)
    upper_row = jnp.maximum(row_index - 1, 0)
    strip_ids = jnp.arange(width, dtype=jnp.int32)

    def across(extent):
        return (strip_ids < extent).astype(jnp.float32)[None, None, :]

    def along(extent):
        return (strip_ids < extent).astype(jnp.float32)[None, :, None]

    f32 = jnp.float32
    right_stats = strip_stats(
        right_strip.astype(f32), from_right.astype(f32), across(extents[0, row_index, col_index])
    )
    down_stats = strip_stats(
        down_strip.astype(f32), from_down.astype(f32), along(extents[1, row_index, col_index])
    )
    left_stats = strip_stats(
        from_left.astype(f32), left_strip.astype(f32), across(extents[0, row_index, left_col])
    )
    up_stats = strip_stats(
        from_up.astype(f32), up_strip.astype(f32), along(extents[1, upper_row, col_index])
    )
    has_right = col_index < n_col - 1
    has_down = row_index < n_row - 1
    has_left_pair = col_index > 0
    has_up_pair = row_index > 0
    gain_one, level_one = combine(
        masked_terms(right_stats, has_right),
        masked_terms(down_stats, has_down),
        masked_terms(left_stats, has_left_pair),
        masked_terms(up_stats, has_up_pair),
    )
    first = jnp.concatenate([gain_one, level_one])
    near = [
        shifted(first, "col", n_col, -1),
        shifted(first, "row", n_row, -1),
        shifted(first, "col", n_col, 1),
        shifted(first, "row", n_row, 1),
    ]
    scale = jnp.exp(gain_one)
    near_scale = [jnp.exp(item[:planes]) for item in near]
    near_level = [item[planes:] for item in near]
    right_two = corrected_stats(right_stats, scale, level_one, near_scale[0], near_level[0])
    down_two = corrected_stats(down_stats, scale, level_one, near_scale[1], near_level[1])
    left_two = corrected_stats(left_stats, near_scale[2], near_level[2], scale, level_one)
    up_two = corrected_stats(up_stats, near_scale[3], near_level[3], scale, level_one)
    gain_two, level_two = combine(
        masked_terms(right_two, has_right),
        masked_terms(down_two, has_down),
        masked_terms(left_two, has_left_pair),
        masked_terms(up_two, has_up_pair),
    )
    own_gain = gain_one + gain_two
    own_level = jnp.exp(gain_two) * level_one + level_two
    final = jnp.concatenate([own_gain, own_level])
    final_left = shifted(final, "col", n_col, 1)
    final_up = shifted(final, "row", n_row, 1)
    final_corner = lax.ppermute(final, ("col", "row"), diagonal)
    terms = jnp.concatenate([
        jnp.exp(own_gain), own_level,
        jnp.exp(final_left[:planes]), final_left[planes:],
        jnp.exp(final_up[:planes]), final_up[planes:],
        jnp.exp(final_corner[:planes]), final_corner[planes:],
    ])
    idx = jnp.stack([row_index, col_index]).astype(jnp.int32)
    return blend(idx, offsets, bands, terms, tiles, from_left, from_up, from_corner, n_row, n_col)


def solution(mesh):
    return jax.shard_map(
        local,
        mesh=mesh,
        in_specs=(P(None, "row", "col"), P(), P(), P()),
        out_specs=(P(None, "row", "col"), P("row", "col")),
        check_vma=False,
    )
```

```python
import jax
import jax.numpy as jnp
from jax import lax
from jax.sharding import PartitionSpec as P

STRIP = 128
SPILL = 128
BLOCK = 128


eps = 1e-06


def strip_stats(former, latter, window):
    full = jnp.broadcast_to(window, former.shape)
    number = jnp.sum(full, axis=(-2, -1))
    mean_former = jnp.sum(former * full, axis=(-2, -1)) / number
    mean_latter = jnp.sum(latter * full, axis=(-2, -1)) / number
    dev_former = (former - mean_former[:, None, None]) * full
    dev_latter = (latter - mean_latter[:, None, None]) * full
    var_former = jnp.sum(dev_former * dev_former, axis=(-2, -1)) / number
    var_latter = jnp.sum(dev_latter * dev_latter, axis=(-2, -1)) / number
    covariance = jnp.sum(dev_former * dev_latter, axis=(-2, -1)) / number
    return jnp.stack([mean_former, mean_latter, var_former, var_latter, covariance])


def pair_terms(stats):
    mean_former, mean_latter, var_former, var_latter, covariance = stats
    weight = covariance * covariance / ((var_former + eps) * (var_latter + eps))
    log_ratio = 0.25 * (jnp.log(var_latter + eps) - jnp.log(var_former + eps))
    shift_term = 0.5 * (mean_latter - mean_former)
    return (weight, weight * log_ratio, weight * shift_term)


def corrected_stats(stats, gain_a, level_a, gain_b, level_b):
    mean_former, mean_latter, var_former, var_latter, covariance = stats
    return (
        gain_a * mean_former + level_a,
        gain_b * mean_latter + level_b,
        gain_a * gain_a * var_former,
        gain_b * gain_b * var_latter,
        gain_a * gain_b * covariance,
    )


def fade(ids, tile_px):
    return (jnp.minimum(ids, tile_px - 1 - ids) + 1).astype(jnp.float32) / (tile_px / 2.0)


def row_weight(ids, band_low, band_high, tile_px, present):
    live = (ids >= band_low * BLOCK) & (ids < band_high * BLOCK) & (ids >= 0) & (ids < tile_px)
    return live.astype(jnp.float32) * present * fade(ids, tile_px)


def col_weight(ids, tile_px, present):
    live = (ids >= 0) & (ids < tile_px)
    return live.astype(jnp.float32) * present * fade(ids, tile_px)


def piece(source, pads, start, size, rows_w, cols_w, log_gain, level):
    padded = jnp.pad(source, pads)
    zero = jnp.zeros((), jnp.int32)
    window = lax.dynamic_slice(padded, (zero, start[0], start[1]), size)
    weight = rows_w[:, None] * cols_w[None, :]
    values = (
        jnp.exp(log_gain)[:, None, None] * window.astype(jnp.float32) + level[:, None, None]
    ) * weight[None]
    return values, weight


def shifted(block, axis, count, step):
    if step > 0:
        route = [(i, i + 1) for i in range(count - 1)]
    else:
        route = [(i + 1, i) for i in range(count - 1)]
    return lax.ppermute(block, axis, route)


def combine(right_pair, down_pair, left_pair, upper_pair):
    denominator = 1.0 + right_pair[0] + down_pair[0] + left_pair[0] + upper_pair[0]
    log_gain = (right_pair[1] + down_pair[1] - left_pair[1] - upper_pair[1]) / denominator
    offset = (right_pair[2] + down_pair[2] - left_pair[2] - upper_pair[2]) / denominator
    return log_gain, offset


def masked_terms(stats, present):
    return tuple(jnp.where(present, item, 0.0) for item in pair_terms(stats))


def local(tiles, extents, offsets, bands):
    planes, tile_px, _ = tiles.shape
    n_row = lax.axis_size("row")
    n_col = lax.axis_size("col")
    row_index = lax.axis_index("row")
    col_index = lax.axis_index("col")
    width = STRIP

    right_strip = tiles[:, :, tile_px - width :]
    down_strip = tiles[:, tile_px - width :, :]
    left_strip = tiles[:, :, :width]
    up_strip = tiles[:, :width, :]
    corner = tiles[:, tile_px - width :, tile_px - width :]
    from_left = shifted(right_strip, "col", n_col, 1)
    from_up = shifted(down_strip, "row", n_row, 1)
    diagonal = [
        (j * n_row + i, (j + 1) * n_row + i + 1) for i in range(n_row - 1) for j in range(n_col - 1)
    ]
    from_corner = lax.ppermute(corner, ("col", "row"), diagonal)

    left_col = jnp.maximum(col_index - 1, 0)
    upper_row = jnp.maximum(row_index - 1, 0)
    strip_ids = jnp.arange(width, dtype=jnp.int32)

    def across(extent):
        return (strip_ids < extent).astype(jnp.float32)[None, None, :]

    def along(extent):
        return (strip_ids < extent).astype(jnp.float32)[None, :, None]

    f32 = jnp.float32
    left_stats = strip_stats(
        from_left.astype(f32), left_strip.astype(f32), across(extents[0, row_index, left_col])
    )
    up_stats = strip_stats(
        from_up.astype(f32), up_strip.astype(f32), along(extents[1, upper_row, col_index])
    )
    right_stats = shifted(left_stats, "col", n_col, -1)
    down_stats = shifted(up_stats, "row", n_row, -1)
    has_right = col_index < n_col - 1
    has_down = row_index < n_row - 1
    has_left_pair = col_index > 0
    has_up_pair = row_index > 0
    gain_one, level_one = combine(
        masked_terms(right_stats, has_right),
        masked_terms(down_stats, has_down),
        masked_terms(left_stats, has_left_pair),
        masked_terms(up_stats, has_up_pair),
    )
    first = jnp.concatenate([gain_one, level_one])
    near = [
        shifted(first, "col", n_col, -1),
        shifted(first, "row", n_row, -1),
        shifted(first, "col", n_col, 1),
        shifted(first, "row", n_row, 1),
    ]
    scale = jnp.exp(gain_one)
    near_scale = [jnp.exp(item[:planes]) for item in near]
    near_level = [item[planes:] for item in near]
    right_two = corrected_stats(right_stats, scale, level_one, near_scale[0], near_level[0])
    down_two = corrected_stats(down_stats, scale, level_one, near_scale[1], near_level[1])
    left_two = corrected_stats(left_stats, near_scale[2], near_level[2], scale, level_one)
    up_two = corrected_stats(up_stats, near_scale[3], near_level[3], scale, level_one)
    gain_two, level_two = combine(
        masked_terms(right_two, has_right),
        masked_terms(down_two, has_down),
        masked_terms(left_two, has_left_pair),
        masked_terms(up_two, has_up_pair),
    )
    own_gain = gain_one + gain_two
    own_level = jnp.exp(gain_two) * level_one + level_two
    final = jnp.concatenate([own_gain, own_level])
    final_left = shifted(final, "col", n_col, 1)
    final_up = shifted(final, "row", n_row, 1)
    final_corner = lax.ppermute(final, ("col", "row"), diagonal)
    found = {
        "own": (own_gain, own_level),
        "left": (final_left[:planes], final_left[planes:]),
        "up": (final_up[:planes], final_up[planes:]),
        "corner": (final_corner[:planes], final_corner[planes:]),
    }

    def terms_at(which):
        return found[which]

    has_left = (col_index > 0).astype(jnp.float32)
    has_up = (row_index > 0).astype(jnp.float32)
    ids = jnp.arange(tile_px, dtype=jnp.int32)
    edge = jnp.arange(width, dtype=jnp.int32)

    def weights_of(r, c, row_ids, col_ids, present):
        rows_w = row_weight(row_ids, bands[0, r, c], bands[1, r, c], tile_px, present)
        cols_w = col_weight(col_ids, tile_px, jnp.float32(1.0))
        return rows_w, cols_w

    top, left = offsets[0, row_index, col_index], offsets[1, row_index, col_index]
    rows_w, cols_w = weights_of(row_index, col_index, ids - top, ids - left, jnp.float32(1.0))
    own_vals, own_w = piece(
        tiles, ((0, 0), (SPILL, 0), (SPILL, 0)), (SPILL - top, SPILL - left),
        (planes, tile_px, tile_px), rows_w, cols_w, *terms_at("own"),
    )
    top_l, left_l = offsets[0, row_index, left_col], offsets[1, row_index, left_col]
    rows_w, cols_w = weights_of(
        row_index, left_col, ids - top_l, edge + tile_px - left_l, has_left
    )
    left_vals, left_w = piece(
        from_left, ((0, 0), (SPILL, 0), (0, width)), (SPILL - top_l, width - left_l),
        (planes, tile_px, width), rows_w, cols_w, *terms_at("left"),
    )
    top_u, left_u = offsets[0, upper_row, col_index], offsets[1, upper_row, col_index]
    rows_w, cols_w = weights_of(
        upper_row, col_index, edge + tile_px - top_u, ids - left_u, has_up
    )
    up_vals, up_w = piece(
        from_up, ((0, 0), (0, width), (SPILL, 0)), (width - top_u, SPILL - left_u),
        (planes, width, tile_px), rows_w, cols_w, *terms_at("up"),
    )
    top_c, left_c = offsets[0, upper_row, left_col], offsets[1, upper_row, left_col]
    rows_w, cols_w = weights_of(
        upper_row, left_col, edge + tile_px - top_c, edge + tile_px - left_c, has_up * has_left
    )
    corner_vals, corner_w = piece(
        from_corner, ((0, 0), (0, width), (0, width)), (width - top_c, width - left_c),
        (planes, width, width), rows_w, cols_w, *terms_at("corner"),
    )

    blended = own_vals.at[:, :, :width].add(left_vals)
    blended = blended.at[:, :width, :].add(up_vals)
    blended = blended.at[:, :width, :width].add(corner_vals)
    weight = own_w.at[:, :width].add(left_w)
    weight = weight.at[:width, :].add(up_w)
    weight = weight.at[:width, :width].add(corner_w)
    return blended, weight


def solution(mesh):
    return jax.shard_map(
        local,
        mesh=mesh,
        in_specs=(P(None, "row", "col"), P(), P(), P()),
        out_specs=(P(None, "row", "col"), P("row", "col")),
        check_vma=False,
    )
```

```python
import functools

import jax
import jax.numpy as jnp
from jax import lax
from jax.sharding import PartitionSpec as P
from jax.experimental import pallas as pl
from jax.experimental.pallas import tpu as pltpu

STRIP = 128
SPILL = 128
BLOCK = 128
ROWS = 256


eps = 1e-06


def strip_stats(former, latter, window):
    full = jnp.broadcast_to(window, former.shape)
    number = jnp.sum(full, axis=(-2, -1))
    mean_former = jnp.sum(former * full, axis=(-2, -1)) / number
    mean_latter = jnp.sum(latter * full, axis=(-2, -1)) / number
    dev_former = (former - mean_former[:, None, None]) * full
    dev_latter = (latter - mean_latter[:, None, None]) * full
    var_former = jnp.sum(dev_former * dev_former, axis=(-2, -1)) / number
    var_latter = jnp.sum(dev_latter * dev_latter, axis=(-2, -1)) / number
    covariance = jnp.sum(dev_former * dev_latter, axis=(-2, -1)) / number
    return jnp.stack([mean_former, mean_latter, var_former, var_latter, covariance])


def pair_terms(stats):
    mean_former, mean_latter, var_former, var_latter, covariance = stats
    weight = covariance * covariance / ((var_former + eps) * (var_latter + eps))
    log_ratio = 0.25 * (jnp.log(var_latter + eps) - jnp.log(var_former + eps))
    shift_term = 0.5 * (mean_latter - mean_former)
    return (weight, weight * log_ratio, weight * shift_term)


def corrected_stats(stats, gain_a, level_a, gain_b, level_b):
    mean_former, mean_latter, var_former, var_latter, covariance = stats
    return (
        gain_a * mean_former + level_a,
        gain_b * mean_latter + level_b,
        gain_a * gain_a * var_former,
        gain_b * gain_b * var_latter,
        gain_a * gain_b * covariance,
    )


def pick(rows_out, rows_in, shift):
    a = lax.broadcasted_iota(jnp.int32, (rows_out, rows_in), 0)
    b = lax.broadcasted_iota(jnp.int32, (rows_out, rows_in), 1)
    return jnp.where(b == a + shift, 1.0, 0.0).astype(jnp.bfloat16)


def move_lanes(rows, left, lanes, emit):
    width = STRIP
    same = pick(width, width, -left).T
    carry = pick(width, width, width - left).T
    for k in range(lanes // width):
        part = rows[:, k * width : (k + 1) * width]
        block = jnp.dot(part, same, preferred_element_type=jnp.float32)
        if k > 0:
            before = rows[:, (k - 1) * width : k * width]
            block = block + jnp.dot(before, carry, preferred_element_type=jnp.float32)
        emit(k, block)


def blend_kernel(idx_ref, off_ref, band_ref, terms_ref, cur_ref, prev_ref, lcur_ref, lprev_ref,
                 up_ref, corner_ref, out_ref, w_ref, *, n_row, n_col):
    f32 = jnp.float32
    bf16 = jnp.bfloat16
    step = pl.program_id(0)
    planes, rows, tile_px = cur_ref.shape
    width = lcur_ref.shape[2]
    cells = n_row * n_col
    r = idx_ref[0]
    c = idx_ref[1]
    lc = jnp.maximum(c - 1, 0)
    ur = jnp.maximum(r - 1, 0)
    has_left = c > 0
    has_up = r > 0

    def table(ref, k, rr, cc):
        return ref[k * cells + rr * n_col + cc]

    def fade(ids):
        return (jnp.minimum(ids, tile_px - 1 - ids) + 1).astype(f32) / (tile_px / 2.0)

    def band_rows(ids, rr, cc, extra):
        live = (ids >= table(band_ref, 0, rr, cc) * BLOCK) & (ids < table(band_ref, 1, rr, cc) * BLOCK)
        live = live & (ids >= 0) & (ids < tile_px) & extra
        return jnp.where(live, fade(ids), 0.0)

    def gain(k, p):
        return terms_ref[k * 2 * planes + p], terms_ref[k * 2 * planes + planes + p]

    t = lax.broadcasted_iota(jnp.int32, (rows, 1), 0)
    x = lax.broadcasted_iota(jnp.int32, (1, tile_px), 1)
    xs = lax.broadcasted_iota(jnp.int32, (1, width), 1)
    y = step * rows + t
    top = table(off_ref, 0, r, c)
    left = table(off_ref, 1, r, c)
    top_l = table(off_ref, 0, r, lc)
    left_l = table(off_ref, 1, r, lc)
    j = x - left
    w_own = band_rows(y - top, r, c, True) * jnp.where(j >= 0, fade(j), 0.0)
    j_l = xs + tile_px - left_l
    w_left = band_rows(y - top_l, r, lc, has_left) * jnp.where(j_l < tile_px, fade(j_l), 0.0)
    w_ref[...] = w_own
    w_ref[:, :width] += w_left
    down_own = pick(rows, 2 * rows, rows - top)
    down_left = pick(rows, 2 * rows, rows - top_l)
    carry_left = pick(width, width, width - left_l).T
    for p in range(planes):
        src = jnp.concatenate([prev_ref[p], cur_ref[p]], axis=0)
        shifted_rows = jnp.dot(down_own, src, preferred_element_type=f32).astype(bf16)
        scale, level = gain(0, p)

        def emit(k, block, p=p, scale=scale, level=level):
            span = slice(k * width, (k + 1) * width)
            out_ref[p, :, span] = (scale * block + level) * w_own[:, span]

        move_lanes(shifted_rows, left, tile_px, emit)
        lsrc = jnp.concatenate([lprev_ref[p], lcur_ref[p]], axis=0)
        lrows = jnp.dot(down_left, lsrc, preferred_element_type=f32).astype(bf16)
        window = jnp.dot(lrows, carry_left, preferred_element_type=f32)
        scale, level = gain(1, p)
        out_ref[p, :, :width] += (scale * window + level) * w_left

    @pl.when(step == 0)
    def _():
        te = lax.broadcasted_iota(jnp.int32, (width, 1), 0)
        top_u = table(off_ref, 0, ur, c)
        left_u = table(off_ref, 1, ur, c)
        top_c = table(off_ref, 0, ur, lc)
        left_c = table(off_ref, 1, ur, lc)
        j_u = x - left_u
        w_up = band_rows(te + tile_px - top_u, ur, c, has_up) * jnp.where(j_u >= 0, fade(j_u), 0.0)
        j_c = xs + tile_px - left_c
        w_corner = band_rows(te + tile_px - top_c, ur, lc, has_up & has_left) * jnp.where(
            j_c < tile_px, fade(j_c), 0.0
        )
        w_ref[:width, :] += w_up
        w_ref[:width, :width] += w_corner
        down_up = pick(width, width, width - top_u)
        down_corner = pick(width, width, width - top_c)
        carry_corner = pick(width, width, width - left_c).T
        for p in range(planes):
            urows = jnp.dot(down_up, up_ref[p], preferred_element_type=f32).astype(bf16)
            scale, level = gain(2, p)

            def emit(k, block, p=p, scale=scale, level=level):
                span = slice(k * width, (k + 1) * width)
                out_ref[p, :width, span] += (scale * block + level) * w_up[:, span]

            move_lanes(urows, left_u, tile_px, emit)
            crows = jnp.dot(down_corner, corner_ref[p], preferred_element_type=f32).astype(bf16)
            window = jnp.dot(crows, carry_corner, preferred_element_type=f32)
            scale, level = gain(3, p)
            out_ref[p, :width, :width] += (scale * window + level) * w_corner


def blend(idx, offsets, bands, terms, tiles, from_left, from_up, from_corner, n_row, n_col):
    planes, tile_px, _ = tiles.shape
    width = from_left.shape[2]
    rows = min(ROWS, tile_px)
    steps = tile_px // rows

    def cur(b, *_):
        return (0, b, 0)

    def prev(b, *_):
        return (0, jnp.maximum(b - 1, 0), 0)

    def fixed(b, *_):
        return (0, 0, 0)

    grid_spec = pltpu.PrefetchScalarGridSpec(
        num_scalar_prefetch=3,
        grid=(steps,),
        in_specs=[
            pl.BlockSpec(memory_space=pltpu.SMEM),
            pl.BlockSpec((planes, rows, tile_px), cur),
            pl.BlockSpec((planes, rows, tile_px), prev),
            pl.BlockSpec((planes, rows, width), cur),
            pl.BlockSpec((planes, rows, width), prev),
            pl.BlockSpec((planes, width, tile_px), fixed),
            pl.BlockSpec((planes, width, width), fixed),
        ],
        out_specs=[
            pl.BlockSpec((planes, rows, tile_px), cur),
            pl.BlockSpec((rows, tile_px), lambda b, *_: (b, 0)),
        ],
    )
    out_bytes = 4 * (planes + 1) * tile_px * tile_px
    in_bytes = 2 * 2 * planes * tile_px * (tile_px + width)
    return pl.pallas_call(
        functools.partial(blend_kernel, n_row=n_row, n_col=n_col),
        grid_spec=grid_spec,
        out_shape=[
            jax.ShapeDtypeStruct((planes, tile_px, tile_px), jnp.float32),
            jax.ShapeDtypeStruct((tile_px, tile_px), jnp.float32),
        ],
        compiler_params=pltpu.CompilerParams(dimension_semantics=("arbitrary",)),
        cost_estimate=pl.CostEstimate(
            flops=12 * planes * tile_px * tile_px, transcendentals=0,
            bytes_accessed=out_bytes + in_bytes,
        ),
    )(idx, offsets.reshape(-1), bands.reshape(-1), terms, tiles, tiles, from_left, from_left,
      from_up, from_corner)


def shifted(block, axis, count, step):
    if step > 0:
        route = [(i, i + 1) for i in range(count - 1)]
    else:
        route = [(i + 1, i) for i in range(count - 1)]
    return lax.ppermute(block, axis, route)


def combine(right_pair, down_pair, left_pair, upper_pair):
    denominator = 1.0 + right_pair[0] + down_pair[0] + left_pair[0] + upper_pair[0]
    log_gain = (right_pair[1] + down_pair[1] - left_pair[1] - upper_pair[1]) / denominator
    offset = (right_pair[2] + down_pair[2] - left_pair[2] - upper_pair[2]) / denominator
    return log_gain, offset


def masked_terms(stats, present):
    return tuple(jnp.where(present, item, 0.0) for item in pair_terms(stats))


def local(tiles, extents, offsets, bands):
    planes, tile_px, _ = tiles.shape
    n_row = lax.axis_size("row")
    n_col = lax.axis_size("col")
    row_index = lax.axis_index("row")
    col_index = lax.axis_index("col")
    width = STRIP

    right_strip = tiles[:, :, tile_px - width :]
    down_strip = tiles[:, tile_px - width :, :]
    left_strip = tiles[:, :, :width]
    up_strip = tiles[:, :width, :]
    corner = tiles[:, tile_px - width :, tile_px - width :]
    from_left = shifted(right_strip, "col", n_col, 1)
    from_up = shifted(down_strip, "row", n_row, 1)
    diagonal = [
        (j * n_row + i, (j + 1) * n_row + i + 1) for i in range(n_row - 1) for j in range(n_col - 1)
    ]
    from_corner = lax.ppermute(corner, ("col", "row"), diagonal)

    left_col = jnp.maximum(col_index - 1, 0)
    upper_row = jnp.maximum(row_index - 1, 0)
    strip_ids = jnp.arange(width, dtype=jnp.int32)

    def across(extent):
        return (strip_ids < extent).astype(jnp.float32)[None, None, :]

    def along(extent):
        return (strip_ids < extent).astype(jnp.float32)[None, :, None]

    f32 = jnp.float32
    left_stats = strip_stats(
        from_left.astype(f32), left_strip.astype(f32), across(extents[0, row_index, left_col])
    )
    up_stats = strip_stats(
        from_up.astype(f32), up_strip.astype(f32), along(extents[1, upper_row, col_index])
    )
    right_stats = shifted(left_stats, "col", n_col, -1)
    down_stats = shifted(up_stats, "row", n_row, -1)
    has_right = col_index < n_col - 1
    has_down = row_index < n_row - 1
    has_left_pair = col_index > 0
    has_up_pair = row_index > 0
    gain_one, level_one = combine(
        masked_terms(right_stats, has_right),
        masked_terms(down_stats, has_down),
        masked_terms(left_stats, has_left_pair),
        masked_terms(up_stats, has_up_pair),
    )
    first = jnp.concatenate([gain_one, level_one])
    near = [
        shifted(first, "col", n_col, -1),
        shifted(first, "row", n_row, -1),
        shifted(first, "col", n_col, 1),
        shifted(first, "row", n_row, 1),
    ]
    scale = jnp.exp(gain_one)
    near_scale = [jnp.exp(item[:planes]) for item in near]
    near_level = [item[planes:] for item in near]
    right_two = corrected_stats(right_stats, scale, level_one, near_scale[0], near_level[0])
    down_two = corrected_stats(down_stats, scale, level_one, near_scale[1], near_level[1])
    left_two = corrected_stats(left_stats, near_scale[2], near_level[2], scale, level_one)
    up_two = corrected_stats(up_stats, near_scale[3], near_level[3], scale, level_one)
    gain_two, level_two = combine(
        masked_terms(right_two, has_right),
        masked_terms(down_two, has_down),
        masked_terms(left_two, has_left_pair),
        masked_terms(up_two, has_up_pair),
    )
    own_gain = gain_one + gain_two
    own_level = jnp.exp(gain_two) * level_one + level_two
    final = jnp.concatenate([own_gain, own_level])
    final_left = shifted(final, "col", n_col, 1)
    final_up = shifted(final, "row", n_row, 1)
    final_corner = lax.ppermute(final, ("col", "row"), diagonal)
    terms = jnp.concatenate([
        jnp.exp(own_gain), own_level,
        jnp.exp(final_left[:planes]), final_left[planes:],
        jnp.exp(final_up[:planes]), final_up[planes:],
        jnp.exp(final_corner[:planes]), final_corner[planes:],
    ])
    idx = jnp.stack([row_index, col_index]).astype(jnp.int32)
    return blend(idx, offsets, bands, terms, tiles, from_left, from_up, from_corner, n_row, n_col)


def solution(mesh):
    return jax.shard_map(
        local,
        mesh=mesh,
        in_specs=(P(None, "row", "col"), P(), P(), P()),
        out_specs=(P(None, "row", "col"), P("row", "col")),
        check_vma=False,
    )
```

```python
import functools

import jax
import jax.numpy as jnp
from jax import lax
from jax.sharding import PartitionSpec as P
from jax.experimental import pallas as pl
from jax.experimental.pallas import tpu as pltpu

STRIP = 128
SPILL = 128
BLOCK = 128
ROWS = 256


eps = 1e-06


def strip_stats(former, latter, window):
    full = jnp.broadcast_to(window, former.shape)
    number = jnp.sum(full, axis=(-2, -1))
    mean_former = jnp.sum(former * full, axis=(-2, -1)) / number
    mean_latter = jnp.sum(latter * full, axis=(-2, -1)) / number
    dev_former = (former - mean_former[:, None, None]) * full
    dev_latter = (latter - mean_latter[:, None, None]) * full
    var_former = jnp.sum(dev_former * dev_former, axis=(-2, -1)) / number
    var_latter = jnp.sum(dev_latter * dev_latter, axis=(-2, -1)) / number
    covariance = jnp.sum(dev_former * dev_latter, axis=(-2, -1)) / number
    return jnp.stack([mean_former, mean_latter, var_former, var_latter, covariance])


def pair_terms(stats):
    mean_former, mean_latter, var_former, var_latter, covariance = stats
    weight = covariance * covariance / ((var_former + eps) * (var_latter + eps))
    log_ratio = 0.25 * (jnp.log(var_latter + eps) - jnp.log(var_former + eps))
    shift_term = 0.5 * (mean_latter - mean_former)
    return (weight, weight * log_ratio, weight * shift_term)


def corrected_stats(stats, gain_a, level_a, gain_b, level_b):
    mean_former, mean_latter, var_former, var_latter, covariance = stats
    return (
        gain_a * mean_former + level_a,
        gain_b * mean_latter + level_b,
        gain_a * gain_a * var_former,
        gain_b * gain_b * var_latter,
        gain_a * gain_b * covariance,
    )


def pick(rows_out, rows_in, shift):
    a = lax.broadcasted_iota(jnp.int32, (rows_out, rows_in), 0)
    b = lax.broadcasted_iota(jnp.int32, (rows_out, rows_in), 1)
    return jnp.where(b == a + shift, 1.0, 0.0).astype(jnp.bfloat16)


def move_lanes(rows, left, lanes, emit):
    width = STRIP
    same = pick(width, width, -left).T
    both = pick(width, 2 * width, width - left).T
    for k in range(lanes // width):
        if k == 0:
            block = jnp.dot(rows[:, :width], same, preferred_element_type=jnp.float32)
        else:
            pair = rows[:, (k - 1) * width : (k + 1) * width]
            block = jnp.dot(pair, both, preferred_element_type=jnp.float32)
        emit(k, block)


def blend_kernel(idx_ref, off_ref, band_ref, terms_ref, cur_ref, prev_ref, lcur_ref, lprev_ref,
                 up_ref, corner_ref, out_ref, w_ref, *, n_row, n_col):
    f32 = jnp.float32
    bf16 = jnp.bfloat16
    step = pl.program_id(0)
    planes, rows, tile_px = cur_ref.shape
    width = lcur_ref.shape[2]
    cells = n_row * n_col
    r = idx_ref[0]
    c = idx_ref[1]
    lc = jnp.maximum(c - 1, 0)
    ur = jnp.maximum(r - 1, 0)
    has_left = c > 0
    has_up = r > 0

    def table(ref, k, rr, cc):
        return ref[k * cells + rr * n_col + cc]

    def fade(ids):
        return (jnp.minimum(ids, tile_px - 1 - ids) + 1).astype(f32) / (tile_px / 2.0)

    def band_rows(ids, rr, cc, extra):
        live = (ids >= table(band_ref, 0, rr, cc) * BLOCK) & (ids < table(band_ref, 1, rr, cc) * BLOCK)
        live = live & (ids >= 0) & (ids < tile_px) & extra
        return jnp.where(live, fade(ids), 0.0)

    def gain(k, p):
        return terms_ref[k * 2 * planes + p], terms_ref[k * 2 * planes + planes + p]

    t = lax.broadcasted_iota(jnp.int32, (rows, 1), 0)
    x = lax.broadcasted_iota(jnp.int32, (1, tile_px), 1)
    xs = lax.broadcasted_iota(jnp.int32, (1, width), 1)
    y = step * rows + t
    top = table(off_ref, 0, r, c)
    left = table(off_ref, 1, r, c)
    top_l = table(off_ref, 0, r, lc)
    left_l = table(off_ref, 1, r, lc)
    j = x - left
    w_own = band_rows(y - top, r, c, True) * jnp.where(j >= 0, fade(j), 0.0)
    j_l = xs + tile_px - left_l
    w_left = band_rows(y - top_l, r, lc, has_left) * jnp.where(j_l < tile_px, fade(j_l), 0.0)
    w_ref[...] = w_own
    w_ref[:, :width] += w_left
    reach = SPILL
    down_own = pick(rows, reach + rows, reach - top)
    down_left = pick(rows, reach + rows, reach - top_l)
    carry_left = pick(width, width, width - left_l).T
    for p in range(planes):
        src = jnp.concatenate([prev_ref[p, rows - reach :], cur_ref[p]], axis=0)
        shifted_rows = jnp.dot(down_own, src, preferred_element_type=f32).astype(bf16)
        scale, level = gain(0, p)

        def emit(k, block, p=p, scale=scale, level=level):
            span = slice(k * width, (k + 1) * width)
            out_ref[p, :, span] = (scale * block + level) * w_own[:, span]

        move_lanes(shifted_rows, left, tile_px, emit)
        lsrc = jnp.concatenate([lprev_ref[p, rows - reach :], lcur_ref[p]], axis=0)
        lrows = jnp.dot(down_left, lsrc, preferred_element_type=f32).astype(bf16)
        window = jnp.dot(lrows, carry_left, preferred_element_type=f32)
        scale, level = gain(1, p)
        out_ref[p, :, :width] += (scale * window + level) * w_left

    @pl.when(step == 0)
    def _():
        te = lax.broadcasted_iota(jnp.int32, (width, 1), 0)
        top_u = table(off_ref, 0, ur, c)
        left_u = table(off_ref, 1, ur, c)
        top_c = table(off_ref, 0, ur, lc)
        left_c = table(off_ref, 1, ur, lc)
        j_u = x - left_u
        w_up = band_rows(te + tile_px - top_u, ur, c, has_up) * jnp.where(j_u >= 0, fade(j_u), 0.0)
        j_c = xs + tile_px - left_c
        w_corner = band_rows(te + tile_px - top_c, ur, lc, has_up & has_left) * jnp.where(
            j_c < tile_px, fade(j_c), 0.0
        )
        w_ref[:width, :] += w_up
        w_ref[:width, :width] += w_corner
        down_up = pick(width, width, width - top_u)
        down_corner = pick(width, width, width - top_c)
        carry_corner = pick(width, width, width - left_c).T
        for p in range(planes):
            urows = jnp.dot(down_up, up_ref[p], preferred_element_type=f32).astype(bf16)
            scale, level = gain(2, p)

            def emit(k, block, p=p, scale=scale, level=level):
                span = slice(k * width, (k + 1) * width)
                out_ref[p, :width, span] += (scale * block + level) * w_up[:, span]

            move_lanes(urows, left_u, tile_px, emit)
            crows = jnp.dot(down_corner, corner_ref[p], preferred_element_type=f32).astype(bf16)
            window = jnp.dot(crows, carry_corner, preferred_element_type=f32)
            scale, level = gain(3, p)
            out_ref[p, :width, :width] += (scale * window + level) * w_corner


def blend(idx, offsets, bands, terms, tiles, from_left, from_up, from_corner, n_row, n_col):
    planes, tile_px, _ = tiles.shape
    width = from_left.shape[2]
    rows = min(ROWS, tile_px)
    steps = tile_px // rows

    def cur(b, *_):
        return (0, b, 0)

    def prev(b, *_):
        return (0, jnp.maximum(b - 1, 0), 0)

    def fixed(b, *_):
        return (0, 0, 0)

    grid_spec = pltpu.PrefetchScalarGridSpec(
        num_scalar_prefetch=3,
        grid=(steps,),
        in_specs=[
            pl.BlockSpec(memory_space=pltpu.SMEM),
            pl.BlockSpec((planes, rows, tile_px), cur),
            pl.BlockSpec((planes, rows, tile_px), prev),
            pl.BlockSpec((planes, rows, width), cur),
            pl.BlockSpec((planes, rows, width), prev),
            pl.BlockSpec((planes, width, tile_px), fixed),
            pl.BlockSpec((planes, width, width), fixed),
        ],
        out_specs=[
            pl.BlockSpec((planes, rows, tile_px), cur),
            pl.BlockSpec((rows, tile_px), lambda b, *_: (b, 0)),
        ],
    )
    out_bytes = 4 * (planes + 1) * tile_px * tile_px
    in_bytes = 2 * 2 * planes * tile_px * (tile_px + width)
    return pl.pallas_call(
        functools.partial(blend_kernel, n_row=n_row, n_col=n_col),
        grid_spec=grid_spec,
        out_shape=[
            jax.ShapeDtypeStruct((planes, tile_px, tile_px), jnp.float32),
            jax.ShapeDtypeStruct((tile_px, tile_px), jnp.float32),
        ],
        compiler_params=pltpu.CompilerParams(dimension_semantics=("arbitrary",)),
        cost_estimate=pl.CostEstimate(
            flops=12 * planes * tile_px * tile_px, transcendentals=0,
            bytes_accessed=out_bytes + in_bytes,
        ),
    )(idx, offsets.reshape(-1), bands.reshape(-1), terms, tiles, tiles, from_left, from_left,
      from_up, from_corner)


def shifted(block, axis, count, step):
    if step > 0:
        route = [(i, i + 1) for i in range(count - 1)]
    else:
        route = [(i + 1, i) for i in range(count - 1)]
    return lax.ppermute(block, axis, route)


def combine(right_pair, down_pair, left_pair, upper_pair):
    denominator = 1.0 + right_pair[0] + down_pair[0] + left_pair[0] + upper_pair[0]
    log_gain = (right_pair[1] + down_pair[1] - left_pair[1] - upper_pair[1]) / denominator
    offset = (right_pair[2] + down_pair[2] - left_pair[2] - upper_pair[2]) / denominator
    return log_gain, offset


def masked_terms(stats, present):
    return tuple(jnp.where(present, item, 0.0) for item in pair_terms(stats))


def local(tiles, extents, offsets, bands):
    planes, tile_px, _ = tiles.shape
    n_row = lax.axis_size("row")
    n_col = lax.axis_size("col")
    row_index = lax.axis_index("row")
    col_index = lax.axis_index("col")
    width = STRIP

    right_strip = tiles[:, :, tile_px - width :]
    down_strip = tiles[:, tile_px - width :, :]
    left_strip = tiles[:, :, :width]
    up_strip = tiles[:, :width, :]
    corner = tiles[:, tile_px - width :, tile_px - width :]
    from_left = shifted(right_strip, "col", n_col, 1)
    from_up = shifted(down_strip, "row", n_row, 1)
    diagonal = [
        (j * n_row + i, (j + 1) * n_row + i + 1) for i in range(n_row - 1) for j in range(n_col - 1)
    ]
    from_corner = lax.ppermute(corner, ("col", "row"), diagonal)

    left_col = jnp.maximum(col_index - 1, 0)
    upper_row = jnp.maximum(row_index - 1, 0)
    strip_ids = jnp.arange(width, dtype=jnp.int32)

    def across(extent):
        return (strip_ids < extent).astype(jnp.float32)[None, None, :]

    def along(extent):
        return (strip_ids < extent).astype(jnp.float32)[None, :, None]

    f32 = jnp.float32
    left_stats = strip_stats(
        from_left.astype(f32), left_strip.astype(f32), across(extents[0, row_index, left_col])
    )
    up_stats = strip_stats(
        from_up.astype(f32), up_strip.astype(f32), along(extents[1, upper_row, col_index])
    )
    right_stats = shifted(left_stats, "col", n_col, -1)
    down_stats = shifted(up_stats, "row", n_row, -1)
    has_right = col_index < n_col - 1
    has_down = row_index < n_row - 1
    has_left_pair = col_index > 0
    has_up_pair = row_index > 0
    gain_one, level_one = combine(
        masked_terms(right_stats, has_right),
        masked_terms(down_stats, has_down),
        masked_terms(left_stats, has_left_pair),
        masked_terms(up_stats, has_up_pair),
    )
    first = jnp.concatenate([gain_one, level_one])
    near = [
        shifted(first, "col", n_col, -1),
        shifted(first, "row", n_row, -1),
        shifted(first, "col", n_col, 1),
        shifted(first, "row", n_row, 1),
    ]
    scale = jnp.exp(gain_one)
    near_scale = [jnp.exp(item[:planes]) for item in near]
    near_level = [item[planes:] for item in near]
    right_two = corrected_stats(right_stats, scale, level_one, near_scale[0], near_level[0])
    down_two = corrected_stats(down_stats, scale, level_one, near_scale[1], near_level[1])
    left_two = corrected_stats(left_stats, near_scale[2], near_level[2], scale, level_one)
    up_two = corrected_stats(up_stats, near_scale[3], near_level[3], scale, level_one)
    gain_two, level_two = combine(
        masked_terms(right_two, has_right),
        masked_terms(down_two, has_down),
        masked_terms(left_two, has_left_pair),
        masked_terms(up_two, has_up_pair),
    )
    own_gain = gain_one + gain_two
    own_level = jnp.exp(gain_two) * level_one + level_two
    final = jnp.concatenate([own_gain, own_level])
    final_left = shifted(final, "col", n_col, 1)
    final_up = shifted(final, "row", n_row, 1)
    final_corner = lax.ppermute(final, ("col", "row"), diagonal)
    terms = jnp.concatenate([
        jnp.exp(own_gain), own_level,
        jnp.exp(final_left[:planes]), final_left[planes:],
        jnp.exp(final_up[:planes]), final_up[planes:],
        jnp.exp(final_corner[:planes]), final_corner[planes:],
    ])
    idx = jnp.stack([row_index, col_index]).astype(jnp.int32)
    return blend(idx, offsets, bands, terms, tiles, from_left, from_up, from_corner, n_row, n_col)


def solution(mesh):
    return jax.shard_map(
        local,
        mesh=mesh,
        in_specs=(P(None, "row", "col"), P(), P(), P()),
        out_specs=(P(None, "row", "col"), P("row", "col")),
        check_vma=False,
    )
```

```python
import functools

import jax
import jax.numpy as jnp
from jax import lax
from jax.sharding import PartitionSpec as P
from jax.experimental import pallas as pl
from jax.experimental.pallas import tpu as pltpu

STRIP = 128
SPILL = 128
BLOCK = 128
ROWS = 256


eps = 1e-06


def strip_stats(former, latter, window):
    full = jnp.broadcast_to(window, former.shape)
    number = jnp.sum(full, axis=(-2, -1))
    mean_former = jnp.sum(former * full, axis=(-2, -1)) / number
    mean_latter = jnp.sum(latter * full, axis=(-2, -1)) / number
    dev_former = (former - mean_former[:, None, None]) * full
    dev_latter = (latter - mean_latter[:, None, None]) * full
    var_former = jnp.sum(dev_former * dev_former, axis=(-2, -1)) / number
    var_latter = jnp.sum(dev_latter * dev_latter, axis=(-2, -1)) / number
    covariance = jnp.sum(dev_former * dev_latter, axis=(-2, -1)) / number
    return jnp.stack([mean_former, mean_latter, var_former, var_latter, covariance])


def pair_terms(stats):
    mean_former, mean_latter, var_former, var_latter, covariance = stats
    weight = covariance * covariance / ((var_former + eps) * (var_latter + eps))
    log_ratio = 0.25 * (jnp.log(var_latter + eps) - jnp.log(var_former + eps))
    shift_term = 0.5 * (mean_latter - mean_former)
    return (weight, weight * log_ratio, weight * shift_term)


def corrected_stats(stats, gain_a, level_a, gain_b, level_b):
    mean_former, mean_latter, var_former, var_latter, covariance = stats
    return (
        gain_a * mean_former + level_a,
        gain_b * mean_latter + level_b,
        gain_a * gain_a * var_former,
        gain_b * gain_b * var_latter,
        gain_a * gain_b * covariance,
    )


def pick(rows_out, rows_in, shift):
    a = lax.broadcasted_iota(jnp.int32, (rows_out, rows_in), 0)
    b = lax.broadcasted_iota(jnp.int32, (rows_out, rows_in), 1)
    return jnp.where(b == a + shift, 1.0, 0.0).astype(jnp.bfloat16)


def move_lanes(rows, left, lanes, emit):
    width = STRIP
    lane = lax.broadcasted_iota(jnp.int32, (1, width), 1)
    before = None
    for k in range(lanes // width):
        turned = pltpu.roll(rows[:, k * width : (k + 1) * width], left, 1)
        block = turned if before is None else jnp.where(lane >= left, turned, before)
        before = turned
        emit(k, block)


def blend_kernel(idx_ref, off_ref, band_ref, terms_ref, cur_ref, prev_ref, lcur_ref, lprev_ref,
                 up_ref, corner_ref, out_ref, w_ref, *, n_row, n_col):
    f32 = jnp.float32
    bf16 = jnp.bfloat16
    step = pl.program_id(0)
    planes, rows, tile_px = cur_ref.shape
    width = lcur_ref.shape[2]
    cells = n_row * n_col
    r = idx_ref[0]
    c = idx_ref[1]
    lc = jnp.maximum(c - 1, 0)
    ur = jnp.maximum(r - 1, 0)
    has_left = c > 0
    has_up = r > 0

    def table(ref, k, rr, cc):
        return ref[k * cells + rr * n_col + cc]

    def fade(ids):
        return (jnp.minimum(ids, tile_px - 1 - ids) + 1).astype(f32) / (tile_px / 2.0)

    def band_rows(ids, rr, cc, extra):
        live = (ids >= table(band_ref, 0, rr, cc) * BLOCK) & (ids < table(band_ref, 1, rr, cc) * BLOCK)
        live = live & (ids >= 0) & (ids < tile_px) & extra
        return jnp.where(live, fade(ids), 0.0)

    def gain(k, p):
        return terms_ref[k * 2 * planes + p], terms_ref[k * 2 * planes + planes + p]

    t = lax.broadcasted_iota(jnp.int32, (rows, 1), 0)
    x = lax.broadcasted_iota(jnp.int32, (1, tile_px), 1)
    xs = lax.broadcasted_iota(jnp.int32, (1, width), 1)
    y = step * rows + t
    top = table(off_ref, 0, r, c)
    left = table(off_ref, 1, r, c)
    top_l = table(off_ref, 0, r, lc)
    left_l = table(off_ref, 1, r, lc)
    j = x - left
    w_own = band_rows(y - top, r, c, True) * jnp.where(j >= 0, fade(j), 0.0)
    j_l = xs + tile_px - left_l
    w_left = band_rows(y - top_l, r, lc, has_left) * jnp.where(j_l < tile_px, fade(j_l), 0.0)
    w_ref[...] = w_own
    w_ref[:, :width] += w_left
    reach = SPILL
    down_own = pick(rows, reach + rows, reach - top)
    down_left = pick(rows, reach + rows, reach - top_l)
    for p in range(planes):
        src = jnp.concatenate([prev_ref[p, rows - reach :], cur_ref[p]], axis=0)
        shifted_rows = jnp.dot(down_own, src, preferred_element_type=f32)
        scale, level = gain(0, p)

        def emit(k, block, p=p, scale=scale, level=level):
            span = slice(k * width, (k + 1) * width)
            out_ref[p, :, span] = (scale * block + level) * w_own[:, span]

        move_lanes(shifted_rows, left, tile_px, emit)
        lsrc = jnp.concatenate([lprev_ref[p, rows - reach :], lcur_ref[p]], axis=0)
        lrows = jnp.dot(down_left, lsrc, preferred_element_type=f32)
        window = pltpu.roll(lrows, left_l, 1)
        scale, level = gain(1, p)
        out_ref[p, :, :width] += (scale * window + level) * w_left

    @pl.when(step == 0)
    def _():
        te = lax.broadcasted_iota(jnp.int32, (width, 1), 0)
        top_u = table(off_ref, 0, ur, c)
        left_u = table(off_ref, 1, ur, c)
        top_c = table(off_ref, 0, ur, lc)
        left_c = table(off_ref, 1, ur, lc)
        j_u = x - left_u
        w_up = band_rows(te + tile_px - top_u, ur, c, has_up) * jnp.where(j_u >= 0, fade(j_u), 0.0)
        j_c = xs + tile_px - left_c
        w_corner = band_rows(te + tile_px - top_c, ur, lc, has_up & has_left) * jnp.where(
            j_c < tile_px, fade(j_c), 0.0
        )
        w_ref[:width, :] += w_up
        w_ref[:width, :width] += w_corner
        down_up = pick(width, width, width - top_u)
        down_corner = pick(width, width, width - top_c)
        for p in range(planes):
            urows = jnp.dot(down_up, up_ref[p], preferred_element_type=f32)
            scale, level = gain(2, p)

            def emit(k, block, p=p, scale=scale, level=level):
                span = slice(k * width, (k + 1) * width)
                out_ref[p, :width, span] += (scale * block + level) * w_up[:, span]

            move_lanes(urows, left_u, tile_px, emit)
            crows = jnp.dot(down_corner, corner_ref[p], preferred_element_type=f32)
            window = pltpu.roll(crows, left_c, 1)
            scale, level = gain(3, p)
            out_ref[p, :width, :width] += (scale * window + level) * w_corner


def blend(idx, offsets, bands, terms, tiles, from_left, from_up, from_corner, n_row, n_col):
    planes, tile_px, _ = tiles.shape
    width = from_left.shape[2]
    rows = min(ROWS, tile_px)
    steps = tile_px // rows

    def cur(b, *_):
        return (0, b, 0)

    def prev(b, *_):
        return (0, jnp.maximum(b - 1, 0), 0)

    def fixed(b, *_):
        return (0, 0, 0)

    grid_spec = pltpu.PrefetchScalarGridSpec(
        num_scalar_prefetch=3,
        grid=(steps,),
        in_specs=[
            pl.BlockSpec(memory_space=pltpu.SMEM),
            pl.BlockSpec((planes, rows, tile_px), cur),
            pl.BlockSpec((planes, rows, tile_px), prev),
            pl.BlockSpec((planes, rows, width), cur),
            pl.BlockSpec((planes, rows, width), prev),
            pl.BlockSpec((planes, width, tile_px), fixed),
            pl.BlockSpec((planes, width, width), fixed),
        ],
        out_specs=[
            pl.BlockSpec((planes, rows, tile_px), cur),
            pl.BlockSpec((rows, tile_px), lambda b, *_: (b, 0)),
        ],
    )
    out_bytes = 4 * (planes + 1) * tile_px * tile_px
    in_bytes = 2 * 2 * planes * tile_px * (tile_px + width)
    return pl.pallas_call(
        functools.partial(blend_kernel, n_row=n_row, n_col=n_col),
        grid_spec=grid_spec,
        out_shape=[
            jax.ShapeDtypeStruct((planes, tile_px, tile_px), jnp.float32),
            jax.ShapeDtypeStruct((tile_px, tile_px), jnp.float32),
        ],
        compiler_params=pltpu.CompilerParams(dimension_semantics=("arbitrary",)),
        cost_estimate=pl.CostEstimate(
            flops=12 * planes * tile_px * tile_px, transcendentals=0,
            bytes_accessed=out_bytes + in_bytes,
        ),
    )(idx, offsets.reshape(-1), bands.reshape(-1), terms, tiles, tiles, from_left, from_left,
      from_up, from_corner)


def shifted(block, axis, count, step):
    if step > 0:
        route = [(i, i + 1) for i in range(count - 1)]
    else:
        route = [(i + 1, i) for i in range(count - 1)]
    return lax.ppermute(block, axis, route)


def combine(right_pair, down_pair, left_pair, upper_pair):
    denominator = 1.0 + right_pair[0] + down_pair[0] + left_pair[0] + upper_pair[0]
    log_gain = (right_pair[1] + down_pair[1] - left_pair[1] - upper_pair[1]) / denominator
    offset = (right_pair[2] + down_pair[2] - left_pair[2] - upper_pair[2]) / denominator
    return log_gain, offset


def masked_terms(stats, present):
    return tuple(jnp.where(present, item, 0.0) for item in pair_terms(stats))


def local(tiles, extents, offsets, bands):
    planes, tile_px, _ = tiles.shape
    n_row = lax.axis_size("row")
    n_col = lax.axis_size("col")
    row_index = lax.axis_index("row")
    col_index = lax.axis_index("col")
    width = STRIP

    right_strip = tiles[:, :, tile_px - width :]
    down_strip = tiles[:, tile_px - width :, :]
    left_strip = tiles[:, :, :width]
    up_strip = tiles[:, :width, :]
    corner = tiles[:, tile_px - width :, tile_px - width :]
    from_left = shifted(right_strip, "col", n_col, 1)
    from_up = shifted(down_strip, "row", n_row, 1)
    diagonal = [
        (j * n_row + i, (j + 1) * n_row + i + 1) for i in range(n_row - 1) for j in range(n_col - 1)
    ]
    from_corner = lax.ppermute(corner, ("col", "row"), diagonal)

    left_col = jnp.maximum(col_index - 1, 0)
    upper_row = jnp.maximum(row_index - 1, 0)
    strip_ids = jnp.arange(width, dtype=jnp.int32)

    def across(extent):
        return (strip_ids < extent).astype(jnp.float32)[None, None, :]

    def along(extent):
        return (strip_ids < extent).astype(jnp.float32)[None, :, None]

    f32 = jnp.float32
    left_stats = strip_stats(
        from_left.astype(f32), left_strip.astype(f32), across(extents[0, row_index, left_col])
    )
    up_stats = strip_stats(
        from_up.astype(f32), up_strip.astype(f32), along(extents[1, upper_row, col_index])
    )
    right_stats = shifted(left_stats, "col", n_col, -1)
    down_stats = shifted(up_stats, "row", n_row, -1)
    has_right = col_index < n_col - 1
    has_down = row_index < n_row - 1
    has_left_pair = col_index > 0
    has_up_pair = row_index > 0
    gain_one, level_one = combine(
        masked_terms(right_stats, has_right),
        masked_terms(down_stats, has_down),
        masked_terms(left_stats, has_left_pair),
        masked_terms(up_stats, has_up_pair),
    )
    first = jnp.concatenate([gain_one, level_one])
    near = [
        shifted(first, "col", n_col, -1),
        shifted(first, "row", n_row, -1),
        shifted(first, "col", n_col, 1),
        shifted(first, "row", n_row, 1),
    ]
    scale = jnp.exp(gain_one)
    near_scale = [jnp.exp(item[:planes]) for item in near]
    near_level = [item[planes:] for item in near]
    right_two = corrected_stats(right_stats, scale, level_one, near_scale[0], near_level[0])
    down_two = corrected_stats(down_stats, scale, level_one, near_scale[1], near_level[1])
    left_two = corrected_stats(left_stats, near_scale[2], near_level[2], scale, level_one)
    up_two = corrected_stats(up_stats, near_scale[3], near_level[3], scale, level_one)
    gain_two, level_two = combine(
        masked_terms(right_two, has_right),
        masked_terms(down_two, has_down),
        masked_terms(left_two, has_left_pair),
        masked_terms(up_two, has_up_pair),
    )
    own_gain = gain_one + gain_two
    own_level = jnp.exp(gain_two) * level_one + level_two
    final = jnp.concatenate([own_gain, own_level])
    final_left = shifted(final, "col", n_col, 1)
    final_up = shifted(final, "row", n_row, 1)
    final_corner = lax.ppermute(final, ("col", "row"), diagonal)
    terms = jnp.concatenate([
        jnp.exp(own_gain), own_level,
        jnp.exp(final_left[:planes]), final_left[planes:],
        jnp.exp(final_up[:planes]), final_up[planes:],
        jnp.exp(final_corner[:planes]), final_corner[planes:],
    ])
    idx = jnp.stack([row_index, col_index]).astype(jnp.int32)
    return blend(idx, offsets, bands, terms, tiles, from_left, from_up, from_corner, n_row, n_col)


def solution(mesh):
    return jax.shard_map(
        local,
        mesh=mesh,
        in_specs=(P(None, "row", "col"), P(), P(), P()),
        out_specs=(P(None, "row", "col"), P("row", "col")),
        check_vma=False,
    )
```

```python
import functools

import jax
import jax.numpy as jnp
from jax import lax
from jax.sharding import PartitionSpec as P
from jax.experimental import pallas as pl
from jax.experimental.pallas import tpu as pltpu

STRIP = 128
SPILL = 128
BLOCK = 128
ROWS = 256


eps = 1e-06


def strip_stats(former, latter, window):
    full = jnp.broadcast_to(window, former.shape)
    number = jnp.sum(full, axis=(-2, -1))
    mean_former = jnp.sum(former * full, axis=(-2, -1)) / number
    mean_latter = jnp.sum(latter * full, axis=(-2, -1)) / number
    dev_former = (former - mean_former[:, None, None]) * full
    dev_latter = (latter - mean_latter[:, None, None]) * full
    var_former = jnp.sum(dev_former * dev_former, axis=(-2, -1)) / number
    var_latter = jnp.sum(dev_latter * dev_latter, axis=(-2, -1)) / number
    covariance = jnp.sum(dev_former * dev_latter, axis=(-2, -1)) / number
    return jnp.stack([mean_former, mean_latter, var_former, var_latter, covariance])


def pair_terms(stats):
    mean_former, mean_latter, var_former, var_latter, covariance = stats
    weight = covariance * covariance / ((var_former + eps) * (var_latter + eps))
    log_ratio = 0.25 * (jnp.log(var_latter + eps) - jnp.log(var_former + eps))
    shift_term = 0.5 * (mean_latter - mean_former)
    return (weight, weight * log_ratio, weight * shift_term)


def corrected_stats(stats, gain_a, level_a, gain_b, level_b):
    mean_former, mean_latter, var_former, var_latter, covariance = stats
    return (
        gain_a * mean_former + level_a,
        gain_b * mean_latter + level_b,
        gain_a * gain_a * var_former,
        gain_b * gain_b * var_latter,
        gain_a * gain_b * covariance,
    )


def pick(rows_out, rows_in, shift):
    a = lax.broadcasted_iota(jnp.int32, (rows_out, rows_in), 0)
    b = lax.broadcasted_iota(jnp.int32, (rows_out, rows_in), 1)
    return jnp.where(b == a + shift, 1.0, 0.0).astype(jnp.bfloat16)


def move_lanes(rows, left, lanes, emit):
    width = STRIP
    lane = lax.broadcasted_iota(jnp.int32, (1, width), 1)
    before = None
    for k in range(lanes // width):
        turned = pltpu.roll(rows[:, k * width : (k + 1) * width], left, 1)
        block = turned if before is None else jnp.where(lane >= left, turned, before)
        before = turned
        emit(k, block)


def blend_kernel(off_ref, band_ref, terms_ref, cur_ref, prev_ref, lcur_ref, lprev_ref,
                 up_ref, corner_ref, out_ref, w_ref, *, n_row, n_col):
    f32 = jnp.float32
    bf16 = jnp.bfloat16
    step = pl.program_id(0)
    planes, rows, tile_px = cur_ref.shape
    width = lcur_ref.shape[2]
    cells = n_row * n_col
    r = lax.axis_index("row")
    c = lax.axis_index("col")
    lc = jnp.maximum(c - 1, 0)
    ur = jnp.maximum(r - 1, 0)
    has_left = c > 0
    has_up = r > 0

    def table(ref, k, rr, cc):
        return ref[k, rr, cc]

    def fade(ids):
        return (jnp.minimum(ids, tile_px - 1 - ids) + 1).astype(f32) / (tile_px / 2.0)

    def band_rows(ids, rr, cc, extra):
        live = (ids >= table(band_ref, 0, rr, cc) * BLOCK) & (ids < table(band_ref, 1, rr, cc) * BLOCK)
        live = live & (ids >= 0) & (ids < tile_px) & extra
        return jnp.where(live, fade(ids), 0.0)

    def gain(k, p):
        return terms_ref[k * 2 * planes + p], terms_ref[k * 2 * planes + planes + p]

    t = lax.broadcasted_iota(jnp.int32, (rows, 1), 0)
    x = lax.broadcasted_iota(jnp.int32, (1, tile_px), 1)
    xs = lax.broadcasted_iota(jnp.int32, (1, width), 1)
    y = step * rows + t
    top = table(off_ref, 0, r, c)
    left = table(off_ref, 1, r, c)
    top_l = table(off_ref, 0, r, lc)
    left_l = table(off_ref, 1, r, lc)
    j = x - left
    w_own = band_rows(y - top, r, c, True) * jnp.where(j >= 0, fade(j), 0.0)
    j_l = xs + tile_px - left_l
    w_left = band_rows(y - top_l, r, lc, has_left) * jnp.where(j_l < tile_px, fade(j_l), 0.0)
    w_ref[...] = w_own
    w_ref[:, :width] += w_left
    reach = SPILL
    down_own = pick(rows, reach + rows, reach - top)
    down_left = pick(rows, reach + rows, reach - top_l)
    for p in range(planes):
        src = jnp.concatenate([prev_ref[p, rows - reach :], cur_ref[p]], axis=0)
        shifted_rows = jnp.dot(down_own, src, preferred_element_type=f32)
        scale, level = gain(0, p)

        def emit(k, block, p=p, scale=scale, level=level):
            span = slice(k * width, (k + 1) * width)
            out_ref[p, :, span] = (scale * block + level) * w_own[:, span]

        move_lanes(shifted_rows, left, tile_px, emit)
        lsrc = jnp.concatenate([lprev_ref[p, rows - reach :], lcur_ref[p]], axis=0)
        lrows = jnp.dot(down_left, lsrc, preferred_element_type=f32)
        window = pltpu.roll(lrows, left_l, 1)
        scale, level = gain(1, p)
        out_ref[p, :, :width] += (scale * window + level) * w_left

    @pl.when(step == 0)
    def _():
        te = lax.broadcasted_iota(jnp.int32, (width, 1), 0)
        top_u = table(off_ref, 0, ur, c)
        left_u = table(off_ref, 1, ur, c)
        top_c = table(off_ref, 0, ur, lc)
        left_c = table(off_ref, 1, ur, lc)
        j_u = x - left_u
        w_up = band_rows(te + tile_px - top_u, ur, c, has_up) * jnp.where(j_u >= 0, fade(j_u), 0.0)
        j_c = xs + tile_px - left_c
        w_corner = band_rows(te + tile_px - top_c, ur, lc, has_up & has_left) * jnp.where(
            j_c < tile_px, fade(j_c), 0.0
        )
        w_ref[:width, :] += w_up
        w_ref[:width, :width] += w_corner
        down_up = pick(width, width, width - top_u)
        down_corner = pick(width, width, width - top_c)
        for p in range(planes):
            urows = jnp.dot(down_up, up_ref[p], preferred_element_type=f32)
            scale, level = gain(2, p)

            def emit(k, block, p=p, scale=scale, level=level):
                span = slice(k * width, (k + 1) * width)
                out_ref[p, :width, span] += (scale * block + level) * w_up[:, span]

            move_lanes(urows, left_u, tile_px, emit)
            crows = jnp.dot(down_corner, corner_ref[p], preferred_element_type=f32)
            window = pltpu.roll(crows, left_c, 1)
            scale, level = gain(3, p)
            out_ref[p, :width, :width] += (scale * window + level) * w_corner


def blend(offsets, bands, terms, tiles, from_left, from_up, from_corner, n_row, n_col):
    planes, tile_px, _ = tiles.shape
    width = from_left.shape[2]
    rows = min(ROWS, tile_px)
    steps = tile_px // rows

    def cur(b, *_):
        return (0, b, 0)

    def prev(b, *_):
        return (0, jnp.maximum(b - 1, 0), 0)

    def fixed(b, *_):
        return (0, 0, 0)

    grid_spec = pltpu.PrefetchScalarGridSpec(
        num_scalar_prefetch=2,
        grid=(steps,),
        in_specs=[
            pl.BlockSpec(memory_space=pltpu.SMEM),
            pl.BlockSpec((planes, rows, tile_px), cur),
            pl.BlockSpec((planes, rows, tile_px), prev),
            pl.BlockSpec((planes, rows, width), cur),
            pl.BlockSpec((planes, rows, width), prev),
            pl.BlockSpec((planes, width, tile_px), fixed),
            pl.BlockSpec((planes, width, width), fixed),
        ],
        out_specs=[
            pl.BlockSpec((planes, rows, tile_px), cur),
            pl.BlockSpec((rows, tile_px), lambda b, *_: (b, 0)),
        ],
    )
    out_bytes = 4 * (planes + 1) * tile_px * tile_px
    in_bytes = 2 * 2 * planes * tile_px * (tile_px + width)
    return pl.pallas_call(
        functools.partial(blend_kernel, n_row=n_row, n_col=n_col),
        grid_spec=grid_spec,
        out_shape=[
            jax.ShapeDtypeStruct((planes, tile_px, tile_px), jnp.float32),
            jax.ShapeDtypeStruct((tile_px, tile_px), jnp.float32),
        ],
        compiler_params=pltpu.CompilerParams(dimension_semantics=("arbitrary",)),
        cost_estimate=pl.CostEstimate(
            flops=12 * planes * tile_px * tile_px, transcendentals=0,
            bytes_accessed=out_bytes + in_bytes,
        ),
    )(offsets, bands, terms, tiles, tiles, from_left, from_left,
      from_up, from_corner)


def shifted(block, axis, count, step):
    if step > 0:
        route = [(i, i + 1) for i in range(count - 1)]
    else:
        route = [(i + 1, i) for i in range(count - 1)]
    return lax.ppermute(block, axis, route)


def combine(right_pair, down_pair, left_pair, upper_pair):
    denominator = 1.0 + right_pair[0] + down_pair[0] + left_pair[0] + upper_pair[0]
    log_gain = (right_pair[1] + down_pair[1] - left_pair[1] - upper_pair[1]) / denominator
    offset = (right_pair[2] + down_pair[2] - left_pair[2] - upper_pair[2]) / denominator
    return log_gain, offset


def masked_terms(stats, present):
    return tuple(jnp.where(present, item, 0.0) for item in pair_terms(stats))


def local(tiles, extents, offsets, bands):
    planes, tile_px, _ = tiles.shape
    n_row = lax.axis_size("row")
    n_col = lax.axis_size("col")
    row_index = lax.axis_index("row")
    col_index = lax.axis_index("col")
    width = STRIP

    right_strip = tiles[:, :, tile_px - width :]
    down_strip = tiles[:, tile_px - width :, :]
    left_strip = tiles[:, :, :width]
    up_strip = tiles[:, :width, :]
    corner = tiles[:, tile_px - width :, tile_px - width :]
    from_left = shifted(right_strip, "col", n_col, 1)
    from_up = shifted(down_strip, "row", n_row, 1)
    diagonal = [
        (j * n_row + i, (j + 1) * n_row + i + 1) for i in range(n_row - 1) for j in range(n_col - 1)
    ]
    from_corner = lax.ppermute(corner, ("col", "row"), diagonal)

    left_col = jnp.maximum(col_index - 1, 0)
    upper_row = jnp.maximum(row_index - 1, 0)
    strip_ids = jnp.arange(width, dtype=jnp.int32)

    def across(extent):
        return (strip_ids < extent).astype(jnp.float32)[None, None, :]

    def along(extent):
        return (strip_ids < extent).astype(jnp.float32)[None, :, None]

    f32 = jnp.float32
    left_stats = strip_stats(
        from_left.astype(f32), left_strip.astype(f32), across(extents[0, row_index, left_col])
    )
    up_stats = strip_stats(
        from_up.astype(f32), up_strip.astype(f32), along(extents[1, upper_row, col_index])
    )
    right_stats = shifted(left_stats, "col", n_col, -1)
    down_stats = shifted(up_stats, "row", n_row, -1)
    has_right = col_index < n_col - 1
    has_down = row_index < n_row - 1
    has_left_pair = col_index > 0
    has_up_pair = row_index > 0
    gain_one, level_one = combine(
        masked_terms(right_stats, has_right),
        masked_terms(down_stats, has_down),
        masked_terms(left_stats, has_left_pair),
        masked_terms(up_stats, has_up_pair),
    )
    first = jnp.concatenate([gain_one, level_one])
    near = [
        shifted(first, "col", n_col, -1),
        shifted(first, "row", n_row, -1),
        shifted(first, "col", n_col, 1),
        shifted(first, "row", n_row, 1),
    ]
    scale = jnp.exp(gain_one)
    near_scale = [jnp.exp(item[:planes]) for item in near]
    near_level = [item[planes:] for item in near]
    right_two = corrected_stats(right_stats, scale, level_one, near_scale[0], near_level[0])
    down_two = corrected_stats(down_stats, scale, level_one, near_scale[1], near_level[1])
    left_two = corrected_stats(left_stats, near_scale[2], near_level[2], scale, level_one)
    up_two = corrected_stats(up_stats, near_scale[3], near_level[3], scale, level_one)
    gain_two, level_two = combine(
        masked_terms(right_two, has_right),
        masked_terms(down_two, has_down),
        masked_terms(left_two, has_left_pair),
        masked_terms(up_two, has_up_pair),
    )
    own_gain = gain_one + gain_two
    own_level = jnp.exp(gain_two) * level_one + level_two
    final = jnp.concatenate([own_gain, own_level])
    final_left = shifted(final, "col", n_col, 1)
    final_up = shifted(final, "row", n_row, 1)
    final_corner = lax.ppermute(final, ("col", "row"), diagonal)
    terms = jnp.concatenate([
        jnp.exp(own_gain), own_level,
        jnp.exp(final_left[:planes]), final_left[planes:],
        jnp.exp(final_up[:planes]), final_up[planes:],
        jnp.exp(final_corner[:planes]), final_corner[planes:],
    ])
    return blend(offsets, bands, terms, tiles, from_left, from_up, from_corner, n_row, n_col)


def solution(mesh):
    return jax.shard_map(
        local,
        mesh=mesh,
        in_specs=(P(None, "row", "col"), P(), P(), P()),
        out_specs=(P(None, "row", "col"), P("row", "col")),
        check_vma=False,
    )
```

```python
import functools

import jax
import jax.numpy as jnp
from jax import lax
from jax.sharding import PartitionSpec as P
from jax.experimental import pallas as pl
from jax.experimental.pallas import tpu as pltpu

STRIP = 128
SPILL = 128
BLOCK = 128
ROWS = 256


eps = 1e-06


def pair_terms(stats):
    mean_former, mean_latter, var_former, var_latter, covariance = stats
    weight = covariance * covariance / ((var_former + eps) * (var_latter + eps))
    log_ratio = 0.25 * (jnp.log(var_latter + eps) - jnp.log(var_former + eps))
    shift_term = 0.5 * (mean_latter - mean_former)
    return (weight, weight * log_ratio, weight * shift_term)


def corrected_stats(stats, gain_a, level_a, gain_b, level_b):
    mean_former, mean_latter, var_former, var_latter, covariance = stats
    return (
        gain_a * mean_former + level_a,
        gain_b * mean_latter + level_b,
        gain_a * gain_a * var_former,
        gain_b * gain_b * var_latter,
        gain_a * gain_b * covariance,
    )


def pick(rows_out, rows_in, shift):
    a = lax.broadcasted_iota(jnp.int32, (rows_out, rows_in), 0)
    b = lax.broadcasted_iota(jnp.int32, (rows_out, rows_in), 1)
    return jnp.where(b == a + shift, 1.0, 0.0).astype(jnp.bfloat16)


def move_lanes(rows, left, lanes, emit):
    width = STRIP
    lane = lax.broadcasted_iota(jnp.int32, (1, width), 1)
    before = None
    for k in range(lanes // width):
        turned = pltpu.roll(rows[:, k * width : (k + 1) * width], left, 1)
        block = turned if before is None else jnp.where(lane >= left, turned, before)
        before = turned
        emit(k, block)


def blend_kernel(off_ref, band_ref, terms_ref, cur_ref, prev_ref, lcur_ref, lprev_ref,
                 up_ref, corner_ref, out_ref, w_ref, *, n_row, n_col):
    f32 = jnp.float32
    bf16 = jnp.bfloat16
    step = pl.program_id(0)
    planes, rows, tile_px = cur_ref.shape
    width = lcur_ref.shape[2]
    cells = n_row * n_col
    r = lax.axis_index("row")
    c = lax.axis_index("col")
    lc = jnp.maximum(c - 1, 0)
    ur = jnp.maximum(r - 1, 0)
    has_left = c > 0
    has_up = r > 0

    def table(ref, k, rr, cc):
        return ref[k, rr, cc]

    def fade(ids):
        return (jnp.minimum(ids, tile_px - 1 - ids) + 1).astype(f32) / (tile_px / 2.0)

    def band_rows(ids, rr, cc, extra):
        live = (ids >= table(band_ref, 0, rr, cc) * BLOCK) & (ids < table(band_ref, 1, rr, cc) * BLOCK)
        live = live & (ids >= 0) & (ids < tile_px) & extra
        return jnp.where(live, fade(ids), 0.0)

    def gain(k, p):
        return terms_ref[k * 2 * planes + p], terms_ref[k * 2 * planes + planes + p]

    t = lax.broadcasted_iota(jnp.int32, (rows, 1), 0)
    x = lax.broadcasted_iota(jnp.int32, (1, tile_px), 1)
    xs = lax.broadcasted_iota(jnp.int32, (1, width), 1)
    y = step * rows + t
    top = table(off_ref, 0, r, c)
    left = table(off_ref, 1, r, c)
    top_l = table(off_ref, 0, r, lc)
    left_l = table(off_ref, 1, r, lc)
    j = x - left
    w_own = band_rows(y - top, r, c, True) * jnp.where(j >= 0, fade(j), 0.0)
    j_l = xs + tile_px - left_l
    w_left = band_rows(y - top_l, r, lc, has_left) * jnp.where(j_l < tile_px, fade(j_l), 0.0)
    w_ref[...] = w_own
    w_ref[:, :width] += w_left
    reach = SPILL
    down_own = pick(rows, reach + rows, reach - top)
    down_left = pick(rows, reach + rows, reach - top_l)
    for p in range(planes):
        src = jnp.concatenate([prev_ref[p, rows - reach :], cur_ref[p]], axis=0)
        shifted_rows = jnp.dot(down_own, src, preferred_element_type=f32)
        scale, level = gain(0, p)

        def emit(k, block, p=p, scale=scale, level=level):
            span = slice(k * width, (k + 1) * width)
            out_ref[p, :, span] = (scale * block + level) * w_own[:, span]

        move_lanes(shifted_rows, left, tile_px, emit)
        lsrc = jnp.concatenate([lprev_ref[p, rows - reach :], lcur_ref[p]], axis=0)
        lrows = jnp.dot(down_left, lsrc, preferred_element_type=f32)
        window = pltpu.roll(lrows, left_l, 1)
        scale, level = gain(1, p)
        out_ref[p, :, :width] += (scale * window + level) * w_left

    @pl.when(step == 0)
    def _():
        te = lax.broadcasted_iota(jnp.int32, (width, 1), 0)
        top_u = table(off_ref, 0, ur, c)
        left_u = table(off_ref, 1, ur, c)
        top_c = table(off_ref, 0, ur, lc)
        left_c = table(off_ref, 1, ur, lc)
        j_u = x - left_u
        w_up = band_rows(te + tile_px - top_u, ur, c, has_up) * jnp.where(j_u >= 0, fade(j_u), 0.0)
        j_c = xs + tile_px - left_c
        w_corner = band_rows(te + tile_px - top_c, ur, lc, has_up & has_left) * jnp.where(
            j_c < tile_px, fade(j_c), 0.0
        )
        w_ref[:width, :] += w_up
        w_ref[:width, :width] += w_corner
        down_up = pick(width, width, width - top_u)
        down_corner = pick(width, width, width - top_c)
        for p in range(planes):
            urows = jnp.dot(down_up, up_ref[p], preferred_element_type=f32)
            scale, level = gain(2, p)

            def emit(k, block, p=p, scale=scale, level=level):
                span = slice(k * width, (k + 1) * width)
                out_ref[p, :width, span] += (scale * block + level) * w_up[:, span]

            move_lanes(urows, left_u, tile_px, emit)
            crows = jnp.dot(down_corner, corner_ref[p], preferred_element_type=f32)
            window = pltpu.roll(crows, left_c, 1)
            scale, level = gain(3, p)
            out_ref[p, :width, :width] += (scale * window + level) * w_corner


def stats_kernel(ext_ref, far_left_ref, own_left_ref, far_up_ref, own_up_ref, left_ref, up_ref):
    f32 = jnp.float32
    r = lax.axis_index("row")
    c = lax.axis_index("col")
    planes = far_left_ref.shape[0]
    width = left_ref.shape[1]
    extent_h = ext_ref[0, r, jnp.maximum(c - 1, 0)]
    extent_v = ext_ref[1, jnp.maximum(r - 1, 0), c]

    def measure(former_ref, latter_ref, window, out_ref):
        full = jnp.broadcast_to(window.astype(f32), former_ref.shape[1:])
        number = jnp.sum(full)
        out_ref[...] = jnp.zeros(out_ref.shape, f32)
        for p in range(planes):
            former = former_ref[p].astype(f32)
            latter = latter_ref[p].astype(f32)
            mean_former = jnp.sum(former * full) / number
            mean_latter = jnp.sum(latter * full) / number
            dev_former = (former - mean_former) * full
            dev_latter = (latter - mean_latter) * full
            values = (
                mean_former,
                mean_latter,
                jnp.sum(dev_former * dev_former) / number,
                jnp.sum(dev_latter * dev_latter) / number,
                jnp.sum(dev_former * dev_latter) / number,
            )
            for k, value in enumerate(values):
                out_ref[pl.ds(k * planes + p, 1), :] = jnp.broadcast_to(value, (1, width))

    lane = lax.broadcasted_iota(jnp.int32, (1, width), 1)
    line = lax.broadcasted_iota(jnp.int32, (width, 1), 0)
    measure(far_left_ref, own_left_ref, lane < extent_h, left_ref)
    measure(far_up_ref, own_up_ref, line < extent_v, up_ref)


def pair_stats(extents, from_left, from_up, tiles):
    planes, tile_px, _ = tiles.shape
    width = from_left.shape[2]
    rows_out = 16

    def first(*_):
        return (0, 0, 0)

    grid_spec = pltpu.PrefetchScalarGridSpec(
        num_scalar_prefetch=1,
        grid=(1,),
        in_specs=[
            pl.BlockSpec((planes, tile_px, width), first),
            pl.BlockSpec((planes, tile_px, width), first),
            pl.BlockSpec((planes, width, tile_px), first),
            pl.BlockSpec((planes, width, tile_px), first),
        ],
        out_specs=[
            pl.BlockSpec((rows_out, width), lambda *_: (0, 0)),
            pl.BlockSpec((rows_out, width), lambda *_: (0, 0)),
        ],
    )
    return pl.pallas_call(
        stats_kernel,
        grid_spec=grid_spec,
        out_shape=[jax.ShapeDtypeStruct((rows_out, width), jnp.float32)] * 2,
        cost_estimate=pl.CostEstimate(
            flops=24 * planes * tile_px * width, transcendentals=0,
            bytes_accessed=2 * 4 * planes * tile_px * width,
        ),
    )(extents, from_left, tiles, from_up, tiles)


def unpack_stats(block, planes):
    return block[: 5 * planes, 0].reshape(5, planes)


def blend(offsets, bands, terms, tiles, from_left, from_up, from_corner, n_row, n_col):
    planes, tile_px, _ = tiles.shape
    width = from_left.shape[2]
    rows = min(ROWS, tile_px)
    steps = tile_px // rows

    def cur(b, *_):
        return (0, b, 0)

    def prev(b, *_):
        return (0, jnp.maximum(b - 1, 0), 0)

    def fixed(b, *_):
        return (0, 0, 0)

    grid_spec = pltpu.PrefetchScalarGridSpec(
        num_scalar_prefetch=2,
        grid=(steps,),
        in_specs=[
            pl.BlockSpec(memory_space=pltpu.SMEM),
            pl.BlockSpec((planes, rows, tile_px), cur),
            pl.BlockSpec((planes, rows, tile_px), prev),
            pl.BlockSpec((planes, rows, width), cur),
            pl.BlockSpec((planes, rows, width), prev),
            pl.BlockSpec((planes, width, tile_px), fixed),
            pl.BlockSpec((planes, width, width), fixed),
        ],
        out_specs=[
            pl.BlockSpec((planes, rows, tile_px), cur),
            pl.BlockSpec((rows, tile_px), lambda b, *_: (b, 0)),
        ],
    )
    out_bytes = 4 * (planes + 1) * tile_px * tile_px
    in_bytes = 2 * 2 * planes * tile_px * (tile_px + width)
    return pl.pallas_call(
        functools.partial(blend_kernel, n_row=n_row, n_col=n_col),
        grid_spec=grid_spec,
        out_shape=[
            jax.ShapeDtypeStruct((planes, tile_px, tile_px), jnp.float32),
            jax.ShapeDtypeStruct((tile_px, tile_px), jnp.float32),
        ],
        compiler_params=pltpu.CompilerParams(dimension_semantics=("arbitrary",)),
        cost_estimate=pl.CostEstimate(
            flops=12 * planes * tile_px * tile_px, transcendentals=0,
            bytes_accessed=out_bytes + in_bytes,
        ),
    )(offsets, bands, terms, tiles, tiles, from_left, from_left,
      from_up, from_corner)


def shifted(block, axis, count, step):
    if step > 0:
        route = [(i, i + 1) for i in range(count - 1)]
    else:
        route = [(i + 1, i) for i in range(count - 1)]
    return lax.ppermute(block, axis, route)


def combine(right_pair, down_pair, left_pair, upper_pair):
    denominator = 1.0 + right_pair[0] + down_pair[0] + left_pair[0] + upper_pair[0]
    log_gain = (right_pair[1] + down_pair[1] - left_pair[1] - upper_pair[1]) / denominator
    offset = (right_pair[2] + down_pair[2] - left_pair[2] - upper_pair[2]) / denominator
    return log_gain, offset


def masked_terms(stats, present):
    return tuple(jnp.where(present, item, 0.0) for item in pair_terms(stats))


def local(tiles, extents, offsets, bands):
    planes, tile_px, _ = tiles.shape
    n_row = lax.axis_size("row")
    n_col = lax.axis_size("col")
    row_index = lax.axis_index("row")
    col_index = lax.axis_index("col")
    width = STRIP

    right_strip = tiles[:, :, tile_px - width :]
    down_strip = tiles[:, tile_px - width :, :]
    corner = tiles[:, tile_px - width :, tile_px - width :]
    from_left = shifted(right_strip, "col", n_col, 1)
    from_up = shifted(down_strip, "row", n_row, 1)
    diagonal = [
        (j * n_row + i, (j + 1) * n_row + i + 1) for i in range(n_row - 1) for j in range(n_col - 1)
    ]
    from_corner = lax.ppermute(corner, ("col", "row"), diagonal)

    left_col = jnp.maximum(col_index - 1, 0)
    upper_row = jnp.maximum(row_index - 1, 0)
    f32 = jnp.float32
    left_block, up_block = pair_stats(extents, from_left, from_up, tiles)
    right_block = shifted(left_block, "col", n_col, -1)
    down_block = shifted(up_block, "row", n_row, -1)
    left_stats = unpack_stats(left_block, planes)
    up_stats = unpack_stats(up_block, planes)
    right_stats = unpack_stats(right_block, planes)
    down_stats = unpack_stats(down_block, planes)
    has_right = col_index < n_col - 1
    has_down = row_index < n_row - 1
    has_left_pair = col_index > 0
    has_up_pair = row_index > 0
    gain_one, level_one = combine(
        masked_terms(right_stats, has_right),
        masked_terms(down_stats, has_down),
        masked_terms(left_stats, has_left_pair),
        masked_terms(up_stats, has_up_pair),
    )
    first = jnp.concatenate([gain_one, level_one])
    near = [
        shifted(first, "col", n_col, -1),
        shifted(first, "row", n_row, -1),
        shifted(first, "col", n_col, 1),
        shifted(first, "row", n_row, 1),
    ]
    scale = jnp.exp(gain_one)
    near_scale = [jnp.exp(item[:planes]) for item in near]
    near_level = [item[planes:] for item in near]
    right_two = corrected_stats(right_stats, scale, level_one, near_scale[0], near_level[0])
    down_two = corrected_stats(down_stats, scale, level_one, near_scale[1], near_level[1])
    left_two = corrected_stats(left_stats, near_scale[2], near_level[2], scale, level_one)
    up_two = corrected_stats(up_stats, near_scale[3], near_level[3], scale, level_one)
    gain_two, level_two = combine(
        masked_terms(right_two, has_right),
        masked_terms(down_two, has_down),
        masked_terms(left_two, has_left_pair),
        masked_terms(up_two, has_up_pair),
    )
    own_gain = gain_one + gain_two
    own_level = jnp.exp(gain_two) * level_one + level_two
    final = jnp.concatenate([own_gain, own_level])
    final_left = shifted(final, "col", n_col, 1)
    final_up = shifted(final, "row", n_row, 1)
    final_corner = lax.ppermute(final, ("col", "row"), diagonal)
    terms = jnp.concatenate([
        jnp.exp(own_gain), own_level,
        jnp.exp(final_left[:planes]), final_left[planes:],
        jnp.exp(final_up[:planes]), final_up[planes:],
        jnp.exp(final_corner[:planes]), final_corner[planes:],
    ])
    return blend(offsets, bands, terms, tiles, from_left, from_up, from_corner, n_row, n_col)


def solution(mesh):
    return jax.shard_map(
        local,
        mesh=mesh,
        in_specs=(P(None, "row", "col"), P(), P(), P()),
        out_specs=(P(None, "row", "col"), P("row", "col")),
        check_vma=False,
    )
```

```python
import functools

import jax
import jax.numpy as jnp
from jax import lax
from jax.sharding import PartitionSpec as P
from jax.experimental import pallas as pl
from jax.experimental.pallas import tpu as pltpu

STRIP = 128
SPILL = 128
BLOCK = 128
ROWS = 256


eps = 1e-06


def pair_terms(stats):
    mean_former, mean_latter, var_former, var_latter, covariance = stats
    weight = covariance * covariance / ((var_former + eps) * (var_latter + eps))
    log_ratio = 0.25 * (jnp.log(var_latter + eps) - jnp.log(var_former + eps))
    shift_term = 0.5 * (mean_latter - mean_former)
    return (weight, weight * log_ratio, weight * shift_term)


def corrected_stats(stats, gain_a, level_a, gain_b, level_b):
    mean_former, mean_latter, var_former, var_latter, covariance = stats
    return (
        gain_a * mean_former + level_a,
        gain_b * mean_latter + level_b,
        gain_a * gain_a * var_former,
        gain_b * gain_b * var_latter,
        gain_a * gain_b * covariance,
    )


def pick(rows_out, rows_in, shift):
    a = lax.broadcasted_iota(jnp.int32, (rows_out, rows_in), 0)
    b = lax.broadcasted_iota(jnp.int32, (rows_out, rows_in), 1)
    return jnp.where(b == a + shift, 1.0, 0.0).astype(jnp.bfloat16)


def move_lanes(rows, left, lanes, emit):
    width = STRIP
    lane = lax.broadcasted_iota(jnp.int32, (1, width), 1)
    before = None
    for k in range(lanes // width):
        turned = pltpu.roll(rows[:, k * width : (k + 1) * width], left, 1)
        block = turned if before is None else jnp.where(lane >= left, turned, before)
        before = turned
        emit(k, block)


def blend_kernel(off_ref, band_ref, terms_ref, cur_ref, prev_ref, lcur_ref, lprev_ref,
                 up_ref, corner_ref, out_ref, w_ref, *, n_row, n_col):
    f32 = jnp.float32
    bf16 = jnp.bfloat16
    step = pl.program_id(0)
    planes, rows, tile_px = cur_ref.shape
    width = lcur_ref.shape[2]
    cells = n_row * n_col
    r = lax.axis_index("row")
    c = lax.axis_index("col")
    lc = jnp.maximum(c - 1, 0)
    ur = jnp.maximum(r - 1, 0)
    has_left = c > 0
    has_up = r > 0

    def table(ref, k, rr, cc):
        return ref[k, rr, cc]

    def fade(ids):
        return (jnp.minimum(ids, tile_px - 1 - ids) + 1).astype(f32) / (tile_px / 2.0)

    def band_rows(ids, rr, cc, extra):
        live = (ids >= table(band_ref, 0, rr, cc) * BLOCK) & (ids < table(band_ref, 1, rr, cc) * BLOCK)
        live = live & (ids >= 0) & (ids < tile_px) & extra
        return jnp.where(live, fade(ids), 0.0)

    def gain(k, p):
        return terms_ref[k * 2 * planes + p], terms_ref[k * 2 * planes + planes + p]

    t = lax.broadcasted_iota(jnp.int32, (rows, 1), 0)
    x = lax.broadcasted_iota(jnp.int32, (1, tile_px), 1)
    xs = lax.broadcasted_iota(jnp.int32, (1, width), 1)
    y = step * rows + t
    top = table(off_ref, 0, r, c)
    left = table(off_ref, 1, r, c)
    top_l = table(off_ref, 0, r, lc)
    left_l = table(off_ref, 1, r, lc)
    j = x - left
    w_own = band_rows(y - top, r, c, True) * jnp.where(j >= 0, fade(j), 0.0)
    j_l = xs + tile_px - left_l
    w_left = band_rows(y - top_l, r, lc, has_left) * jnp.where(j_l < tile_px, fade(j_l), 0.0)
    w_ref[...] = w_own
    w_ref[:, :width] += w_left
    reach = SPILL
    down_own = pick(rows, reach + rows, reach - top)
    down_left = pick(rows, reach + rows, reach - top_l)
    for p in range(planes):
        src = jnp.concatenate([prev_ref[p, rows - reach :], cur_ref[p]], axis=0)
        shifted_rows = jnp.dot(down_own, src, preferred_element_type=f32)
        scale, level = gain(0, p)

        def emit(k, block, p=p, scale=scale, level=level):
            span = slice(k * width, (k + 1) * width)
            out_ref[p, :, span] = (scale * block + level) * w_own[:, span]

        move_lanes(shifted_rows, left, tile_px, emit)
        lsrc = jnp.concatenate([lprev_ref[p, rows - reach :], lcur_ref[p]], axis=0)
        lrows = jnp.dot(down_left, lsrc, preferred_element_type=f32)
        window = pltpu.roll(lrows, left_l, 1)
        scale, level = gain(1, p)
        out_ref[p, :, :width] += (scale * window + level) * w_left

    @pl.when(step == 0)
    def _():
        te = lax.broadcasted_iota(jnp.int32, (width, 1), 0)
        top_u = table(off_ref, 0, ur, c)
        left_u = table(off_ref, 1, ur, c)
        top_c = table(off_ref, 0, ur, lc)
        left_c = table(off_ref, 1, ur, lc)
        j_u = x - left_u
        w_up = band_rows(te + tile_px - top_u, ur, c, has_up) * jnp.where(j_u >= 0, fade(j_u), 0.0)
        j_c = xs + tile_px - left_c
        w_corner = band_rows(te + tile_px - top_c, ur, lc, has_up & has_left) * jnp.where(
            j_c < tile_px, fade(j_c), 0.0
        )
        w_ref[:width, :] += w_up
        w_ref[:width, :width] += w_corner
        down_up = pick(width, width, width - top_u)
        down_corner = pick(width, width, width - top_c)
        for p in range(planes):
            urows = jnp.dot(down_up, up_ref[p], preferred_element_type=f32)
            scale, level = gain(2, p)

            def emit(k, block, p=p, scale=scale, level=level):
                span = slice(k * width, (k + 1) * width)
                out_ref[p, :width, span] += (scale * block + level) * w_up[:, span]

            move_lanes(urows, left_u, tile_px, emit)
            crows = jnp.dot(down_corner, corner_ref[p], preferred_element_type=f32)
            window = pltpu.roll(crows, left_c, 1)
            scale, level = gain(3, p)
            out_ref[p, :width, :width] += (scale * window + level) * w_corner


def stats_kernel(ext_ref, far_left_ref, own_left_ref, far_up_ref, own_up_ref, left_ref, up_ref):
    f32 = jnp.float32
    r = lax.axis_index("row")
    c = lax.axis_index("col")
    planes = far_left_ref.shape[0]
    width = left_ref.shape[1]
    extent_h = ext_ref[0, r, jnp.maximum(c - 1, 0)]
    extent_v = ext_ref[1, jnp.maximum(r - 1, 0), c]

    def measure(former_ref, latter_ref, window, out_ref):
        full = jnp.broadcast_to(window.astype(f32), former_ref.shape[1:])
        number = jnp.sum(full)
        out_ref[...] = jnp.zeros(out_ref.shape, f32)
        for p in range(planes):
            former = former_ref[p].astype(f32)
            latter = latter_ref[p].astype(f32)
            mean_former = jnp.sum(former * full) / number
            mean_latter = jnp.sum(latter * full) / number
            dev_former = (former - mean_former) * full
            dev_latter = (latter - mean_latter) * full
            values = (
                mean_former,
                mean_latter,
                jnp.sum(dev_former * dev_former) / number,
                jnp.sum(dev_latter * dev_latter) / number,
                jnp.sum(dev_former * dev_latter) / number,
            )
            for k, value in enumerate(values):
                out_ref[pl.ds(k * planes + p, 1), :] = jnp.broadcast_to(value, (1, width))

    lane = lax.broadcasted_iota(jnp.int32, (1, width), 1)
    line = lax.broadcasted_iota(jnp.int32, (width, 1), 0)
    measure(far_left_ref, own_left_ref, lane < extent_h, left_ref)
    measure(far_up_ref, own_up_ref, line < extent_v, up_ref)


def pair_stats(extents, from_left, from_up, tiles):
    planes, tile_px, _ = tiles.shape
    width = from_left.shape[2]
    rows_out = 16

    def first(*_):
        return (0, 0, 0)

    grid_spec = pltpu.PrefetchScalarGridSpec(
        num_scalar_prefetch=1,
        grid=(1,),
        in_specs=[
            pl.BlockSpec((planes, tile_px, width), first),
            pl.BlockSpec((planes, tile_px, width), first),
            pl.BlockSpec((planes, width, tile_px), first),
            pl.BlockSpec((planes, width, tile_px), first),
        ],
        out_specs=[
            pl.BlockSpec((rows_out, width), lambda *_: (0, 0)),
            pl.BlockSpec((rows_out, width), lambda *_: (0, 0)),
        ],
    )
    return pl.pallas_call(
        stats_kernel,
        grid_spec=grid_spec,
        out_shape=[jax.ShapeDtypeStruct((rows_out, width), jnp.float32)] * 2,
        cost_estimate=pl.CostEstimate(
            flops=24 * planes * tile_px * width, transcendentals=0,
            bytes_accessed=2 * 4 * planes * tile_px * width,
        ),
    )(extents, from_left, tiles, from_up, tiles)


def unpack_stats(block, planes):
    return block[: 5 * planes, 0].reshape(5, planes)


def blend(offsets, bands, terms, tiles, from_left, from_up, from_corner, n_row, n_col):
    planes, tile_px, _ = tiles.shape
    width = from_left.shape[2]
    rows = min(ROWS, tile_px)
    steps = tile_px // rows

    def cur(b, *_):
        return (0, b, 0)

    def prev(b, *_):
        return (0, jnp.maximum(b - 1, 0), 0)

    def fixed(b, *_):
        return (0, 0, 0)

    grid_spec = pltpu.PrefetchScalarGridSpec(
        num_scalar_prefetch=2,
        grid=(steps,),
        in_specs=[
            pl.BlockSpec(memory_space=pltpu.SMEM),
            pl.BlockSpec((planes, rows, tile_px), cur),
            pl.BlockSpec((planes, rows, tile_px), prev),
            pl.BlockSpec((planes, rows, width), cur),
            pl.BlockSpec((planes, rows, width), prev),
            pl.BlockSpec((planes, width, tile_px), fixed),
            pl.BlockSpec((planes, width, width), fixed),
        ],
        out_specs=[
            pl.BlockSpec((planes, rows, tile_px), cur),
            pl.BlockSpec((rows, tile_px), lambda b, *_: (b, 0)),
        ],
    )
    out_bytes = 4 * (planes + 1) * tile_px * tile_px
    in_bytes = 2 * 2 * planes * tile_px * (tile_px + width)
    return pl.pallas_call(
        functools.partial(blend_kernel, n_row=n_row, n_col=n_col),
        grid_spec=grid_spec,
        out_shape=[
            jax.ShapeDtypeStruct((planes, tile_px, tile_px), jnp.float32),
            jax.ShapeDtypeStruct((tile_px, tile_px), jnp.float32),
        ],
        compiler_params=pltpu.CompilerParams(dimension_semantics=("arbitrary",)),
        cost_estimate=pl.CostEstimate(
            flops=12 * planes * tile_px * tile_px, transcendentals=0,
            bytes_accessed=out_bytes + in_bytes,
        ),
    )(offsets, bands, terms, tiles, tiles, from_left, from_left,
      from_up, from_corner)


def shifted(block, axis, count, step):
    if step > 0:
        route = [(i, i + 1) for i in range(count - 1)]
    else:
        route = [(i + 1, i) for i in range(count - 1)]
    return lax.ppermute(block, axis, route)


def combine(right_pair, down_pair, left_pair, upper_pair):
    denominator = 1.0 + right_pair[0] + down_pair[0] + left_pair[0] + upper_pair[0]
    log_gain = (right_pair[1] + down_pair[1] - left_pair[1] - upper_pair[1]) / denominator
    offset = (right_pair[2] + down_pair[2] - left_pair[2] - upper_pair[2]) / denominator
    return log_gain, offset


def masked_terms(stats, present):
    return tuple(jnp.where(present, item, 0.0) for item in pair_terms(stats))


def local(tiles, extents, offsets, bands):
    planes, tile_px, _ = tiles.shape
    n_row = lax.axis_size("row")
    n_col = lax.axis_size("col")
    row_index = lax.axis_index("row")
    col_index = lax.axis_index("col")
    width = STRIP

    right_strip = tiles[:, :, tile_px - width :]
    down_strip = tiles[:, tile_px - width :, :]
    corner = tiles[:, tile_px - width :, tile_px - width :]
    from_left = shifted(right_strip, "col", n_col, 1)
    from_up = shifted(down_strip, "row", n_row, 1)
    diagonal = [
        (j * n_row + i, (j + 1) * n_row + i + 1) for i in range(n_row - 1) for j in range(n_col - 1)
    ]

    left_col = jnp.maximum(col_index - 1, 0)
    upper_row = jnp.maximum(row_index - 1, 0)
    f32 = jnp.float32
    left_block, up_block = pair_stats(extents, from_left, from_up, tiles)
    right_block = shifted(left_block, "col", n_col, -1)
    down_block = shifted(up_block, "row", n_row, -1)
    left_stats = unpack_stats(left_block, planes)
    up_stats = unpack_stats(up_block, planes)
    right_stats = unpack_stats(right_block, planes)
    down_stats = unpack_stats(down_block, planes)
    has_right = col_index < n_col - 1
    has_down = row_index < n_row - 1
    has_left_pair = col_index > 0
    has_up_pair = row_index > 0
    gain_one, level_one = combine(
        masked_terms(right_stats, has_right),
        masked_terms(down_stats, has_down),
        masked_terms(left_stats, has_left_pair),
        masked_terms(up_stats, has_up_pair),
    )
    first = jnp.concatenate([gain_one, level_one])
    near = [
        shifted(first, "col", n_col, -1),
        shifted(first, "row", n_row, -1),
        shifted(first, "col", n_col, 1),
        shifted(first, "row", n_row, 1),
    ]
    scale = jnp.exp(gain_one)
    near_scale = [jnp.exp(item[:planes]) for item in near]
    near_level = [item[planes:] for item in near]
    right_two = corrected_stats(right_stats, scale, level_one, near_scale[0], near_level[0])
    down_two = corrected_stats(down_stats, scale, level_one, near_scale[1], near_level[1])
    left_two = corrected_stats(left_stats, near_scale[2], near_level[2], scale, level_one)
    up_two = corrected_stats(up_stats, near_scale[3], near_level[3], scale, level_one)
    gain_two, level_two = combine(
        masked_terms(right_two, has_right),
        masked_terms(down_two, has_down),
        masked_terms(left_two, has_left_pair),
        masked_terms(up_two, has_up_pair),
    )
    own_gain = gain_one + gain_two
    own_level = jnp.exp(gain_two) * level_one + level_two
    final = jnp.concatenate([own_gain, own_level])
    final_left = shifted(final, "col", n_col, 1)
    final_up = shifted(final, "row", n_row, 1)
    lanes = corner.shape[2]
    packet = jnp.concatenate(
        [
            corner.astype(jnp.float32).reshape(planes * width, lanes),
            jnp.pad(final[None, :], ((0, 7), (0, lanes - final.shape[0]))),
        ]
    )
    packet = lax.ppermute(packet, ("col", "row"), diagonal)
    final_corner = packet[planes * width, : final.shape[0]]
    from_corner = packet[: planes * width].reshape(planes, width, lanes).astype(jnp.bfloat16)
    terms = jnp.concatenate([
        jnp.exp(own_gain), own_level,
        jnp.exp(final_left[:planes]), final_left[planes:],
        jnp.exp(final_up[:planes]), final_up[planes:],
        jnp.exp(final_corner[:planes]), final_corner[planes:],
    ])
    return blend(offsets, bands, terms, tiles, from_left, from_up, from_corner, n_row, n_col)


def solution(mesh):
    return jax.shard_map(
        local,
        mesh=mesh,
        in_specs=(P(None, "row", "col"), P(), P(), P()),
        out_specs=(P(None, "row", "col"), P("row", "col")),
        check_vma=False,
    )
```

```python
import functools

import jax
import jax.numpy as jnp
from jax import lax
from jax.sharding import PartitionSpec as P
from jax.experimental import pallas as pl
from jax.experimental.pallas import tpu as pltpu

STRIP = 128
SPILL = 128
BLOCK = 128
ROWS = 256


eps = 1e-06


def pair_terms(stats):
    mean_former, mean_latter, var_former, var_latter, covariance = stats
    weight = covariance * covariance / ((var_former + eps) * (var_latter + eps))
    log_ratio = 0.25 * (jnp.log(var_latter + eps) - jnp.log(var_former + eps))
    shift_term = 0.5 * (mean_latter - mean_former)
    return (weight, weight * log_ratio, weight * shift_term)


def corrected_stats(stats, gain_a, level_a, gain_b, level_b):
    mean_former, mean_latter, var_former, var_latter, covariance = stats
    return (
        gain_a * mean_former + level_a,
        gain_b * mean_latter + level_b,
        gain_a * gain_a * var_former,
        gain_b * gain_b * var_latter,
        gain_a * gain_b * covariance,
    )


def pick(rows_out, rows_in, shift):
    a = lax.broadcasted_iota(jnp.int32, (rows_out, rows_in), 0)
    b = lax.broadcasted_iota(jnp.int32, (rows_out, rows_in), 1)
    return jnp.where(b == a + shift, 1.0, 0.0).astype(jnp.bfloat16)


def move_lanes(rows, left, lanes, emit):
    width = STRIP
    lane = lax.broadcasted_iota(jnp.int32, (1, width), 1)
    before = None
    for k in range(lanes // width):
        turned = pltpu.roll(rows[:, k * width : (k + 1) * width], left, 1)
        block = turned if before is None else jnp.where(lane >= left, turned, before)
        before = turned
        emit(k, block)


def shift_kernel(off_ref, band_ref, cur_ref, prev_ref, moved_ref, w_ref, *, n_row, n_col):
    f32 = jnp.float32
    bf16 = jnp.bfloat16
    step = pl.program_id(0)
    planes, rows, tile_px = cur_ref.shape
    width = STRIP
    cells = n_row * n_col
    r = lax.axis_index("row")
    c = lax.axis_index("col")
    lc = jnp.maximum(c - 1, 0)
    ur = jnp.maximum(r - 1, 0)
    has_left = c > 0
    has_up = r > 0

    def table(ref, k, rr, cc):
        return ref[k, rr, cc]

    def fade(ids):
        return (jnp.minimum(ids, tile_px - 1 - ids) + 1).astype(f32) / (tile_px / 2.0)

    def band_rows(ids, rr, cc, extra):
        live = (ids >= table(band_ref, 0, rr, cc) * BLOCK) & (ids < table(band_ref, 1, rr, cc) * BLOCK)
        live = live & (ids >= 0) & (ids < tile_px) & extra
        return jnp.where(live, fade(ids), 0.0)

    def gain(k, p):
        return terms_ref[k * 2 * planes + p], terms_ref[k * 2 * planes + planes + p]

    t = lax.broadcasted_iota(jnp.int32, (rows, 1), 0)
    x = lax.broadcasted_iota(jnp.int32, (1, tile_px), 1)
    xs = lax.broadcasted_iota(jnp.int32, (1, width), 1)
    y = step * rows + t
    top = table(off_ref, 0, r, c)
    left = table(off_ref, 1, r, c)
    top_l = table(off_ref, 0, r, lc)
    left_l = table(off_ref, 1, r, lc)
    j = x - left
    w_own = band_rows(y - top, r, c, True) * jnp.where(j >= 0, fade(j), 0.0)
    j_l = xs + tile_px - left_l
    w_left = band_rows(y - top_l, r, lc, has_left) * jnp.where(j_l < tile_px, fade(j_l), 0.0)
    w_ref[...] = w_own
    w_ref[:, :width] += w_left
    reach = SPILL
    down_own = pick(rows, reach + rows, reach - top)
    down_left = pick(rows, reach + rows, reach - top_l)
    for p in range(planes):
        src = jnp.concatenate([prev_ref[p, rows - reach :], cur_ref[p]], axis=0)
        shifted_rows = jnp.dot(down_own, src, preferred_element_type=f32)

        def emit(k, block, p=p):
            span = slice(k * width, (k + 1) * width)
            moved_ref[p, :, span] = block.astype(moved_ref.dtype)

        move_lanes(shifted_rows, left, tile_px, emit)

    @pl.when(step == 0)
    def _():
        te = lax.broadcasted_iota(jnp.int32, (width, 1), 0)
        top_u = table(off_ref, 0, ur, c)
        left_u = table(off_ref, 1, ur, c)
        top_c = table(off_ref, 0, ur, lc)
        left_c = table(off_ref, 1, ur, lc)
        j_u = x - left_u
        w_up = band_rows(te + tile_px - top_u, ur, c, has_up) * jnp.where(j_u >= 0, fade(j_u), 0.0)
        j_c = xs + tile_px - left_c
        w_corner = band_rows(te + tile_px - top_c, ur, lc, has_up & has_left) * jnp.where(
            j_c < tile_px, fade(j_c), 0.0
        )
        w_ref[:width, :] += w_up
        w_ref[:width, :width] += w_corner


def blend_kernel(off_ref, band_ref, terms_ref, moved_ref, lcur_ref, lprev_ref,
                 up_ref, corner_ref, out_ref, *, n_row, n_col):
    f32 = jnp.float32
    bf16 = jnp.bfloat16
    step = pl.program_id(0)
    planes, rows, tile_px = moved_ref.shape
    width = lcur_ref.shape[2]
    cells = n_row * n_col
    r = lax.axis_index("row")
    c = lax.axis_index("col")
    lc = jnp.maximum(c - 1, 0)
    ur = jnp.maximum(r - 1, 0)
    has_left = c > 0
    has_up = r > 0

    def table(ref, k, rr, cc):
        return ref[k, rr, cc]

    def fade(ids):
        return (jnp.minimum(ids, tile_px - 1 - ids) + 1).astype(f32) / (tile_px / 2.0)

    def band_rows(ids, rr, cc, extra):
        live = (ids >= table(band_ref, 0, rr, cc) * BLOCK) & (ids < table(band_ref, 1, rr, cc) * BLOCK)
        live = live & (ids >= 0) & (ids < tile_px) & extra
        return jnp.where(live, fade(ids), 0.0)

    def gain(k, p):
        return terms_ref[k * 2 * planes + p], terms_ref[k * 2 * planes + planes + p]

    t = lax.broadcasted_iota(jnp.int32, (rows, 1), 0)
    x = lax.broadcasted_iota(jnp.int32, (1, tile_px), 1)
    xs = lax.broadcasted_iota(jnp.int32, (1, width), 1)
    y = step * rows + t
    top = table(off_ref, 0, r, c)
    left = table(off_ref, 1, r, c)
    top_l = table(off_ref, 0, r, lc)
    left_l = table(off_ref, 1, r, lc)
    j = x - left
    w_own = band_rows(y - top, r, c, True) * jnp.where(j >= 0, fade(j), 0.0)
    j_l = xs + tile_px - left_l
    w_left = band_rows(y - top_l, r, lc, has_left) * jnp.where(j_l < tile_px, fade(j_l), 0.0)
    reach = SPILL
    down_left = pick(rows, reach + rows, reach - top_l)
    for p in range(planes):
        scale, level = gain(0, p)
        out_ref[p] = (scale * moved_ref[p].astype(f32) + level) * w_own
        lsrc = jnp.concatenate([lprev_ref[p, rows - reach :], lcur_ref[p]], axis=0)
        lrows = jnp.dot(down_left, lsrc, preferred_element_type=f32)
        window = pltpu.roll(lrows, left_l, 1)
        scale, level = gain(1, p)
        out_ref[p, :, :width] += (scale * window + level) * w_left

    @pl.when(step == 0)
    def _():
        te = lax.broadcasted_iota(jnp.int32, (width, 1), 0)
        top_u = table(off_ref, 0, ur, c)
        left_u = table(off_ref, 1, ur, c)
        top_c = table(off_ref, 0, ur, lc)
        left_c = table(off_ref, 1, ur, lc)
        j_u = x - left_u
        w_up = band_rows(te + tile_px - top_u, ur, c, has_up) * jnp.where(j_u >= 0, fade(j_u), 0.0)
        j_c = xs + tile_px - left_c
        w_corner = band_rows(te + tile_px - top_c, ur, lc, has_up & has_left) * jnp.where(
            j_c < tile_px, fade(j_c), 0.0
        )
        down_up = pick(width, width, width - top_u)
        down_corner = pick(width, width, width - top_c)
        for p in range(planes):
            urows = jnp.dot(down_up, up_ref[p], preferred_element_type=f32)
            scale, level = gain(2, p)

            def emit(k, block, p=p, scale=scale, level=level):
                span = slice(k * width, (k + 1) * width)
                out_ref[p, :width, span] += (scale * block + level) * w_up[:, span]

            move_lanes(urows, left_u, tile_px, emit)
            crows = jnp.dot(down_corner, corner_ref[p], preferred_element_type=f32)
            window = pltpu.roll(crows, left_c, 1)
            scale, level = gain(3, p)
            out_ref[p, :width, :width] += (scale * window + level) * w_corner


def stats_kernel(ext_ref, far_left_ref, own_left_ref, far_up_ref, own_up_ref, left_ref, up_ref):
    f32 = jnp.float32
    r = lax.axis_index("row")
    c = lax.axis_index("col")
    planes = far_left_ref.shape[0]
    width = left_ref.shape[1]
    extent_h = ext_ref[0, r, jnp.maximum(c - 1, 0)]
    extent_v = ext_ref[1, jnp.maximum(r - 1, 0), c]

    def measure(former_ref, latter_ref, window, out_ref):
        full = jnp.broadcast_to(window.astype(f32), former_ref.shape[1:])
        number = jnp.sum(full)
        out_ref[...] = jnp.zeros(out_ref.shape, f32)
        for p in range(planes):
            former = former_ref[p].astype(f32)
            latter = latter_ref[p].astype(f32)
            mean_former = jnp.sum(former * full) / number
            mean_latter = jnp.sum(latter * full) / number
            dev_former = (former - mean_former) * full
            dev_latter = (latter - mean_latter) * full
            values = (
                mean_former,
                mean_latter,
                jnp.sum(dev_former * dev_former) / number,
                jnp.sum(dev_latter * dev_latter) / number,
                jnp.sum(dev_former * dev_latter) / number,
            )
            for k, value in enumerate(values):
                out_ref[pl.ds(k * planes + p, 1), :] = jnp.broadcast_to(value, (1, width))

    lane = lax.broadcasted_iota(jnp.int32, (1, width), 1)
    line = lax.broadcasted_iota(jnp.int32, (width, 1), 0)
    measure(far_left_ref, own_left_ref, lane < extent_h, left_ref)
    measure(far_up_ref, own_up_ref, line < extent_v, up_ref)


def pair_stats(extents, from_left, from_up, tiles):
    planes, tile_px, _ = tiles.shape
    width = from_left.shape[2]
    rows_out = 16

    def first(*_):
        return (0, 0, 0)

    grid_spec = pltpu.PrefetchScalarGridSpec(
        num_scalar_prefetch=1,
        grid=(1,),
        in_specs=[
            pl.BlockSpec((planes, tile_px, width), first),
            pl.BlockSpec((planes, tile_px, width), first),
            pl.BlockSpec((planes, width, tile_px), first),
            pl.BlockSpec((planes, width, tile_px), first),
        ],
        out_specs=[
            pl.BlockSpec((rows_out, width), lambda *_: (0, 0)),
            pl.BlockSpec((rows_out, width), lambda *_: (0, 0)),
        ],
    )
    return pl.pallas_call(
        stats_kernel,
        grid_spec=grid_spec,
        out_shape=[jax.ShapeDtypeStruct((rows_out, width), jnp.float32)] * 2,
        cost_estimate=pl.CostEstimate(
            flops=24 * planes * tile_px * width, transcendentals=0,
            bytes_accessed=2 * 4 * planes * tile_px * width,
        ),
    )(extents, from_left, tiles, from_up, tiles)


def unpack_stats(block, planes):
    return block[: 5 * planes, 0].reshape(5, planes)


def shift_tile(offsets, bands, tiles, n_row, n_col):
    planes, tile_px, _ = tiles.shape
    rows = min(ROWS, tile_px)

    def cur(b, *_):
        return (0, b, 0)

    def prev(b, *_):
        return (0, jnp.maximum(b - 1, 0), 0)

    grid_spec = pltpu.PrefetchScalarGridSpec(
        num_scalar_prefetch=2,
        grid=(tile_px // rows,),
        in_specs=[
            pl.BlockSpec((planes, rows, tile_px), cur),
            pl.BlockSpec((planes, rows, tile_px), prev),
        ],
        out_specs=[
            pl.BlockSpec((planes, rows, tile_px), cur),
            pl.BlockSpec((rows, tile_px), lambda b, *_: (b, 0)),
        ],
    )
    return pl.pallas_call(
        functools.partial(shift_kernel, n_row=n_row, n_col=n_col),
        grid_spec=grid_spec,
        out_shape=[
            jax.ShapeDtypeStruct((planes, tile_px, tile_px), tiles.dtype),
            jax.ShapeDtypeStruct((tile_px, tile_px), jnp.float32),
        ],
        compiler_params=pltpu.CompilerParams(dimension_semantics=("arbitrary",)),
        cost_estimate=pl.CostEstimate(
            flops=2 * planes * tile_px * tile_px * 2 * rows, transcendentals=0,
            bytes_accessed=2 * 2 * planes * tile_px * tile_px + 4 * tile_px * tile_px,
        ),
    )(offsets, bands, tiles, tiles)


def blend(offsets, bands, terms, moved, from_left, from_up, from_corner, n_row, n_col):
    planes, tile_px, _ = moved.shape
    width = from_left.shape[2]
    rows = min(ROWS, tile_px)

    def cur(b, *_):
        return (0, b, 0)

    def prev(b, *_):
        return (0, jnp.maximum(b - 1, 0), 0)

    def fixed(b, *_):
        return (0, 0, 0)

    grid_spec = pltpu.PrefetchScalarGridSpec(
        num_scalar_prefetch=2,
        grid=(tile_px // rows,),
        in_specs=[
            pl.BlockSpec(memory_space=pltpu.SMEM),
            pl.BlockSpec((planes, rows, tile_px), cur),
            pl.BlockSpec((planes, rows, width), cur),
            pl.BlockSpec((planes, rows, width), prev),
            pl.BlockSpec((planes, width, tile_px), fixed),
            pl.BlockSpec((planes, width, width), fixed),
        ],
        out_specs=pl.BlockSpec((planes, rows, tile_px), cur),
    )
    return pl.pallas_call(
        functools.partial(blend_kernel, n_row=n_row, n_col=n_col),
        grid_spec=grid_spec,
        out_shape=jax.ShapeDtypeStruct((planes, tile_px, tile_px), jnp.float32),
        compiler_params=pltpu.CompilerParams(dimension_semantics=("arbitrary",)),
        cost_estimate=pl.CostEstimate(
            flops=4 * planes * tile_px * tile_px, transcendentals=0,
            bytes_accessed=(2 + 4) * planes * tile_px * tile_px,
        ),
    )(offsets, bands, terms, moved, from_left, from_left, from_up, from_corner)


def shifted(block, axis, count, step):
    if step > 0:
        route = [(i, i + 1) for i in range(count - 1)]
    else:
        route = [(i + 1, i) for i in range(count - 1)]
    return lax.ppermute(block, axis, route)


def combine(right_pair, down_pair, left_pair, upper_pair):
    denominator = 1.0 + right_pair[0] + down_pair[0] + left_pair[0] + upper_pair[0]
    log_gain = (right_pair[1] + down_pair[1] - left_pair[1] - upper_pair[1]) / denominator
    offset = (right_pair[2] + down_pair[2] - left_pair[2] - upper_pair[2]) / denominator
    return log_gain, offset


def masked_terms(stats, present):
    return tuple(jnp.where(present, item, 0.0) for item in pair_terms(stats))


def local(tiles, extents, offsets, bands):
    planes, tile_px, _ = tiles.shape
    n_row = lax.axis_size("row")
    n_col = lax.axis_size("col")
    row_index = lax.axis_index("row")
    col_index = lax.axis_index("col")
    width = STRIP

    right_strip = tiles[:, :, tile_px - width :]
    down_strip = tiles[:, tile_px - width :, :]
    corner = tiles[:, tile_px - width :, tile_px - width :]
    from_left = shifted(right_strip, "col", n_col, 1)
    from_up = shifted(down_strip, "row", n_row, 1)
    diagonal = [
        (j * n_row + i, (j + 1) * n_row + i + 1) for i in range(n_row - 1) for j in range(n_col - 1)
    ]
    from_corner = lax.ppermute(corner, ("col", "row"), diagonal)

    left_col = jnp.maximum(col_index - 1, 0)
    upper_row = jnp.maximum(row_index - 1, 0)
    f32 = jnp.float32
    moved, weight = shift_tile(offsets, bands, tiles, n_row, n_col)
    left_block, up_block = pair_stats(extents, from_left, from_up, tiles)
    right_block = shifted(left_block, "col", n_col, -1)
    down_block = shifted(up_block, "row", n_row, -1)
    left_stats = unpack_stats(left_block, planes)
    up_stats = unpack_stats(up_block, planes)
    right_stats = unpack_stats(right_block, planes)
    down_stats = unpack_stats(down_block, planes)
    has_right = col_index < n_col - 1
    has_down = row_index < n_row - 1
    has_left_pair = col_index > 0
    has_up_pair = row_index > 0
    gain_one, level_one = combine(
        masked_terms(right_stats, has_right),
        masked_terms(down_stats, has_down),
        masked_terms(left_stats, has_left_pair),
        masked_terms(up_stats, has_up_pair),
    )
    first = jnp.concatenate([gain_one, level_one])
    near = [
        shifted(first, "col", n_col, -1),
        shifted(first, "row", n_row, -1),
        shifted(first, "col", n_col, 1),
        shifted(first, "row", n_row, 1),
    ]
    scale = jnp.exp(gain_one)
    near_scale = [jnp.exp(item[:planes]) for item in near]
    near_level = [item[planes:] for item in near]
    right_two = corrected_stats(right_stats, scale, level_one, near_scale[0], near_level[0])
    down_two = corrected_stats(down_stats, scale, level_one, near_scale[1], near_level[1])
    left_two = corrected_stats(left_stats, near_scale[2], near_level[2], scale, level_one)
    up_two = corrected_stats(up_stats, near_scale[3], near_level[3], scale, level_one)
    gain_two, level_two = combine(
        masked_terms(right_two, has_right),
        masked_terms(down_two, has_down),
        masked_terms(left_two, has_left_pair),
        masked_terms(up_two, has_up_pair),
    )
    own_gain = gain_one + gain_two
    own_level = jnp.exp(gain_two) * level_one + level_two
    final = jnp.concatenate([own_gain, own_level])
    final_left = shifted(final, "col", n_col, 1)
    final_up = shifted(final, "row", n_row, 1)
    final_corner = lax.ppermute(final, ("col", "row"), diagonal)
    terms = jnp.concatenate([
        jnp.exp(own_gain), own_level,
        jnp.exp(final_left[:planes]), final_left[planes:],
        jnp.exp(final_up[:planes]), final_up[planes:],
        jnp.exp(final_corner[:planes]), final_corner[planes:],
    ])
    blended = blend(offsets, bands, terms, moved, from_left, from_up, from_corner, n_row, n_col)
    return blended, weight


def solution(mesh):
    return jax.shard_map(
        local,
        mesh=mesh,
        in_specs=(P(None, "row", "col"), P(), P(), P()),
        out_specs=(P(None, "row", "col"), P("row", "col")),
        check_vma=False,
    )
```

```python
import functools

import jax
import jax.numpy as jnp
from jax import lax
from jax.sharding import PartitionSpec as P
from jax.experimental import pallas as pl
from jax.experimental.pallas import tpu as pltpu

STRIP = 128
SPILL = 128
BLOCK = 128
ROWS = 256


eps = 1e-06


def strip_stats(former, latter, window):
    full = jnp.broadcast_to(window, former.shape)
    number = jnp.sum(full, axis=(-2, -1))
    mean_former = jnp.sum(former * full, axis=(-2, -1)) / number
    mean_latter = jnp.sum(latter * full, axis=(-2, -1)) / number
    dev_former = (former - mean_former[:, None, None]) * full
    dev_latter = (latter - mean_latter[:, None, None]) * full
    var_former = jnp.sum(dev_former * dev_former, axis=(-2, -1)) / number
    var_latter = jnp.sum(dev_latter * dev_latter, axis=(-2, -1)) / number
    covariance = jnp.sum(dev_former * dev_latter, axis=(-2, -1)) / number
    return jnp.stack([mean_former, mean_latter, var_former, var_latter, covariance])


def pair_terms(stats):
    mean_former, mean_latter, var_former, var_latter, covariance = stats
    weight = covariance * covariance / ((var_former + eps) * (var_latter + eps))
    log_ratio = 0.25 * (jnp.log(var_latter + eps) - jnp.log(var_former + eps))
    shift_term = 0.5 * (mean_latter - mean_former)
    return (weight, weight * log_ratio, weight * shift_term)


def corrected_stats(stats, gain_a, level_a, gain_b, level_b):
    mean_former, mean_latter, var_former, var_latter, covariance = stats
    return (
        gain_a * mean_former + level_a,
        gain_b * mean_latter + level_b,
        gain_a * gain_a * var_former,
        gain_b * gain_b * var_latter,
        gain_a * gain_b * covariance,
    )


def pick(rows_out, rows_in, shift):
    a = lax.broadcasted_iota(jnp.int32, (rows_out, rows_in), 0)
    b = lax.broadcasted_iota(jnp.int32, (rows_out, rows_in), 1)
    return jnp.where(b == a + shift, 1.0, 0.0).astype(jnp.bfloat16)


def move_lanes(rows, left, lanes, emit):
    width = STRIP
    lane = lax.broadcasted_iota(jnp.int32, (1, width), 1)
    before = None
    for k in range(lanes // width):
        turned = pltpu.roll(rows[:, k * width : (k + 1) * width], left, 1)
        block = turned if before is None else jnp.where(lane >= left, turned, before)
        before = turned
        emit(k, block)


def blend_kernel(off_ref, band_ref, own_ref, left_terms_ref, up_terms_ref, corner_terms_ref, cur_ref, prev_ref, lcur_ref, lprev_ref,
                 up_ref, corner_ref, out_ref, w_ref, *, n_row, n_col):
    f32 = jnp.float32
    bf16 = jnp.bfloat16
    step = pl.program_id(0)
    planes, rows, tile_px = cur_ref.shape
    width = lcur_ref.shape[2]
    cells = n_row * n_col
    r = lax.axis_index("row")
    c = lax.axis_index("col")
    lc = jnp.maximum(c - 1, 0)
    ur = jnp.maximum(r - 1, 0)
    has_left = c > 0
    has_up = r > 0

    def table(ref, k, rr, cc):
        return ref[k, rr, cc]

    def fade(ids):
        return (jnp.minimum(ids, tile_px - 1 - ids) + 1).astype(f32) / (tile_px / 2.0)

    def band_rows(ids, rr, cc, extra):
        live = (ids >= table(band_ref, 0, rr, cc) * BLOCK) & (ids < table(band_ref, 1, rr, cc) * BLOCK)
        live = live & (ids >= 0) & (ids < tile_px) & extra
        return jnp.where(live, fade(ids), 0.0)

    def gain(k, p):
        ref = (own_ref, left_terms_ref, up_terms_ref, corner_terms_ref)[k]
        return ref[p], ref[planes + p]

    t = lax.broadcasted_iota(jnp.int32, (rows, 1), 0)
    x = lax.broadcasted_iota(jnp.int32, (1, tile_px), 1)
    xs = lax.broadcasted_iota(jnp.int32, (1, width), 1)
    y = step * rows + t
    top = table(off_ref, 0, r, c)
    left = table(off_ref, 1, r, c)
    top_l = table(off_ref, 0, r, lc)
    left_l = table(off_ref, 1, r, lc)
    j = x - left
    w_own = band_rows(y - top, r, c, True) * jnp.where(j >= 0, fade(j), 0.0)
    j_l = xs + tile_px - left_l
    w_left = band_rows(y - top_l, r, lc, has_left) * jnp.where(j_l < tile_px, fade(j_l), 0.0)
    w_ref[...] = w_own
    w_ref[:, :width] += w_left
    reach = SPILL
    down_own = pick(rows, reach + rows, reach - top)
    down_left = pick(rows, reach + rows, reach - top_l)
    for p in range(planes):
        src = jnp.concatenate([prev_ref[p, rows - reach :], cur_ref[p]], axis=0)
        shifted_rows = jnp.dot(down_own, src, preferred_element_type=f32)
        scale, level = gain(0, p)

        def emit(k, block, p=p, scale=scale, level=level):
            span = slice(k * width, (k + 1) * width)
            out_ref[p, :, span] = (scale * block + level) * w_own[:, span]

        move_lanes(shifted_rows, left, tile_px, emit)
        lsrc = jnp.concatenate([lprev_ref[p, rows - reach :], lcur_ref[p]], axis=0)
        lrows = jnp.dot(down_left, lsrc, preferred_element_type=f32)
        window = pltpu.roll(lrows, left_l, 1)
        scale, level = gain(1, p)
        out_ref[p, :, :width] += (scale * window + level) * w_left

    @pl.when(step == 0)
    def _():
        te = lax.broadcasted_iota(jnp.int32, (width, 1), 0)
        top_u = table(off_ref, 0, ur, c)
        left_u = table(off_ref, 1, ur, c)
        top_c = table(off_ref, 0, ur, lc)
        left_c = table(off_ref, 1, ur, lc)
        j_u = x - left_u
        w_up = band_rows(te + tile_px - top_u, ur, c, has_up) * jnp.where(j_u >= 0, fade(j_u), 0.0)
        j_c = xs + tile_px - left_c
        w_corner = band_rows(te + tile_px - top_c, ur, lc, has_up & has_left) * jnp.where(
            j_c < tile_px, fade(j_c), 0.0
        )
        w_ref[:width, :] += w_up
        w_ref[:width, :width] += w_corner
        down_up = pick(width, width, width - top_u)
        down_corner = pick(width, width, width - top_c)
        for p in range(planes):
            urows = jnp.dot(down_up, up_ref[p], preferred_element_type=f32)
            scale, level = gain(2, p)

            def emit(k, block, p=p, scale=scale, level=level):
                span = slice(k * width, (k + 1) * width)
                out_ref[p, :width, span] += (scale * block + level) * w_up[:, span]

            move_lanes(urows, left_u, tile_px, emit)
            crows = jnp.dot(down_corner, corner_ref[p], preferred_element_type=f32)
            window = pltpu.roll(crows, left_c, 1)
            scale, level = gain(3, p)
            out_ref[p, :width, :width] += (scale * window + level) * w_corner


def blend(offsets, bands, terms, tiles, from_left, from_up, from_corner, n_row, n_col):
    planes, tile_px, _ = tiles.shape
    width = from_left.shape[2]
    rows = min(ROWS, tile_px)
    steps = tile_px // rows

    def cur(b, *_):
        return (0, b, 0)

    def prev(b, *_):
        return (0, jnp.maximum(b - 1, 0), 0)

    def fixed(b, *_):
        return (0, 0, 0)

    grid_spec = pltpu.PrefetchScalarGridSpec(
        num_scalar_prefetch=2,
        grid=(steps,),
        in_specs=[
            pl.BlockSpec(memory_space=pltpu.SMEM),
            pl.BlockSpec(memory_space=pltpu.SMEM),
            pl.BlockSpec(memory_space=pltpu.SMEM),
            pl.BlockSpec(memory_space=pltpu.SMEM),
            pl.BlockSpec((planes, rows, tile_px), cur),
            pl.BlockSpec((planes, rows, tile_px), prev),
            pl.BlockSpec((planes, rows, width), cur),
            pl.BlockSpec((planes, rows, width), prev),
            pl.BlockSpec((planes, width, tile_px), fixed),
            pl.BlockSpec((planes, width, width), fixed),
        ],
        out_specs=[
            pl.BlockSpec((planes, rows, tile_px), cur),
            pl.BlockSpec((rows, tile_px), lambda b, *_: (b, 0)),
        ],
    )
    out_bytes = 4 * (planes + 1) * tile_px * tile_px
    in_bytes = 2 * 2 * planes * tile_px * (tile_px + width)
    return pl.pallas_call(
        functools.partial(blend_kernel, n_row=n_row, n_col=n_col),
        grid_spec=grid_spec,
        out_shape=[
            jax.ShapeDtypeStruct((planes, tile_px, tile_px), jnp.float32),
            jax.ShapeDtypeStruct((tile_px, tile_px), jnp.float32),
        ],
        compiler_params=pltpu.CompilerParams(dimension_semantics=("arbitrary",)),
        cost_estimate=pl.CostEstimate(
            flops=12 * planes * tile_px * tile_px, transcendentals=0,
            bytes_accessed=out_bytes + in_bytes,
        ),
    )(offsets, bands, *terms, tiles, tiles, from_left, from_left,
      from_up, from_corner)


def shifted(block, axis, count, step):
    if step > 0:
        route = [(i, i + 1) for i in range(count - 1)]
    else:
        route = [(i + 1, i) for i in range(count - 1)]
    return lax.ppermute(block, axis, route)


def combine(right_pair, down_pair, left_pair, upper_pair):
    denominator = 1.0 + right_pair[0] + down_pair[0] + left_pair[0] + upper_pair[0]
    log_gain = (right_pair[1] + down_pair[1] - left_pair[1] - upper_pair[1]) / denominator
    offset = (right_pair[2] + down_pair[2] - left_pair[2] - upper_pair[2]) / denominator
    return log_gain, offset


def masked_terms(stats, present):
    return tuple(jnp.where(present, item, 0.0) for item in pair_terms(stats))


def local(tiles, extents, offsets, bands):
    planes, tile_px, _ = tiles.shape
    n_row = lax.axis_size("row")
    n_col = lax.axis_size("col")
    row_index = lax.axis_index("row")
    col_index = lax.axis_index("col")
    width = STRIP

    right_strip = tiles[:, :, tile_px - width :]
    down_strip = tiles[:, tile_px - width :, :]
    left_strip = tiles[:, :, :width]
    up_strip = tiles[:, :width, :]
    corner = tiles[:, tile_px - width :, tile_px - width :]
    from_left = shifted(right_strip, "col", n_col, 1)
    from_up = shifted(down_strip, "row", n_row, 1)
    diagonal = [
        (j * n_row + i, (j + 1) * n_row + i + 1) for i in range(n_row - 1) for j in range(n_col - 1)
    ]
    from_corner = lax.ppermute(corner, ("col", "row"), diagonal)

    left_col = jnp.maximum(col_index - 1, 0)
    upper_row = jnp.maximum(row_index - 1, 0)
    strip_ids = jnp.arange(width, dtype=jnp.int32)

    def across(extent):
        return (strip_ids < extent).astype(jnp.float32)[None, None, :]

    def along(extent):
        return (strip_ids < extent).astype(jnp.float32)[None, :, None]

    f32 = jnp.float32
    left_stats = strip_stats(
        from_left.astype(f32), left_strip.astype(f32), across(extents[0, row_index, left_col])
    )
    up_stats = strip_stats(
        from_up.astype(f32), up_strip.astype(f32), along(extents[1, upper_row, col_index])
    )
    right_stats = shifted(left_stats, "col", n_col, -1)
    down_stats = shifted(up_stats, "row", n_row, -1)
    has_right = col_index < n_col - 1
    has_down = row_index < n_row - 1
    has_left_pair = col_index > 0
    has_up_pair = row_index > 0
    gain_one, level_one = combine(
        masked_terms(right_stats, has_right),
        masked_terms(down_stats, has_down),
        masked_terms(left_stats, has_left_pair),
        masked_terms(up_stats, has_up_pair),
    )
    first = jnp.concatenate([gain_one, level_one])
    near = [
        shifted(first, "col", n_col, -1),
        shifted(first, "row", n_row, -1),
        shifted(first, "col", n_col, 1),
        shifted(first, "row", n_row, 1),
    ]
    scale = jnp.exp(gain_one)
    near_scale = [jnp.exp(item[:planes]) for item in near]
    near_level = [item[planes:] for item in near]
    right_two = corrected_stats(right_stats, scale, level_one, near_scale[0], near_level[0])
    down_two = corrected_stats(down_stats, scale, level_one, near_scale[1], near_level[1])
    left_two = corrected_stats(left_stats, near_scale[2], near_level[2], scale, level_one)
    up_two = corrected_stats(up_stats, near_scale[3], near_level[3], scale, level_one)
    gain_two, level_two = combine(
        masked_terms(right_two, has_right),
        masked_terms(down_two, has_down),
        masked_terms(left_two, has_left_pair),
        masked_terms(up_two, has_up_pair),
    )
    own_gain = gain_one + gain_two
    own_level = jnp.exp(gain_two) * level_one + level_two
    final = jnp.concatenate([jnp.exp(own_gain), own_level])
    final_left = shifted(final, "col", n_col, 1)
    final_up = shifted(final, "row", n_row, 1)
    final_corner = lax.ppermute(final, ("col", "row"), diagonal)
    terms = (final, final_left, final_up, final_corner)
    return blend(offsets, bands, terms, tiles, from_left, from_up, from_corner, n_row, n_col)


def solution(mesh):
    return jax.shard_map(
        local,
        mesh=mesh,
        in_specs=(P(None, "row", "col"), P(), P(), P()),
        out_specs=(P(None, "row", "col"), P("row", "col")),
        check_vma=False,
    )
```

```python
import functools

import jax
import jax.numpy as jnp
from jax import lax
from jax.sharding import PartitionSpec as P
from jax.experimental import pallas as pl
from jax.experimental.pallas import tpu as pltpu

STRIP = 128
SPILL = 128
BLOCK = 128
ROWS = 256


eps = 1e-06


def strip_stats(former, latter, window):
    full = jnp.broadcast_to(window, former.shape)
    number = jnp.sum(full, axis=(-2, -1))
    mean_former = jnp.sum(former * full, axis=(-2, -1)) / number
    mean_latter = jnp.sum(latter * full, axis=(-2, -1)) / number
    dev_former = (former - mean_former[:, None, None]) * full
    dev_latter = (latter - mean_latter[:, None, None]) * full
    var_former = jnp.sum(dev_former * dev_former, axis=(-2, -1)) / number
    var_latter = jnp.sum(dev_latter * dev_latter, axis=(-2, -1)) / number
    covariance = jnp.sum(dev_former * dev_latter, axis=(-2, -1)) / number
    return jnp.stack([mean_former, mean_latter, var_former, var_latter, covariance])


def pair_terms(stats):
    mean_former, mean_latter, var_former, var_latter, covariance = stats
    weight = covariance * covariance / ((var_former + eps) * (var_latter + eps))
    log_ratio = 0.25 * (jnp.log(var_latter + eps) - jnp.log(var_former + eps))
    shift_term = 0.5 * (mean_latter - mean_former)
    return (weight, weight * log_ratio, weight * shift_term)


def corrected_stats(stats, gain_a, level_a, gain_b, level_b):
    mean_former, mean_latter, var_former, var_latter, covariance = stats
    return (
        gain_a * mean_former + level_a,
        gain_b * mean_latter + level_b,
        gain_a * gain_a * var_former,
        gain_b * gain_b * var_latter,
        gain_a * gain_b * covariance,
    )


def pick(rows_out, rows_in, shift):
    a = lax.broadcasted_iota(jnp.int32, (rows_out, rows_in), 0)
    b = lax.broadcasted_iota(jnp.int32, (rows_out, rows_in), 1)
    return jnp.where(b == a + shift, 1.0, 0.0).astype(jnp.bfloat16)


def move_lanes(rows, left, lanes, emit):
    width = STRIP
    lane = lax.broadcasted_iota(jnp.int32, (1, width), 1)
    before = None
    for k in range(lanes // width):
        turned = pltpu.roll(rows[:, k * width : (k + 1) * width], left, 1)
        block = turned if before is None else jnp.where(lane >= left, turned, before)
        before = turned
        emit(k, block)


def blend_kernel(off_ref, band_ref, own_ref, left_terms_ref, up_terms_ref, corner_terms_ref, cur_ref, prev_ref, lcur_ref, lprev_ref,
                 up_ref, corner_ref, out_ref, w_ref, *, n_row, n_col):
    f32 = jnp.float32
    bf16 = jnp.bfloat16
    step = pl.program_id(0)
    planes, rows, tile_px = cur_ref.shape
    width = lcur_ref.shape[2]
    cells = n_row * n_col
    r = lax.axis_index("row")
    c = lax.axis_index("col")
    lc = jnp.maximum(c - 1, 0)
    ur = jnp.maximum(r - 1, 0)
    has_left = c > 0
    has_up = r > 0

    def table(ref, k, rr, cc):
        return ref[k, rr, cc]

    def fade(ids):
        return (jnp.minimum(ids, tile_px - 1 - ids) + 1).astype(f32) / (tile_px / 2.0)

    def band_rows(ids, rr, cc, extra):
        live = (ids >= table(band_ref, 0, rr, cc) * BLOCK) & (ids < table(band_ref, 1, rr, cc) * BLOCK)
        live = live & (ids >= 0) & (ids < tile_px) & extra
        return jnp.where(live, fade(ids), 0.0)

    def gain(k, p):
        ref = (own_ref, left_terms_ref, up_terms_ref, corner_terms_ref)[k]
        return ref[p], ref[planes + p]

    t = lax.broadcasted_iota(jnp.int32, (rows, 1), 0)
    x = lax.broadcasted_iota(jnp.int32, (1, tile_px), 1)
    xs = lax.broadcasted_iota(jnp.int32, (1, width), 1)
    y = step * rows + t
    top = table(off_ref, 0, r, c)
    left = table(off_ref, 1, r, c)
    top_l = table(off_ref, 0, r, lc)
    left_l = table(off_ref, 1, r, lc)
    j = x - left
    w_own = band_rows(y - top, r, c, True) * jnp.where(j >= 0, fade(j), 0.0)
    j_l = xs + tile_px - left_l
    w_left = band_rows(y - top_l, r, lc, has_left) * jnp.where(j_l < tile_px, fade(j_l), 0.0)
    w_ref[...] = w_own
    w_ref[:, :width] += w_left
    reach = SPILL
    down_own = pick(rows, reach + rows, reach - top)
    down_left = pick(rows, reach + rows, reach - top_l)
    for p in range(planes):
        src = jnp.concatenate([prev_ref[p, rows - reach :], cur_ref[p]], axis=0)
        shifted_rows = jnp.dot(down_own, src, preferred_element_type=f32)
        scale, level = gain(0, p)

        def emit(k, block, p=p, scale=scale, level=level):
            span = slice(k * width, (k + 1) * width)
            out_ref[p, :, span] = (scale * block + level) * w_own[:, span]

        move_lanes(shifted_rows, left, tile_px, emit)
        lsrc = jnp.concatenate([lprev_ref[p, rows - reach :], lcur_ref[p]], axis=0)
        lrows = jnp.dot(down_left, lsrc, preferred_element_type=f32)
        window = pltpu.roll(lrows, left_l, 1)
        scale, level = gain(1, p)
        out_ref[p, :, :width] += (scale * window + level) * w_left

    @pl.when(step == 0)
    def _():
        te = lax.broadcasted_iota(jnp.int32, (width, 1), 0)
        top_u = table(off_ref, 0, ur, c)
        left_u = table(off_ref, 1, ur, c)
        top_c = table(off_ref, 0, ur, lc)
        left_c = table(off_ref, 1, ur, lc)
        j_u = x - left_u
        w_up = band_rows(te + tile_px - top_u, ur, c, has_up) * jnp.where(j_u >= 0, fade(j_u), 0.0)
        j_c = xs + tile_px - left_c
        w_corner = band_rows(te + tile_px - top_c, ur, lc, has_up & has_left) * jnp.where(
            j_c < tile_px, fade(j_c), 0.0
        )
        w_ref[:width, :] += w_up
        w_ref[:width, :width] += w_corner
        down_up = pick(width, width, width - top_u)
        down_corner = pick(width, width, width - top_c)
        for p in range(planes):
            urows = jnp.dot(down_up, up_ref[p], preferred_element_type=f32)
            scale, level = gain(2, p)

            def emit(k, block, p=p, scale=scale, level=level):
                span = slice(k * width, (k + 1) * width)
                out_ref[p, :width, span] += (scale * block + level) * w_up[:, span]

            move_lanes(urows, left_u, tile_px, emit)
            crows = jnp.dot(down_corner, corner_ref[p], preferred_element_type=f32)
            window = pltpu.roll(crows, left_c, 1)
            scale, level = gain(3, p)
            out_ref[p, :width, :width] += (scale * window + level) * w_corner


def blend(offsets, bands, terms, tiles, from_left, from_up, from_corner, n_row, n_col):
    planes, tile_px, _ = tiles.shape
    width = from_left.shape[2]
    rows = min(ROWS, tile_px)
    steps = tile_px // rows

    def cur(b, *_):
        return (0, b, 0)

    def prev(b, *_):
        return (0, jnp.maximum(b - 1, 0), 0)

    def fixed(b, *_):
        return (0, 0, 0)

    grid_spec = pltpu.PrefetchScalarGridSpec(
        num_scalar_prefetch=2,
        grid=(steps,),
        in_specs=[
            pl.BlockSpec(memory_space=pltpu.SMEM),
            pl.BlockSpec(memory_space=pltpu.SMEM),
            pl.BlockSpec(memory_space=pltpu.SMEM),
            pl.BlockSpec(memory_space=pltpu.SMEM),
            pl.BlockSpec((planes, rows, tile_px), cur),
            pl.BlockSpec((planes, rows, tile_px), prev),
            pl.BlockSpec((planes, rows, width), cur),
            pl.BlockSpec((planes, rows, width), prev),
            pl.BlockSpec((planes, width, tile_px), fixed),
            pl.BlockSpec((planes, width, width), fixed),
        ],
        out_specs=[
            pl.BlockSpec((planes, rows, tile_px), cur),
            pl.BlockSpec((rows, tile_px), lambda b, *_: (b, 0)),
        ],
    )
    out_bytes = 4 * (planes + 1) * tile_px * tile_px
    in_bytes = 2 * 2 * planes * tile_px * (tile_px + width)
    return pl.pallas_call(
        functools.partial(blend_kernel, n_row=n_row, n_col=n_col),
        grid_spec=grid_spec,
        out_shape=[
            jax.ShapeDtypeStruct((planes, tile_px, tile_px), jnp.float32),
            jax.ShapeDtypeStruct((tile_px, tile_px), jnp.float32),
        ],
        compiler_params=pltpu.CompilerParams(dimension_semantics=("arbitrary",)),
        cost_estimate=pl.CostEstimate(
            flops=12 * planes * tile_px * tile_px, transcendentals=0,
            bytes_accessed=out_bytes + in_bytes,
        ),
    )(offsets, bands, *terms, tiles, tiles, from_left, from_left,
      from_up, from_corner)


def shifted(block, axis, count, step):
    if step > 0:
        route = [(i, i + 1) for i in range(count - 1)]
    else:
        route = [(i + 1, i) for i in range(count - 1)]
    return lax.ppermute(block, axis, route)


def combine(right_pair, down_pair, left_pair, upper_pair):
    denominator = 1.0 + right_pair[0] + down_pair[0] + left_pair[0] + upper_pair[0]
    log_gain = (right_pair[1] + down_pair[1] - left_pair[1] - upper_pair[1]) / denominator
    offset = (right_pair[2] + down_pair[2] - left_pair[2] - upper_pair[2]) / denominator
    return log_gain, offset


def masked_terms(stats, present):
    return tuple(jnp.where(present, item, 0.0) for item in pair_terms(stats))


def local(tiles, extents, offsets, bands):
    planes, tile_px, _ = tiles.shape
    n_row = lax.axis_size("row")
    n_col = lax.axis_size("col")
    row_index = lax.axis_index("row")
    col_index = lax.axis_index("col")
    width = STRIP

    right_strip = tiles[:, :, tile_px - width :]
    down_strip = tiles[:, tile_px - width :, :]
    left_strip = tiles[:, :, :width]
    up_strip = tiles[:, :width, :]
    corner = tiles[:, tile_px - width :, tile_px - width :]
    from_left = shifted(right_strip, "col", n_col, 1)
    from_up = shifted(down_strip, "row", n_row, 1)
    diagonal = [
        (j * n_row + i, (j + 1) * n_row + i + 1) for i in range(n_row - 1) for j in range(n_col - 1)
    ]
    from_corner = lax.ppermute(corner, ("col", "row"), diagonal)

    left_col = jnp.maximum(col_index - 1, 0)
    upper_row = jnp.maximum(row_index - 1, 0)
    strip_ids = jnp.arange(width, dtype=jnp.int32)

    def across(extent):
        return (strip_ids < extent).astype(jnp.float32)[None, None, :]

    def along(extent):
        return (strip_ids < extent).astype(jnp.float32)[None, :, None]

    f32 = jnp.float32
    left_stats = strip_stats(
        from_left.astype(f32), left_strip.astype(f32), across(extents[0, row_index, left_col])
    )
    up_stats = strip_stats(
        from_up.astype(f32), up_strip.astype(f32), along(extents[1, upper_row, col_index])
    )
    right_stats = shifted(left_stats, "col", n_col, -1)
    down_stats = shifted(up_stats, "row", n_row, -1)
    has_right = col_index < n_col - 1
    has_down = row_index < n_row - 1
    has_left_pair = col_index > 0
    has_up_pair = row_index > 0
    gain_one, level_one = combine(
        masked_terms(right_stats, has_right),
        masked_terms(down_stats, has_down),
        masked_terms(left_stats, has_left_pair),
        masked_terms(up_stats, has_up_pair),
    )
    scale = jnp.exp(gain_one)
    first = jnp.concatenate([scale, level_one])
    near = [
        shifted(first, "col", n_col, -1),
        shifted(first, "row", n_row, -1),
        shifted(first, "col", n_col, 1),
        shifted(first, "row", n_row, 1),
    ]
    near_scale = [item[:planes] for item in near]
    near_level = [item[planes:] for item in near]
    right_two = corrected_stats(right_stats, scale, level_one, near_scale[0], near_level[0])
    down_two = corrected_stats(down_stats, scale, level_one, near_scale[1], near_level[1])
    left_two = corrected_stats(left_stats, near_scale[2], near_level[2], scale, level_one)
    up_two = corrected_stats(up_stats, near_scale[3], near_level[3], scale, level_one)
    gain_two, level_two = combine(
        masked_terms(right_two, has_right),
        masked_terms(down_two, has_down),
        masked_terms(left_two, has_left_pair),
        masked_terms(up_two, has_up_pair),
    )
    own_gain = gain_one + gain_two
    own_level = jnp.exp(gain_two) * level_one + level_two
    final = jnp.concatenate([jnp.exp(own_gain), own_level])
    final_left = shifted(final, "col", n_col, 1)
    final_up = shifted(final, "row", n_row, 1)
    final_corner = lax.ppermute(final, ("col", "row"), diagonal)
    terms = (final, final_left, final_up, final_corner)
    return blend(offsets, bands, terms, tiles, from_left, from_up, from_corner, n_row, n_col)


def solution(mesh):
    return jax.shard_map(
        local,
        mesh=mesh,
        in_specs=(P(None, "row", "col"), P(), P(), P()),
        out_specs=(P(None, "row", "col"), P("row", "col")),
        check_vma=False,
    )
```

```python
import functools

import jax
import jax.numpy as jnp
from jax import lax
from jax.sharding import PartitionSpec as P
from jax.experimental import pallas as pl
from jax.experimental.pallas import tpu as pltpu

STRIP = 128
SPILL = 128
BLOCK = 128
ROWS = 256


eps = 1e-06


def strip_stats(former, latter, window):
    full = jnp.broadcast_to(window, former.shape)
    number = jnp.sum(full, axis=(-2, -1))
    means = jnp.sum(jnp.stack([former * full, latter * full]), axis=(-2, -1)) / number
    dev_former = (former - means[0][:, None, None]) * full
    dev_latter = (latter - means[1][:, None, None]) * full
    spreads = jnp.sum(
        jnp.stack([dev_former * dev_former, dev_latter * dev_latter, dev_former * dev_latter]),
        axis=(-2, -1),
    ) / number
    return jnp.concatenate([means, spreads])


def pair_terms(stats):
    mean_former, mean_latter, var_former, var_latter, covariance = stats
    weight = covariance * covariance / ((var_former + eps) * (var_latter + eps))
    log_ratio = 0.25 * (jnp.log(var_latter + eps) - jnp.log(var_former + eps))
    shift_term = 0.5 * (mean_latter - mean_former)
    return (weight, weight * log_ratio, weight * shift_term)


def corrected_stats(stats, gain_a, level_a, gain_b, level_b):
    mean_former, mean_latter, var_former, var_latter, covariance = stats
    return (
        gain_a * mean_former + level_a,
        gain_b * mean_latter + level_b,
        gain_a * gain_a * var_former,
        gain_b * gain_b * var_latter,
        gain_a * gain_b * covariance,
    )


def pick(rows_out, rows_in, shift):
    a = lax.broadcasted_iota(jnp.int32, (rows_out, rows_in), 0)
    b = lax.broadcasted_iota(jnp.int32, (rows_out, rows_in), 1)
    return jnp.where(b == a + shift, 1.0, 0.0).astype(jnp.bfloat16)


def move_lanes(rows, left, lanes, emit):
    width = STRIP
    lane = lax.broadcasted_iota(jnp.int32, (1, width), 1)
    before = None
    for k in range(lanes // width):
        turned = pltpu.roll(rows[:, k * width : (k + 1) * width], left, 1)
        block = turned if before is None else jnp.where(lane >= left, turned, before)
        before = turned
        emit(k, block)


def blend_kernel(off_ref, band_ref, own_ref, left_terms_ref, up_terms_ref, corner_terms_ref, cur_ref, prev_ref, lcur_ref, lprev_ref,
                 up_ref, corner_ref, out_ref, w_ref, *, n_row, n_col):
    f32 = jnp.float32
    bf16 = jnp.bfloat16
    step = pl.program_id(0)
    planes, rows, tile_px = cur_ref.shape
    width = lcur_ref.shape[2]
    cells = n_row * n_col
    r = lax.axis_index("row")
    c = lax.axis_index("col")
    lc = jnp.maximum(c - 1, 0)
    ur = jnp.maximum(r - 1, 0)
    has_left = c > 0
    has_up = r > 0

    def table(ref, k, rr, cc):
        return ref[k, rr, cc]

    def fade(ids):
        return (jnp.minimum(ids, tile_px - 1 - ids) + 1).astype(f32) / (tile_px / 2.0)

    def band_rows(ids, rr, cc, extra):
        live = (ids >= table(band_ref, 0, rr, cc) * BLOCK) & (ids < table(band_ref, 1, rr, cc) * BLOCK)
        live = live & (ids >= 0) & (ids < tile_px) & extra
        return jnp.where(live, fade(ids), 0.0)

    def gain(k, p):
        ref = (own_ref, left_terms_ref, up_terms_ref, corner_terms_ref)[k]
        return ref[p], ref[planes + p]

    t = lax.broadcasted_iota(jnp.int32, (rows, 1), 0)
    x = lax.broadcasted_iota(jnp.int32, (1, tile_px), 1)
    xs = lax.broadcasted_iota(jnp.int32, (1, width), 1)
    y = step * rows + t
    top = table(off_ref, 0, r, c)
    left = table(off_ref, 1, r, c)
    top_l = table(off_ref, 0, r, lc)
    left_l = table(off_ref, 1, r, lc)
    j = x - left
    w_own = band_rows(y - top, r, c, True) * jnp.where(j >= 0, fade(j), 0.0)
    j_l = xs + tile_px - left_l
    w_left = band_rows(y - top_l, r, lc, has_left) * jnp.where(j_l < tile_px, fade(j_l), 0.0)
    w_ref[...] = w_own
    w_ref[:, :width] += w_left
    reach = SPILL
    down_own = pick(rows, reach + rows, reach - top)
    down_left = pick(rows, reach + rows, reach - top_l)
    for p in range(planes):
        src = jnp.concatenate([prev_ref[p, rows - reach :], cur_ref[p]], axis=0)
        shifted_rows = jnp.dot(down_own, src, preferred_element_type=f32)
        scale, level = gain(0, p)

        def emit(k, block, p=p, scale=scale, level=level):
            span = slice(k * width, (k + 1) * width)
            out_ref[p, :, span] = (scale * block + level) * w_own[:, span]

        move_lanes(shifted_rows, left, tile_px, emit)
        lsrc = jnp.concatenate([lprev_ref[p, rows - reach :], lcur_ref[p]], axis=0)
        lrows = jnp.dot(down_left, lsrc, preferred_element_type=f32)
        window = pltpu.roll(lrows, left_l, 1)
        scale, level = gain(1, p)
        out_ref[p, :, :width] += (scale * window + level) * w_left

    @pl.when(step == 0)
    def _():
        te = lax.broadcasted_iota(jnp.int32, (width, 1), 0)
        top_u = table(off_ref, 0, ur, c)
        left_u = table(off_ref, 1, ur, c)
        top_c = table(off_ref, 0, ur, lc)
        left_c = table(off_ref, 1, ur, lc)
        j_u = x - left_u
        w_up = band_rows(te + tile_px - top_u, ur, c, has_up) * jnp.where(j_u >= 0, fade(j_u), 0.0)
        j_c = xs + tile_px - left_c
        w_corner = band_rows(te + tile_px - top_c, ur, lc, has_up & has_left) * jnp.where(
            j_c < tile_px, fade(j_c), 0.0
        )
        w_ref[:width, :] += w_up
        w_ref[:width, :width] += w_corner
        down_up = pick(width, width, width - top_u)
        down_corner = pick(width, width, width - top_c)
        for p in range(planes):
            urows = jnp.dot(down_up, up_ref[p], preferred_element_type=f32)
            scale, level = gain(2, p)

            def emit(k, block, p=p, scale=scale, level=level):
                span = slice(k * width, (k + 1) * width)
                out_ref[p, :width, span] += (scale * block + level) * w_up[:, span]

            move_lanes(urows, left_u, tile_px, emit)
            crows = jnp.dot(down_corner, corner_ref[p], preferred_element_type=f32)
            window = pltpu.roll(crows, left_c, 1)
            scale, level = gain(3, p)
            out_ref[p, :width, :width] += (scale * window + level) * w_corner


def blend(offsets, bands, terms, tiles, from_left, from_up, from_corner, n_row, n_col):
    planes, tile_px, _ = tiles.shape
    width = from_left.shape[2]
    rows = min(ROWS, tile_px)
    steps = tile_px // rows

    def cur(b, *_):
        return (0, b, 0)

    def prev(b, *_):
        return (0, jnp.maximum(b - 1, 0), 0)

    def fixed(b, *_):
        return (0, 0, 0)

    grid_spec = pltpu.PrefetchScalarGridSpec(
        num_scalar_prefetch=2,
        grid=(steps,),
        in_specs=[
            pl.BlockSpec(memory_space=pltpu.SMEM),
            pl.BlockSpec(memory_space=pltpu.SMEM),
            pl.BlockSpec(memory_space=pltpu.SMEM),
            pl.BlockSpec(memory_space=pltpu.SMEM),
            pl.BlockSpec((planes, rows, tile_px), cur),
            pl.BlockSpec((planes, rows, tile_px), prev),
            pl.BlockSpec((planes, rows, width), cur),
            pl.BlockSpec((planes, rows, width), prev),
            pl.BlockSpec((planes, width, tile_px), fixed),
            pl.BlockSpec((planes, width, width), fixed),
        ],
        out_specs=[
            pl.BlockSpec((planes, rows, tile_px), cur),
            pl.BlockSpec((rows, tile_px), lambda b, *_: (b, 0)),
        ],
    )
    out_bytes = 4 * (planes + 1) * tile_px * tile_px
    in_bytes = 2 * 2 * planes * tile_px * (tile_px + width)
    return pl.pallas_call(
        functools.partial(blend_kernel, n_row=n_row, n_col=n_col),
        grid_spec=grid_spec,
        out_shape=[
            jax.ShapeDtypeStruct((planes, tile_px, tile_px), jnp.float32),
            jax.ShapeDtypeStruct((tile_px, tile_px), jnp.float32),
        ],
        compiler_params=pltpu.CompilerParams(dimension_semantics=("arbitrary",)),
        cost_estimate=pl.CostEstimate(
            flops=12 * planes * tile_px * tile_px, transcendentals=0,
            bytes_accessed=out_bytes + in_bytes,
        ),
    )(offsets, bands, *terms, tiles, tiles, from_left, from_left,
      from_up, from_corner)


def shifted(block, axis, count, step):
    if step > 0:
        route = [(i, i + 1) for i in range(count - 1)]
    else:
        route = [(i + 1, i) for i in range(count - 1)]
    return lax.ppermute(block, axis, route)


def combine(right_pair, down_pair, left_pair, upper_pair):
    denominator = 1.0 + right_pair[0] + down_pair[0] + left_pair[0] + upper_pair[0]
    log_gain = (right_pair[1] + down_pair[1] - left_pair[1] - upper_pair[1]) / denominator
    offset = (right_pair[2] + down_pair[2] - left_pair[2] - upper_pair[2]) / denominator
    return log_gain, offset


def masked_terms(stats, present):
    return tuple(jnp.where(present, item, 0.0) for item in pair_terms(stats))


def local(tiles, extents, offsets, bands):
    planes, tile_px, _ = tiles.shape
    n_row = lax.axis_size("row")
    n_col = lax.axis_size("col")
    row_index = lax.axis_index("row")
    col_index = lax.axis_index("col")
    width = STRIP

    right_strip = tiles[:, :, tile_px - width :]
    down_strip = tiles[:, tile_px - width :, :]
    left_strip = tiles[:, :, :width]
    up_strip = tiles[:, :width, :]
    corner = tiles[:, tile_px - width :, tile_px - width :]
    from_left = shifted(right_strip, "col", n_col, 1)
    from_up = shifted(down_strip, "row", n_row, 1)
    diagonal = [
        (j * n_row + i, (j + 1) * n_row + i + 1) for i in range(n_row - 1) for j in range(n_col - 1)
    ]
    from_corner = lax.ppermute(corner, ("col", "row"), diagonal)

    left_col = jnp.maximum(col_index - 1, 0)
    upper_row = jnp.maximum(row_index - 1, 0)
    strip_ids = jnp.arange(width, dtype=jnp.int32)

    def across(extent):
        return (strip_ids < extent).astype(jnp.float32)[None, None, :]

    def along(extent):
        return (strip_ids < extent).astype(jnp.float32)[None, :, None]

    f32 = jnp.float32
    left_stats = strip_stats(
        from_left.astype(f32), left_strip.astype(f32), across(extents[0, row_index, left_col])
    )
    up_stats = strip_stats(
        from_up.astype(f32), up_strip.astype(f32), along(extents[1, upper_row, col_index])
    )
    right_stats = shifted(left_stats, "col", n_col, -1)
    down_stats = shifted(up_stats, "row", n_row, -1)
    has_right = col_index < n_col - 1
    has_down = row_index < n_row - 1
    has_left_pair = col_index > 0
    has_up_pair = row_index > 0
    gain_one, level_one = combine(
        masked_terms(right_stats, has_right),
        masked_terms(down_stats, has_down),
        masked_terms(left_stats, has_left_pair),
        masked_terms(up_stats, has_up_pair),
    )
    first = jnp.concatenate([gain_one, level_one])
    near = [
        shifted(first, "col", n_col, -1),
        shifted(first, "row", n_row, -1),
        shifted(first, "col", n_col, 1),
        shifted(first, "row", n_row, 1),
    ]
    scale = jnp.exp(gain_one)
    near_scale = [jnp.exp(item[:planes]) for item in near]
    near_level = [item[planes:] for item in near]
    right_two = corrected_stats(right_stats, scale, level_one, near_scale[0], near_level[0])
    down_two = corrected_stats(down_stats, scale, level_one, near_scale[1], near_level[1])
    left_two = corrected_stats(left_stats, near_scale[2], near_level[2], scale, level_one)
    up_two = corrected_stats(up_stats, near_scale[3], near_level[3], scale, level_one)
    gain_two, level_two = combine(
        masked_terms(right_two, has_right),
        masked_terms(down_two, has_down),
        masked_terms(left_two, has_left_pair),
        masked_terms(up_two, has_up_pair),
    )
    own_gain = gain_one + gain_two
    own_level = jnp.exp(gain_two) * level_one + level_two
    final = jnp.concatenate([jnp.exp(own_gain), own_level])
    final_left = shifted(final, "col", n_col, 1)
    final_up = shifted(final, "row", n_row, 1)
    final_corner = lax.ppermute(final, ("col", "row"), diagonal)
    terms = (final, final_left, final_up, final_corner)
    return blend(offsets, bands, terms, tiles, from_left, from_up, from_corner, n_row, n_col)


def solution(mesh):
    return jax.shard_map(
        local,
        mesh=mesh,
        in_specs=(P(None, "row", "col"), P(), P(), P()),
        out_specs=(P(None, "row", "col"), P("row", "col")),
        check_vma=False,
    )
```
